32 devices in a mesh: dp: 8 (over z, core), leaf: 4 (over y, x).
Axes of the slice: x: 2, y: 2, z: 4, core: 2. Of those that a mesh axis runs over, the one named last changes fastest.
Arguments:
- features: bfloat16 [51200, 384], P(('dp', 'leaf')), may hold values from -6 to 6
- head_weight: bfloat16 [384, 1536], replicated, may hold values from -0.3125 to 0.3125
- gain: float32 [1536], replicated, may hold values from 0.5 to 1.5
- shift: float32 [1536], replicated, may hold values from -3 to 3
- node_weights: bfloat16 [4096, 1536], P('leaf'), may hold values from -0.15625 to 0.15625
- subtree_map: int32 [64], replicated, may hold values from 0 to 63, each once
- node_ids: int32 [512, 64], P('dp'), may hold values from -1 to 4095, as said below
Outputs:
- head_grad: float32 [384, 1536], P(None, 'dp')
- gain_grad: float32 [1536], P('dp')
- shift_grad: float32 [1536], P('dp')
- node_grad: float32 [4096, 1536], P('leaf', 'dp')
The draws below stay inside these ranges and needn't reach their ends.
Inputs may be any that keep to these rules, and one draw needn't show every extreme that they name: `node_ids`: each image has 1 to 16 positive ids, all in one subtree, in its first columns, then -1; and 1 to 48 hard-negative ids in another subtree from column 16 on, then -1. Ids of one image are distinct. The first image has full counts.
All inputs are finite; a program needn't handle non-finite values.
Results may differ from the reference program's by a relative error of at most 0.0036.
Values may be sent and summed in bfloat16 or wider, within the bound.
No kernel may reach another device: no remote copies, remote signals or barrier semaphores. Data moves between devices by JAX's collectives and lax.ppermute only.
A program may use at most 128 MiB of HBM per device.

```python
import jax
import jax.numpy as jnp
from jax import lax

D = 1536
E = 384
P_SIZE = 100
IMG_DEV = 16
SUB_SIZE = 64
KPOS = 16
KNEG = 48
K = 64
IMAGES = 512
NODES = 4096
SUBTREES = 64
N_LEAF = 4


def draw_node_ids(key, part):
    keys = jax.random.split(jax.random.fold_in(key, 17), 6)
    base = jax.random.randint(keys[0], (IMAGES,), 0, SUBTREES)
    pos_sub = base * base // SUBTREES
    neg_sub = (pos_sub + 1 + jax.random.randint(keys[1], (IMAGES,), 0, SUBTREES - 1)) % SUBTREES
    column = jnp.arange(SUB_SIZE, dtype=jnp.int32)[None, :]
    pos_score = jax.random.randint(keys[2], (IMAGES, SUB_SIZE), 0, 1 << 20) * SUB_SIZE + column
    neg_score = jax.random.randint(keys[3], (IMAGES, SUB_SIZE), 0, 1 << 20) * SUB_SIZE + column
    pos_pick = jnp.argsort(pos_score, axis=1)[:, :KPOS].astype(jnp.int32)
    negative_choice = jnp.argsort(neg_score, axis=1)[:, :KNEG].astype(jnp.int32)
    pos_count = jax.random.randint(keys[4], (IMAGES,), 1, KPOS + 1).at[0].set(KPOS)
    neg_count = jax.random.randint(keys[5], (IMAGES,), 1, KNEG + 1).at[0].set(KNEG)
    pos_ids = jnp.where(jnp.arange(KPOS)[None, :] < pos_count[:, None], pos_sub[:, None] * SUB_SIZE + pos_pick, -1)
    neg_ids = jnp.where(jnp.arange(KNEG)[None, :] < neg_count[:, None], neg_sub[:, None] * SUB_SIZE + negative_choice, -1)
    return jnp.concatenate([pos_ids, neg_ids], axis=1).astype(jnp.int32)


def level_of(stream_key, extent, cuts, least, top_value):
    factor_of, own = 1.0, jax.random.fold_in(stream_key, 6)
    for position, shards_of in cuts:
        draws = jnp.exp(jax.random.uniform(jax.random.fold_in(own, position), (shards_of,), jnp.float32, least / len(cuts), top_value / len(cuts)))
        factor_of = factor_of * jnp.repeat(draws, extent[position] // shards_of).reshape([-1 if axis == position else 1 for axis in range(len(extent))])
    return factor_of


def noise(stream_key, shape, width, reach, pieces=(), kind=jnp.bfloat16):
    level = level_of(stream_key, shape, pieces, -0.22, 0.18) if pieces else 1.0
    values = jax.random.normal(stream_key, shape, jnp.float32) * width * level
    return jnp.minimum(jnp.maximum(values, -reach), reach).astype(kind)


def setup_inputs(seed: int = 0) -> dict:
    seeds = jax.random.split(jax.random.key(seed), 8)
    return {
        "features": noise(seeds[0], (IMAGES * P_SIZE, E), 1.0, 6.0, ((0, 32),)),
        "head_weight": noise(seeds[1], (E, D), E ** -0.5, 0.3125),
        "gain": jnp.clip(1.0 + 0.1 * jax.random.normal(seeds[2], (D,), jnp.float32), 0.5, 1.5),
        "shift": noise(seeds[3], (D,), 0.5, 3.0, (), jnp.float32),
        "node_weights": noise(seeds[4], (NODES, D), D ** -0.5, 0.15625, ((0, 4),)),
        "subtree_map": jax.random.permutation(seeds[5], SUBTREES).astype(jnp.int32),
        "node_ids": draw_node_ids(jax.random.fold_in(seeds[7], 71), 0),
    }


def reference(features, head_weight, gain, shift, node_weights, subtree_map, node_ids):
    group = IMG_DEV * N_LEAF
    blocks = IMAGES // group
    feature_blocks = features.reshape(blocks, group * P_SIZE, E)

    def forward(block):
        linear_scores = jnp.dot(block, head_weight, preferred_element_type=jnp.float32)
        shifted = gain * linear_scores + shift
        active = shifted * jax.nn.sigmoid(shifted)
        return jnp.mean(active.reshape(group, P_SIZE, D), axis=1).astype(jnp.bfloat16)

    embedded = lax.map(forward, feature_blocks)
    valid = node_ids >= 0
    safe_ids = jnp.where(valid, node_ids, 0).astype(jnp.int32)
    slots = (subtree_map[safe_ids // SUB_SIZE] * SUB_SIZE + safe_ids % SUB_SIZE).astype(jnp.int32)
    target = (jnp.arange(K) < KPOS).astype(jnp.float32)
    slot_blocks = slots.reshape(blocks, group, K)
    valid_blocks = valid.reshape(blocks, group, K)

    def heads(carry, inputs):
        emb_block, slot_block, valid_block = inputs
        batch_rows = node_weights[slot_block].astype(jnp.float32)
        embedding_spread = emb_block.astype(jnp.float32)
        logit_values = jnp.einsum("vn,ven->ve", embedding_spread, batch_rows, precision=lax.Precision.HIGHEST)
        coef = jnp.where(valid_block, jax.nn.sigmoid(logit_values) - target, 0.0).astype(jnp.bfloat16)
        coefficient_spread = coef.astype(jnp.float32)
        embedding_gradient_rows = jnp.einsum("es,esf->ef", coefficient_spread, batch_rows, precision=lax.Precision.HIGHEST)
        update = coefficient_spread[:, :, None] * embedding_spread[:, None, :]
        carry = carry.at[slot_block.reshape(-1)].add(update.reshape(-1, D))
        return carry, embedding_gradient_rows

    node_grad, emb_grad = lax.scan(heads, jnp.zeros((NODES, D), jnp.float32),
                                   (embedded, slot_blocks, valid_blocks))

    def backward(carry, inputs):
        block, grad_block = inputs
        linear_scores = jnp.dot(block, head_weight, preferred_element_type=jnp.float32)
        shifted = gain * linear_scores + shift
        sig = jax.nn.sigmoid(shifted)
        act_grad = jnp.repeat(grad_block / P_SIZE, P_SIZE, axis=0)
        pixel_gradient = act_grad * sig * (1.0 + shifted * (1.0 - sig))
        lin_grad = (pixel_gradient * gain).astype(jnp.bfloat16)
        head_acc, gain_acc, shift_acc = carry
        head_acc = head_acc + jnp.dot(block.T, lin_grad, preferred_element_type=jnp.float32)
        gain_acc = gain_acc + jnp.sum(pixel_gradient * linear_scores, axis=0)
        shift_acc = shift_acc + jnp.sum(pixel_gradient, axis=0)
        return (head_acc, gain_acc, shift_acc), None

    start = (jnp.zeros((E, D), jnp.float32), jnp.zeros((D,), jnp.float32), jnp.zeros((D,), jnp.float32))
    (head_grad, gain_grad, shift_grad), unused = lax.scan(backward, start, (feature_blocks, emb_grad))
    return head_grad, gain_grad, shift_grad, node_grad
```

```python
import jax
import jax.numpy as jnp
from jax import lax
from jax.sharding import PartitionSpec as P

P_SIZE = 100
SUB_SIZE = 64
KPOS = 16
HIGHEST = lax.Precision.HIGHEST


def block_table(pos_vec, pos_blk, neg_vec, neg_blk, blocks):
    lane_block = jnp.arange(blocks * SUB_SIZE, dtype=jnp.int32)[None, :] // SUB_SIZE
    pos_wide = jnp.tile(pos_vec, (1, blocks))
    neg_wide = jnp.tile(neg_vec, (1, blocks))
    pos_part = jnp.where(lane_block == pos_blk[:, None], pos_wide, 0.0)
    neg_part = jnp.where(lane_block == neg_blk[:, None], neg_wide, 0.0)
    return pos_part + neg_part


def pick_block(values, blk, blocks):
    rows = values.shape[0]
    split = values.reshape(rows, blocks, SUB_SIZE)
    hit = jnp.arange(blocks, dtype=jnp.int32)[None, :, None] == blk[:, None, None]
    return jnp.sum(jnp.where(hit, split, 0.0), axis=1)


def lane_mask(ids, valid):
    column = jnp.arange(SUB_SIZE, dtype=jnp.int32)[None, None, :]
    hit = ((ids % SUB_SIZE)[:, :, None] == column) & valid[:, :, None]
    return jnp.any(hit, axis=1)


def shards(features, head_weight, gain, shift, node_weights, subtree_map, node_ids):
    rows = features.shape[0]
    images_here = rows // P_SIZE
    width = head_weight.shape[1]
    slots_dev = node_weights.shape[0]
    blocks = slots_dev // SUB_SIZE
    n_dp = lax.axis_size("dp")
    leaf = lax.axis_index("leaf")

    select = (
        jnp.arange(rows, dtype=jnp.int32)[None, :] // P_SIZE
        == jnp.arange(images_here, dtype=jnp.int32)[:, None]
    ).astype(jnp.float32)

    linear_scores = jnp.dot(features, head_weight, preferred_element_type=jnp.float32)
    shifted = gain * linear_scores + shift
    sig = jax.nn.sigmoid(shifted)
    active = shifted * sig
    image_sum = jnp.dot(select, active, precision=HIGHEST, preferred_element_type=jnp.float32)
    embedded = (image_sum / P_SIZE).astype(jnp.bfloat16)
    grouped = lax.all_gather(embedded, "leaf", axis=0, tiled=True)
    group = grouped.shape[0]

    valid = node_ids >= 0
    safe_ids = jnp.where(valid, node_ids, 0)
    block_of = subtree_map[safe_ids // SUB_SIZE]
    pos_block = block_of[:, 0]
    neg_block = block_of[:, KPOS]
    pos_here = jnp.where(pos_block // blocks == leaf, pos_block % blocks, -1)
    neg_here = jnp.where(neg_block // blocks == leaf, neg_block % blocks, -1)
    pos_mask = lane_mask(safe_ids[:, :KPOS], valid[:, :KPOS])
    neg_mask = lane_mask(safe_ids[:, KPOS:], valid[:, KPOS:])

    scores = lax.dot_general(
        grouped, node_weights, (((1,), (1,)), ((), ())), preferred_element_type=jnp.float32
    )
    pos_logit = pick_block(scores, pos_here, blocks)
    neg_logit = pick_block(scores, neg_here, blocks)
    pos_coef = jnp.where(pos_mask & (pos_here >= 0)[:, None], jax.nn.sigmoid(pos_logit) - 1.0, 0.0)
    neg_coef = jnp.where(neg_mask & (neg_here >= 0)[:, None], jax.nn.sigmoid(neg_logit), 0.0)
    pos_coef = pos_coef.astype(jnp.bfloat16)
    neg_coef = neg_coef.astype(jnp.bfloat16)
    table = block_table(pos_coef, pos_here, neg_coef, neg_here, blocks).astype(jnp.bfloat16)
    grad_part = jnp.dot(table, node_weights, preferred_element_type=jnp.float32)
    emb_grad = lax.psum_scatter(grad_part, "leaf", scatter_dimension=0, tiled=True)

    col_width = width // n_dp
    column_chunks = grouped.reshape(group, n_dp, col_width).transpose(1, 0, 2)
    compact = jnp.concatenate(
        [
            pos_coef,
            neg_coef,
            pos_here[:, None].astype(jnp.bfloat16),
            neg_here[:, None].astype(jnp.bfloat16),
        ],
        axis=1,
    )
    send = jnp.concatenate(
        [column_chunks, jnp.broadcast_to(compact[None], (n_dp,) + compact.shape)], axis=2
    )
    recv = lax.all_to_all(send, "dp", split_axis=0, concat_axis=0, tiled=True)
    columns = recv[:, :, :col_width].reshape(n_dp * group, col_width)
    info = recv[:, :, col_width:].reshape(n_dp * group, compact.shape[1])
    all_pos = info[:, :SUB_SIZE]
    all_neg = info[:, SUB_SIZE : 2 * SUB_SIZE]
    all_pos_blk = info[:, 2 * SUB_SIZE].astype(jnp.int32)
    all_neg_blk = info[:, 2 * SUB_SIZE + 1].astype(jnp.int32)
    all_table = block_table(all_pos, all_pos_blk, all_neg, all_neg_blk, blocks).astype(jnp.bfloat16)
    node_grad = lax.dot_general(
        all_table, columns, (((0,), (0,)), ((), ())), preferred_element_type=jnp.float32
    )

    spread = jnp.dot(select.T, emb_grad / P_SIZE, precision=HIGHEST, preferred_element_type=jnp.float32)
    pixel_gradient = spread * (sig * (1.0 + shifted * (1.0 - sig)))
    lin_grad = (pixel_gradient * gain).astype(jnp.bfloat16)
    head_term = lax.dot_general(
        features, lin_grad, (((0,), (0,)), ((), ())), preferred_element_type=jnp.float32
    )
    gain_term = jnp.sum(pixel_gradient * linear_scores, axis=0)
    shift_term = jnp.sum(pixel_gradient, axis=0)
    stacked = jnp.concatenate([head_term, gain_term[None], shift_term[None]], axis=0)
    reduced = lax.psum(lax.psum_scatter(stacked, "dp", scatter_dimension=1, tiled=True), "leaf")
    e_size = head_term.shape[0]
    return (reduced[:e_size], reduced[e_size], reduced[e_size + 1], node_grad)


def solution(mesh):
    in_specs = (P(("dp", "leaf"), None), P(), P(), P(), P("leaf", None), P(), P("dp", None))
    out_specs = (P(None, "dp"), P("dp"), P("dp"), P("leaf", "dp"))
    return jax.shard_map(shards, mesh=mesh, in_specs=in_specs, out_specs=out_specs, check_vma=False)
```

```python
import jax
import jax.numpy as jnp
from jax import lax
from jax.sharding import PartitionSpec as P

P_SIZE = 100
SUB_SIZE = 64
KPOS = 16
HIGHEST = lax.Precision.HIGHEST


def block_table(pos_vec, pos_blk, neg_vec, neg_blk, blocks):
    lane_block = jnp.arange(blocks * SUB_SIZE, dtype=jnp.int32)[None, :] // SUB_SIZE
    pos_wide = jnp.tile(pos_vec, (1, blocks))
    neg_wide = jnp.tile(neg_vec, (1, blocks))
    pos_part = jnp.where(lane_block == pos_blk[:, None], pos_wide, 0.0)
    neg_part = jnp.where(lane_block == neg_blk[:, None], neg_wide, 0.0)
    return pos_part + neg_part


def pick_block(values, blk, blocks):
    rows = values.shape[0]
    split = values.reshape(rows, blocks, SUB_SIZE)
    hit = jnp.arange(blocks, dtype=jnp.int32)[None, :, None] == blk[:, None, None]
    return jnp.sum(jnp.where(hit, split, 0.0), axis=1)


def lane_mask(ids, valid):
    column = jnp.arange(SUB_SIZE, dtype=jnp.int32)[None, None, :]
    hit = ((ids % SUB_SIZE)[:, :, None] == column) & valid[:, :, None]
    return jnp.any(hit, axis=1)


def partners(size, bit):
    return [(i, i ^ (1 << bit)) for i in range(size)]


def doubling_gather(x, name):
    size = lax.axis_size(name)
    idx = lax.axis_index(name)
    cur = x[None]
    bit = 0
    while (1 << bit) < size:
        other = lax.ppermute(cur, name, partners(size, bit))
        low = (idx // (1 << bit)) % 2 == 0
        cur = jnp.where(low, jnp.concatenate([cur, other], 0), jnp.concatenate([other, cur], 0))
        bit += 1
    return cur.reshape((size * x.shape[0],) + x.shape[1:])


def halving_scatter(parts, name):
    size = lax.axis_size(name)
    idx = lax.axis_index(name)
    cur = [p.reshape((size, p.shape[0] // size) + p.shape[1:]) for p in parts]
    bit = 0
    while (1 << bit) < size:
        mine = (idx // (1 << bit)) % 2
        pairs = [c.reshape((c.shape[0] // 2, 2) + c.shape[1:]) for c in cur]
        keep = [lax.dynamic_index_in_dim(p, mine, axis=1, keepdims=False) for p in pairs]
        give = [lax.dynamic_index_in_dim(p, 1 - mine, axis=1, keepdims=False) for p in pairs]
        got = lax.ppermute(tuple(give), name, partners(size, bit))
        cur = [k + g for k, g in zip(keep, got)]
        bit += 1
    return [c.reshape(c.shape[1:]) for c in cur]


def butterfly_sum(parts, name):
    size = lax.axis_size(name)
    cur = tuple(parts)
    bit = 0
    while (1 << bit) < size:
        got = lax.ppermute(cur, name, partners(size, bit))
        cur = tuple(c + g for c, g in zip(cur, got))
        bit += 1
    return cur


def shards(features, head_weight, gain, shift, node_weights, subtree_map, node_ids):
    rows = features.shape[0]
    images_here = rows // P_SIZE
    width = head_weight.shape[1]
    slots_dev = node_weights.shape[0]
    blocks = slots_dev // SUB_SIZE
    n_dp = lax.axis_size("dp")
    leaf = lax.axis_index("leaf")

    select = (
        jnp.arange(rows, dtype=jnp.int32)[None, :] // P_SIZE
        == jnp.arange(images_here, dtype=jnp.int32)[:, None]
    ).astype(jnp.float32)

    linear_scores = jnp.dot(features, head_weight, preferred_element_type=jnp.float32)
    shifted = gain * linear_scores + shift
    sig = jax.nn.sigmoid(shifted)
    active = shifted * sig
    image_sum = jnp.dot(select, active, precision=HIGHEST, preferred_element_type=jnp.float32)
    embedded = (image_sum / P_SIZE).astype(jnp.bfloat16)
    grouped = doubling_gather(embedded, "leaf")
    group = grouped.shape[0]

    valid = node_ids >= 0
    safe_ids = jnp.where(valid, node_ids, 0)
    subtree_ids = jnp.arange(subtree_map.shape[0], dtype=jnp.int32)[None, :]
    lead_sub = safe_ids[:, jnp.array([0, KPOS])] // SUB_SIZE
    pos_block = jnp.sum(jnp.where(lead_sub[:, :1] == subtree_ids, subtree_map[None, :], 0), axis=1)
    neg_block = jnp.sum(jnp.where(lead_sub[:, 1:] == subtree_ids, subtree_map[None, :], 0), axis=1)
    pos_here = jnp.where(pos_block // blocks == leaf, pos_block % blocks, -1)
    neg_here = jnp.where(neg_block // blocks == leaf, neg_block % blocks, -1)
    pos_mask = lane_mask(safe_ids[:, :KPOS], valid[:, :KPOS])
    neg_mask = lane_mask(safe_ids[:, KPOS:], valid[:, KPOS:])

    scores = lax.dot_general(
        grouped, node_weights, (((1,), (1,)), ((), ())), preferred_element_type=jnp.float32
    )
    pos_logit = pick_block(scores, pos_here, blocks)
    neg_logit = pick_block(scores, neg_here, blocks)
    pos_coef = jnp.where(pos_mask & (pos_here >= 0)[:, None], jax.nn.sigmoid(pos_logit) - 1.0, 0.0)
    neg_coef = jnp.where(neg_mask & (neg_here >= 0)[:, None], jax.nn.sigmoid(neg_logit), 0.0)
    pos_coef = pos_coef.astype(jnp.bfloat16)
    neg_coef = neg_coef.astype(jnp.bfloat16)
    table = block_table(pos_coef, pos_here, neg_coef, neg_here, blocks).astype(jnp.bfloat16)
    grad_part = jnp.dot(table, node_weights, preferred_element_type=jnp.float32)
    (emb_grad,) = halving_scatter([grad_part], "leaf")

    col_width = width // n_dp
    column_chunks = grouped.reshape(group, n_dp, col_width).transpose(1, 0, 2)
    compact = jnp.concatenate(
        [
            pos_coef,
            neg_coef,
            pos_here[:, None].astype(jnp.bfloat16),
            neg_here[:, None].astype(jnp.bfloat16),
        ],
        axis=1,
    )
    send = jnp.concatenate(
        [column_chunks, jnp.broadcast_to(compact[None], (n_dp,) + compact.shape)], axis=2
    )
    recv = lax.all_to_all(send, "dp", split_axis=0, concat_axis=0, tiled=True)
    columns = recv[:, :, :col_width].reshape(n_dp * group, col_width)
    info = recv[:, :, col_width:].reshape(n_dp * group, compact.shape[1])
    all_pos = info[:, :SUB_SIZE]
    all_neg = info[:, SUB_SIZE : 2 * SUB_SIZE]
    all_pos_blk = info[:, 2 * SUB_SIZE].astype(jnp.int32)
    all_neg_blk = info[:, 2 * SUB_SIZE + 1].astype(jnp.int32)
    all_table = block_table(all_pos, all_pos_blk, all_neg, all_neg_blk, blocks).astype(jnp.bfloat16)
    node_grad = lax.dot_general(
        all_table, columns, (((0,), (0,)), ((), ())), preferred_element_type=jnp.float32
    )

    spread = jnp.dot(select.T, emb_grad / P_SIZE, precision=HIGHEST, preferred_element_type=jnp.float32)
    pixel_gradient = spread * (sig * (1.0 + shifted * (1.0 - sig)))
    lin_grad = (pixel_gradient * gain).astype(jnp.bfloat16)
    head_term = lax.dot_general(
        lin_grad, features, (((0,), (0,)), ((), ())), preferred_element_type=jnp.float32
    )
    gain_term = jnp.sum(pixel_gradient * linear_scores, axis=0)
    shift_term = jnp.sum(pixel_gradient, axis=0)
    side_terms = jnp.stack([gain_term, shift_term], axis=1)
    head_part, side_part = halving_scatter([head_term, side_terms], "dp")
    head_sum, side_sum = butterfly_sum([head_part, side_part], "leaf")
    return (head_sum.T, side_sum[:, 0], side_sum[:, 1], node_grad)


def solution(mesh):
    in_specs = (P(("dp", "leaf"), None), P(), P(), P(), P("leaf", None), P(), P("dp", None))
    out_specs = (P(None, "dp"), P("dp"), P("dp"), P("leaf", "dp"))
    return jax.shard_map(shards, mesh=mesh, in_specs=in_specs, out_specs=out_specs, check_vma=False)
```

```python
import jax
import jax.numpy as jnp
from jax import lax
from jax.sharding import PartitionSpec as P

P_SIZE = 100
SUB_SIZE = 64
KPOS = 16


def block_table(pos_vec, pos_blk, neg_vec, neg_blk, blocks):
    lane_block = jnp.arange(blocks * SUB_SIZE, dtype=jnp.int32)[None, :] // SUB_SIZE
    pos_wide = jnp.tile(pos_vec, (1, blocks))
    neg_wide = jnp.tile(neg_vec, (1, blocks))
    pos_part = jnp.where(lane_block == pos_blk[:, None], pos_wide, 0.0)
    neg_part = jnp.where(lane_block == neg_blk[:, None], neg_wide, 0.0)
    return pos_part + neg_part


def pick_block(values, blk, blocks):
    rows = values.shape[0]
    split = values.reshape(rows, blocks, SUB_SIZE)
    hit = jnp.arange(blocks, dtype=jnp.int32)[None, :, None] == blk[:, None, None]
    return jnp.sum(jnp.where(hit, split, 0.0), axis=1)


def lane_mask(ids, valid):
    column = jnp.arange(SUB_SIZE, dtype=jnp.int32)[None, None, :]
    hit = ((ids % SUB_SIZE)[:, :, None] == column) & valid[:, :, None]
    return jnp.any(hit, axis=1)


def split3(x):
    hi = x.astype(jnp.bfloat16)
    rest = x - hi.astype(jnp.float32)
    mid = rest.astype(jnp.bfloat16)
    lo = (rest - mid.astype(jnp.float32)).astype(jnp.bfloat16)
    return hi, mid, lo


def partners(size, bit):
    return [(i, i ^ (1 << bit)) for i in range(size)]


def doubling_gather(x, name):
    size = lax.axis_size(name)
    idx = lax.axis_index(name)
    cur = x[None]
    bit = 0
    while (1 << bit) < size:
        other = lax.ppermute(cur, name, partners(size, bit))
        low = (idx // (1 << bit)) % 2 == 0
        cur = jnp.where(low, jnp.concatenate([cur, other], 0), jnp.concatenate([other, cur], 0))
        bit += 1
    return cur.reshape((size * x.shape[0],) + x.shape[1:])


def halving_scatter(parts, name):
    size = lax.axis_size(name)
    idx = lax.axis_index(name)
    cur = [p.reshape((size, p.shape[0] // size) + p.shape[1:]) for p in parts]
    bit = 0
    while (1 << bit) < size:
        mine = (idx // (1 << bit)) % 2
        pairs = [c.reshape((c.shape[0] // 2, 2) + c.shape[1:]) for c in cur]
        keep = [lax.dynamic_index_in_dim(p, mine, axis=1, keepdims=False) for p in pairs]
        give = [lax.dynamic_index_in_dim(p, 1 - mine, axis=1, keepdims=False) for p in pairs]
        got = lax.ppermute(tuple(give), name, partners(size, bit))
        cur = [k + g for k, g in zip(keep, got)]
        bit += 1
    return [c.reshape(c.shape[1:]) for c in cur]


def butterfly_sum(parts, name):
    size = lax.axis_size(name)
    cur = tuple(parts)
    bit = 0
    while (1 << bit) < size:
        got = lax.ppermute(cur, name, partners(size, bit))
        cur = tuple(c + g for c, g in zip(cur, got))
        bit += 1
    return cur


def shards(features, head_weight, gain, shift, node_weights, subtree_map, node_ids):
    rows = features.shape[0]
    images_here = rows // P_SIZE
    width = head_weight.shape[1]
    slots_dev = node_weights.shape[0]
    blocks = slots_dev // SUB_SIZE
    n_dp = lax.axis_size("dp")
    leaf = lax.axis_index("leaf")

    select = (
        jnp.arange(rows, dtype=jnp.int32)[None, :] // P_SIZE
        == jnp.arange(images_here, dtype=jnp.int32)[:, None]
    ).astype(jnp.bfloat16)

    linear_scores = jnp.dot(features, head_weight, preferred_element_type=jnp.float32)
    shifted = gain * linear_scores + shift
    sig = jax.nn.sigmoid(shifted)
    active = shifted * sig
    image_sum = jnp.dot(
        jnp.concatenate([select] * 3, axis=1),
        jnp.concatenate(split3(active), axis=0),
        preferred_element_type=jnp.float32,
    )
    embedded = (image_sum / P_SIZE).astype(jnp.bfloat16)
    grouped = doubling_gather(embedded, "leaf")
    group = grouped.shape[0]

    valid = node_ids >= 0
    safe_ids = jnp.where(valid, node_ids, 0)
    subtree_ids = jnp.arange(subtree_map.shape[0], dtype=jnp.int32)[None, :]
    lead_sub = safe_ids[:, jnp.array([0, KPOS])] // SUB_SIZE
    pos_block = jnp.sum(jnp.where(lead_sub[:, :1] == subtree_ids, subtree_map[None, :], 0), axis=1)
    neg_block = jnp.sum(jnp.where(lead_sub[:, 1:] == subtree_ids, subtree_map[None, :], 0), axis=1)
    pos_here = jnp.where(pos_block // blocks == leaf, pos_block % blocks, -1)
    neg_here = jnp.where(neg_block // blocks == leaf, neg_block % blocks, -1)
    pos_mask = lane_mask(safe_ids[:, :KPOS], valid[:, :KPOS])
    neg_mask = lane_mask(safe_ids[:, KPOS:], valid[:, KPOS:])

    scores = lax.dot_general(
        grouped, node_weights, (((1,), (1,)), ((), ())), preferred_element_type=jnp.float32
    )
    pos_logit = pick_block(scores, pos_here, blocks)
    neg_logit = pick_block(scores, neg_here, blocks)
    pos_coef = jnp.where(pos_mask & (pos_here >= 0)[:, None], jax.nn.sigmoid(pos_logit) - 1.0, 0.0)
    neg_coef = jnp.where(neg_mask & (neg_here >= 0)[:, None], jax.nn.sigmoid(neg_logit), 0.0)
    pos_coef = pos_coef.astype(jnp.bfloat16)
    neg_coef = neg_coef.astype(jnp.bfloat16)
    table = block_table(pos_coef, pos_here, neg_coef, neg_here, blocks).astype(jnp.bfloat16)
    grad_part = jnp.dot(table, node_weights, preferred_element_type=jnp.float32)
    (emb_grad,) = halving_scatter([grad_part], "leaf")

    col_width = width // n_dp
    column_chunks = grouped.reshape(group, n_dp, col_width).transpose(1, 0, 2)
    compact = jnp.concatenate(
        [
            pos_coef,
            neg_coef,
            pos_here[:, None].astype(jnp.bfloat16),
            neg_here[:, None].astype(jnp.bfloat16),
        ],
        axis=1,
    )
    send = jnp.concatenate(
        [column_chunks, jnp.broadcast_to(compact[None], (n_dp,) + compact.shape)], axis=2
    )
    recv = lax.all_to_all(send, "dp", split_axis=0, concat_axis=0, tiled=True)
    recv, emb_grad = lax.optimization_barrier((recv, emb_grad))
    columns = recv[:, :, :col_width].reshape(n_dp * group, col_width)
    info = recv[:, :, col_width:].reshape(n_dp * group, compact.shape[1])
    all_pos = info[:, :SUB_SIZE]
    all_neg = info[:, SUB_SIZE : 2 * SUB_SIZE]
    all_pos_blk = info[:, 2 * SUB_SIZE].astype(jnp.int32)
    all_neg_blk = info[:, 2 * SUB_SIZE + 1].astype(jnp.int32)
    all_table = block_table(all_pos, all_pos_blk, all_neg, all_neg_blk, blocks).astype(jnp.bfloat16)
    node_grad = lax.dot_general(
        all_table, columns, (((0,), (0,)), ((), ())), preferred_element_type=jnp.float32
    )

    spread = jnp.dot(
        jnp.concatenate([select.T] * 3, axis=1),
        jnp.concatenate(split3(emb_grad / P_SIZE), axis=0),
        preferred_element_type=jnp.float32,
    )
    pixel_gradient = spread * (sig * (1.0 + shifted * (1.0 - sig)))
    lin_grad = (pixel_gradient * gain).astype(jnp.bfloat16)
    head_term = lax.dot_general(
        lin_grad, features, (((0,), (0,)), ((), ())), preferred_element_type=jnp.float32
    )
    gain_term = jnp.sum(pixel_gradient * linear_scores, axis=0)
    shift_term = jnp.sum(pixel_gradient, axis=0)
    side_terms = jnp.stack([gain_term, shift_term], axis=1)
    head_part, side_part = halving_scatter([head_term, side_terms], "dp")
    head_sum, side_sum = butterfly_sum([head_part, side_part], "leaf")
    return (head_sum.T, side_sum[:, 0], side_sum[:, 1], node_grad)


def solution(mesh):
    in_specs = (P(("dp", "leaf"), None), P(), P(), P(), P("leaf", None), P(), P("dp", None))
    out_specs = (P(None, "dp"), P("dp"), P("dp"), P("leaf", "dp"))
    return jax.shard_map(shards, mesh=mesh, in_specs=in_specs, out_specs=out_specs, check_vma=False)
```

```python
import jax
import jax.numpy as jnp
from jax import lax
from jax.sharding import PartitionSpec as P

P_SIZE = 100
SUB_SIZE = 64
KPOS = 16


def block_table(pos_vec, pos_blk, neg_vec, neg_blk, blocks):
    lane_block = jnp.arange(blocks * SUB_SIZE, dtype=jnp.int32)[None, :] // SUB_SIZE
    pos_wide = jnp.tile(pos_vec, (1, blocks))
    neg_wide = jnp.tile(neg_vec, (1, blocks))
    pos_part = jnp.where(lane_block == pos_blk[:, None], pos_wide, 0.0)
    neg_part = jnp.where(lane_block == neg_blk[:, None], neg_wide, 0.0)
    return pos_part + neg_part


def pick_block(values, blk, blocks):
    rows = values.shape[0]
    split = values.reshape(rows, blocks, SUB_SIZE)
    hit = jnp.arange(blocks, dtype=jnp.int32)[None, :, None] == blk[:, None, None]
    return jnp.sum(jnp.where(hit, split, 0.0), axis=1)


def lane_mask(ids, valid):
    column = jnp.arange(SUB_SIZE, dtype=jnp.int32)[None, None, :]
    hit = ((ids % SUB_SIZE)[:, :, None] == column) & valid[:, :, None]
    return jnp.any(hit, axis=1)


def split3(x):
    hi = lax.reduce_precision(x, exponent_bits=8, mantissa_bits=7)
    rest = x - hi
    mid = lax.reduce_precision(rest, exponent_bits=8, mantissa_bits=7)
    lo = rest - mid
    return hi.astype(jnp.bfloat16), mid.astype(jnp.bfloat16), lo.astype(jnp.bfloat16)


def partners(size, bit):
    return [(i, i ^ (1 << bit)) for i in range(size)]


def doubling_gather(x, name):
    size = lax.axis_size(name)
    idx = lax.axis_index(name)
    cur = x[None]
    bit = 0
    while (1 << bit) < size:
        other = lax.ppermute(cur, name, partners(size, bit))
        low = (idx // (1 << bit)) % 2 == 0
        cur = jnp.where(low, jnp.concatenate([cur, other], 0), jnp.concatenate([other, cur], 0))
        bit += 1
    return cur.reshape((size * x.shape[0],) + x.shape[1:])


def halving_scatter(parts, name):
    size = lax.axis_size(name)
    idx = lax.axis_index(name)
    cur = [p.reshape((size, p.shape[0] // size) + p.shape[1:]) for p in parts]
    bit = 0
    while (1 << bit) < size:
        mine = (idx // (1 << bit)) % 2
        pairs = [c.reshape((c.shape[0] // 2, 2) + c.shape[1:]) for c in cur]
        keep = [lax.dynamic_index_in_dim(p, mine, axis=1, keepdims=False) for p in pairs]
        give = [lax.dynamic_index_in_dim(p, 1 - mine, axis=1, keepdims=False) for p in pairs]
        got = lax.ppermute(tuple(give), name, partners(size, bit))
        cur = [k + g for k, g in zip(keep, got)]
        bit += 1
    return [c.reshape(c.shape[1:]) for c in cur]


def butterfly_sum(parts, name):
    size = lax.axis_size(name)
    cur = tuple(parts)
    bit = 0
    while (1 << bit) < size:
        got = lax.ppermute(cur, name, partners(size, bit))
        cur = tuple(c + g for c, g in zip(cur, got))
        bit += 1
    return cur


def shards(features, head_weight, gain, shift, node_weights, subtree_map, node_ids):
    rows = features.shape[0]
    images_here = rows // P_SIZE
    width = head_weight.shape[1]
    slots_dev = node_weights.shape[0]
    blocks = slots_dev // SUB_SIZE
    n_dp = lax.axis_size("dp")
    leaf = lax.axis_index("leaf")

    select = (
        jnp.arange(rows, dtype=jnp.int32)[None, :] // P_SIZE
        == jnp.arange(images_here, dtype=jnp.int32)[:, None]
    ).astype(jnp.bfloat16)

    linear_scores = jnp.dot(features, head_weight, preferred_element_type=jnp.float32)
    shifted = gain * linear_scores + shift
    sig = jax.nn.sigmoid(shifted)
    active = shifted * sig
    image_sum = jnp.dot(
        jnp.concatenate([select] * 3, axis=1),
        jnp.concatenate(split3(active), axis=0),
        preferred_element_type=jnp.float32,
    )
    embedded = (image_sum / P_SIZE).astype(jnp.bfloat16)
    grouped = doubling_gather(embedded, "leaf")
    group = grouped.shape[0]

    valid = node_ids >= 0
    safe_ids = jnp.where(valid, node_ids, 0)
    subtree_ids = jnp.arange(subtree_map.shape[0], dtype=jnp.int32)[None, :]
    lead_sub = safe_ids[:, jnp.array([0, KPOS])] // SUB_SIZE
    pos_block = jnp.sum(jnp.where(lead_sub[:, :1] == subtree_ids, subtree_map[None, :], 0), axis=1)
    neg_block = jnp.sum(jnp.where(lead_sub[:, 1:] == subtree_ids, subtree_map[None, :], 0), axis=1)
    pos_here = jnp.where(pos_block // blocks == leaf, pos_block % blocks, -1)
    neg_here = jnp.where(neg_block // blocks == leaf, neg_block % blocks, -1)
    pos_mask = lane_mask(safe_ids[:, :KPOS], valid[:, :KPOS])
    neg_mask = lane_mask(safe_ids[:, KPOS:], valid[:, KPOS:])

    scores = lax.dot_general(
        grouped, node_weights, (((1,), (1,)), ((), ())), preferred_element_type=jnp.float32
    )
    pos_logit = pick_block(scores, pos_here, blocks)
    neg_logit = pick_block(scores, neg_here, blocks)
    pos_coef = jnp.where(pos_mask & (pos_here >= 0)[:, None], jax.nn.sigmoid(pos_logit) - 1.0, 0.0)
    neg_coef = jnp.where(neg_mask & (neg_here >= 0)[:, None], jax.nn.sigmoid(neg_logit), 0.0)
    pos_coef = pos_coef.astype(jnp.bfloat16)
    neg_coef = neg_coef.astype(jnp.bfloat16)
    table = block_table(pos_coef, pos_here, neg_coef, neg_here, blocks).astype(jnp.bfloat16)
    grad_part = jnp.dot(table, node_weights, preferred_element_type=jnp.float32)
    (emb_grad,) = halving_scatter([grad_part], "leaf")

    col_width = width // n_dp
    column_chunks = grouped.reshape(group, n_dp, col_width).transpose(1, 0, 2)
    compact = jnp.concatenate(
        [
            pos_coef,
            neg_coef,
            pos_here[:, None].astype(jnp.bfloat16),
            neg_here[:, None].astype(jnp.bfloat16),
        ],
        axis=1,
    )
    send = jnp.concatenate(
        [column_chunks, jnp.broadcast_to(compact[None], (n_dp,) + compact.shape)], axis=2
    )
    recv = lax.all_to_all(send, "dp", split_axis=0, concat_axis=0, tiled=True)
    recv, emb_grad = lax.optimization_barrier((recv, emb_grad))
    columns = recv[:, :, :col_width].reshape(n_dp * group, col_width)
    info = recv[:, :, col_width:].reshape(n_dp * group, compact.shape[1])
    all_pos = info[:, :SUB_SIZE]
    all_neg = info[:, SUB_SIZE : 2 * SUB_SIZE]
    all_pos_blk = info[:, 2 * SUB_SIZE].astype(jnp.int32)
    all_neg_blk = info[:, 2 * SUB_SIZE + 1].astype(jnp.int32)
    all_table = block_table(all_pos, all_pos_blk, all_neg, all_neg_blk, blocks).astype(jnp.bfloat16)
    node_grad = lax.dot_general(
        all_table, columns, (((0,), (0,)), ((), ())), preferred_element_type=jnp.float32
    )

    spread = jnp.dot(
        jnp.concatenate([select.T] * 3, axis=1),
        jnp.concatenate(split3(emb_grad / P_SIZE), axis=0),
        preferred_element_type=jnp.float32,
    )
    pixel_gradient = spread * (sig * (1.0 + shifted * (1.0 - sig)))
    lin_grad = (pixel_gradient * gain).astype(jnp.bfloat16)
    head_term = lax.dot_general(
        lin_grad, features, (((0,), (0,)), ((), ())), preferred_element_type=jnp.float32
    )
    gain_term = jnp.sum(pixel_gradient * linear_scores, axis=0)
    shift_term = jnp.sum(pixel_gradient, axis=0)
    side_terms = jnp.stack([gain_term, shift_term], axis=1)
    head_part, side_part = halving_scatter([head_term, side_terms], "dp")
    head_sum, side_sum = butterfly_sum([head_part, side_part], "leaf")
    return (head_sum.T, side_sum[:, 0], side_sum[:, 1], node_grad)


def solution(mesh):
    in_specs = (P(("dp", "leaf"), None), P(), P(), P(), P("leaf", None), P(), P("dp", None))
    out_specs = (P(None, "dp"), P("dp"), P("dp"), P("leaf", "dp"))
    return jax.shard_map(shards, mesh=mesh, in_specs=in_specs, out_specs=out_specs, check_vma=False)
```

```python
import jax
import jax.numpy as jnp
from jax import lax
from jax.sharding import PartitionSpec as P

P_SIZE = 100
SUB_SIZE = 64
KPOS = 16


def block_table(pos_vec, pos_blk, neg_vec, neg_blk, blocks):
    lane_block = jnp.arange(blocks * SUB_SIZE, dtype=jnp.int32)[None, :] // SUB_SIZE
    pos_wide = jnp.tile(pos_vec, (1, blocks))
    neg_wide = jnp.tile(neg_vec, (1, blocks))
    pos_part = jnp.where(lane_block == pos_blk[:, None], pos_wide, 0.0)
    neg_part = jnp.where(lane_block == neg_blk[:, None], neg_wide, 0.0)
    return pos_part + neg_part


def pick_block(values, blk, blocks):
    rows = values.shape[0]
    split = values.reshape(rows, blocks, SUB_SIZE)
    hit = jnp.arange(blocks, dtype=jnp.int32)[None, :, None] == blk[:, None, None]
    return jnp.sum(jnp.where(hit, split, 0.0), axis=1)


def lane_mask(ids, valid):
    column = jnp.arange(SUB_SIZE, dtype=jnp.int32)[None, None, :]
    hit = ((ids % SUB_SIZE)[:, :, None] == column) & valid[:, :, None]
    return jnp.any(hit, axis=1)


def split3(x):
    hi = lax.reduce_precision(x, exponent_bits=8, mantissa_bits=7)
    rest = x - hi
    mid = lax.reduce_precision(rest, exponent_bits=8, mantissa_bits=7)
    lo = rest - mid
    return hi.astype(jnp.bfloat16), mid.astype(jnp.bfloat16), lo.astype(jnp.bfloat16)


def partners(size, bit):
    return [(i, i ^ (1 << bit)) for i in range(size)]


def doubling_gather(x, name):
    size = lax.axis_size(name)
    idx = lax.axis_index(name)
    cur = x[None]
    bit = 0
    while (1 << bit) < size:
        other = lax.ppermute(cur, name, partners(size, bit))
        low = (idx // (1 << bit)) % 2 == 0
        cur = jnp.where(low, jnp.concatenate([cur, other], 0), jnp.concatenate([other, cur], 0))
        bit += 1
    return cur.reshape((size * x.shape[0],) + x.shape[1:])


def halving_scatter(parts, name):
    size = lax.axis_size(name)
    idx = lax.axis_index(name)
    cur = [p.reshape((size, p.shape[0] // size) + p.shape[1:]) for p in parts]
    bit = 0
    while (1 << bit) < size:
        mine = (idx // (1 << bit)) % 2
        pairs = [c.reshape((c.shape[0] // 2, 2) + c.shape[1:]) for c in cur]
        keep = [lax.dynamic_index_in_dim(p, mine, axis=1, keepdims=False) for p in pairs]
        give = [lax.dynamic_index_in_dim(p, 1 - mine, axis=1, keepdims=False) for p in pairs]
        got = lax.ppermute(tuple(give), name, partners(size, bit))
        cur = [k + g for k, g in zip(keep, got)]
        bit += 1
    return [c.reshape(c.shape[1:]) for c in cur]


def butterfly_sum(parts, name):
    size = lax.axis_size(name)
    cur = tuple(parts)
    bit = 0
    while (1 << bit) < size:
        got = lax.ppermute(cur, name, partners(size, bit))
        cur = tuple(c + g for c, g in zip(cur, got))
        bit += 1
    return cur


def halve_steps(x, name, axis, bits):
    idx = lax.axis_index(name)
    size = lax.axis_size(name)
    for bit in bits:
        n = x.shape[axis]
        pairs = x.reshape(x.shape[:axis] + (n // 2, 2) + x.shape[axis + 1 :])
        mine = (idx // (1 << bit)) % 2
        keep = lax.dynamic_index_in_dim(pairs, mine, axis + 1, keepdims=False)
        give = lax.dynamic_index_in_dim(pairs, 1 - mine, axis + 1, keepdims=False)
        x = keep + lax.ppermute(give, name, partners(size, bit))
    return x


def double_steps(x, name, axis, bits):
    idx = lax.axis_index(name)
    size = lax.axis_size(name)
    for bit in bits:
        other = lax.ppermute(x, name, partners(size, bit))
        low = (idx // (1 << bit)) % 2 == 0
        x = jnp.where(low, jnp.concatenate([x, other], axis), jnp.concatenate([other, x], axis))
    return x


def axis_bits(name):
    size = lax.axis_size(name)
    bit = 0
    while (1 << bit) < size:
        bit += 1
    return list(range(bit))


def reduce_head(head, side):
    n_dp = lax.axis_size("dp")
    n_leaf = lax.axis_size("leaf")
    rows, cols = head.shape
    w = rows // n_dp
    dbits = axis_bits("dp")
    lbits = axis_bits("leaf")
    h = halve_steps(head.reshape(n_dp, w, cols), "dp", 0, dbits[:1])
    s = halve_steps(side.reshape(n_dp, w, side.shape[1]), "dp", 0, dbits[:1])
    half = cols // 2
    first = halve_steps(h[:, :, :half], "dp", 0, dbits[1:])
    s = halve_steps(s, "dp", 0, dbits[1:])
    second = h[:, :, half:].reshape(h.shape[:2] + (n_leaf, half // n_leaf))
    second = halve_steps(second, "leaf", 2, lbits)
    second = halve_steps(second, "dp", 0, dbits[1:])
    first, s = butterfly_sum((first, s), "leaf")
    second = double_steps(second, "leaf", 2, lbits)
    head_sum = jnp.concatenate([first.reshape(w, half), second.reshape(w, half)], axis=1)
    return head_sum, s.reshape(w, side.shape[1])


def shards(features, head_weight, gain, shift, node_weights, subtree_map, node_ids):
    rows = features.shape[0]
    images_here = rows // P_SIZE
    width = head_weight.shape[1]
    slots_dev = node_weights.shape[0]
    blocks = slots_dev // SUB_SIZE
    n_dp = lax.axis_size("dp")
    leaf = lax.axis_index("leaf")

    select = (
        jnp.arange(rows, dtype=jnp.int32)[None, :] // P_SIZE
        == jnp.arange(images_here, dtype=jnp.int32)[:, None]
    ).astype(jnp.bfloat16)

    linear_scores = jnp.dot(features, head_weight, preferred_element_type=jnp.float32)
    shifted = gain * linear_scores + shift
    sig = jax.nn.sigmoid(shifted)
    active = shifted * sig
    image_sum = jnp.dot(
        jnp.concatenate([select] * 3, axis=1),
        jnp.concatenate(split3(active), axis=0),
        preferred_element_type=jnp.float32,
    )
    embedded = (image_sum / P_SIZE).astype(jnp.bfloat16)
    grouped = doubling_gather(embedded, "leaf")
    group = grouped.shape[0]

    valid = node_ids >= 0
    safe_ids = jnp.where(valid, node_ids, 0)
    subtree_ids = jnp.arange(subtree_map.shape[0], dtype=jnp.int32)[None, :]
    lead_sub = safe_ids[:, jnp.array([0, KPOS])] // SUB_SIZE
    pos_block = jnp.sum(jnp.where(lead_sub[:, :1] == subtree_ids, subtree_map[None, :], 0), axis=1)
    neg_block = jnp.sum(jnp.where(lead_sub[:, 1:] == subtree_ids, subtree_map[None, :], 0), axis=1)
    pos_here = jnp.where(pos_block // blocks == leaf, pos_block % blocks, -1)
    neg_here = jnp.where(neg_block // blocks == leaf, neg_block % blocks, -1)
    pos_mask = lane_mask(safe_ids[:, :KPOS], valid[:, :KPOS])
    neg_mask = lane_mask(safe_ids[:, KPOS:], valid[:, KPOS:])

    scores = lax.dot_general(
        grouped, node_weights, (((1,), (1,)), ((), ())), preferred_element_type=jnp.float32
    )
    pos_logit = pick_block(scores, pos_here, blocks)
    neg_logit = pick_block(scores, neg_here, blocks)
    pos_coef = jnp.where(pos_mask & (pos_here >= 0)[:, None], jax.nn.sigmoid(pos_logit) - 1.0, 0.0)
    neg_coef = jnp.where(neg_mask & (neg_here >= 0)[:, None], jax.nn.sigmoid(neg_logit), 0.0)
    pos_coef = pos_coef.astype(jnp.bfloat16)
    neg_coef = neg_coef.astype(jnp.bfloat16)
    table = block_table(pos_coef, pos_here, neg_coef, neg_here, blocks).astype(jnp.bfloat16)
    grad_part = jnp.dot(table, node_weights, preferred_element_type=jnp.float32)
    (emb_grad,) = halving_scatter([grad_part], "leaf")

    col_width = width // n_dp
    column_chunks = grouped.reshape(group, n_dp, col_width).transpose(1, 0, 2)
    compact = jnp.concatenate(
        [
            pos_coef,
            neg_coef,
            pos_here[:, None].astype(jnp.bfloat16),
            neg_here[:, None].astype(jnp.bfloat16),
        ],
        axis=1,
    )
    send = jnp.concatenate(
        [column_chunks, jnp.broadcast_to(compact[None], (n_dp,) + compact.shape)], axis=2
    )
    recv = lax.all_to_all(send, "dp", split_axis=0, concat_axis=0, tiled=True)
    recv, emb_grad = lax.optimization_barrier((recv, emb_grad))
    columns = recv[:, :, :col_width].reshape(n_dp * group, col_width)
    info = recv[:, :, col_width:].reshape(n_dp * group, compact.shape[1])
    all_pos = info[:, :SUB_SIZE]
    all_neg = info[:, SUB_SIZE : 2 * SUB_SIZE]
    all_pos_blk = info[:, 2 * SUB_SIZE].astype(jnp.int32)
    all_neg_blk = info[:, 2 * SUB_SIZE + 1].astype(jnp.int32)
    all_table = block_table(all_pos, all_pos_blk, all_neg, all_neg_blk, blocks).astype(jnp.bfloat16)
    node_grad = lax.dot_general(
        all_table, columns, (((0,), (0,)), ((), ())), preferred_element_type=jnp.float32
    )

    spread = jnp.dot(
        jnp.concatenate([select.T] * 3, axis=1),
        jnp.concatenate(split3(emb_grad / P_SIZE), axis=0),
        preferred_element_type=jnp.float32,
    )
    pixel_gradient = spread * (sig * (1.0 + shifted * (1.0 - sig)))
    lin_grad = (pixel_gradient * gain).astype(jnp.bfloat16)
    head_term = lax.dot_general(
        lin_grad, features, (((0,), (0,)), ((), ())), preferred_element_type=jnp.float32
    )
    gain_term = jnp.sum(pixel_gradient * linear_scores, axis=0)
    shift_term = jnp.sum(pixel_gradient, axis=0)
    side_terms = jnp.stack([gain_term, shift_term], axis=1)
    head_sum, side_sum = reduce_head(head_term, side_terms)
    return (head_sum.T, side_sum[:, 0], side_sum[:, 1], node_grad)


def solution(mesh):
    in_specs = (P(("dp", "leaf"), None), P(), P(), P(), P("leaf", None), P(), P("dp", None))
    out_specs = (P(None, "dp"), P("dp"), P("dp"), P("leaf", "dp"))
    return jax.shard_map(shards, mesh=mesh, in_specs=in_specs, out_specs=out_specs, check_vma=False)
```

```python
import jax
import jax.numpy as jnp
from jax import lax
from jax.sharding import PartitionSpec as P

P_SIZE = 100
SUB_SIZE = 64
KPOS = 16
HIGHEST = lax.Precision.HIGHEST


def block_table(pos_vec, pos_blk, neg_vec, neg_blk, blocks):
    lane_block = jnp.arange(blocks * SUB_SIZE, dtype=jnp.int32)[None, :] // SUB_SIZE
    pos_wide = jnp.tile(pos_vec, (1, blocks))
    neg_wide = jnp.tile(neg_vec, (1, blocks))
    pos_part = jnp.where(lane_block == pos_blk[:, None], pos_wide, 0.0)
    neg_part = jnp.where(lane_block == neg_blk[:, None], neg_wide, 0.0)
    return pos_part + neg_part


def pick_block(values, blk, blocks):
    rows = values.shape[0]
    split = values.reshape(rows, blocks, SUB_SIZE)
    hit = jnp.arange(blocks, dtype=jnp.int32)[None, :, None] == blk[:, None, None]
    return jnp.sum(jnp.where(hit, split, 0.0), axis=1)


def lane_mask(ids, valid):
    column = jnp.arange(SUB_SIZE, dtype=jnp.int32)[None, None, :]
    hit = ((ids % SUB_SIZE)[:, :, None] == column) & valid[:, :, None]
    return jnp.any(hit, axis=1)


def partners(size, bit):
    return [(i, i ^ (1 << bit)) for i in range(size)]


def doubling_gather(x, name):
    size = lax.axis_size(name)
    idx = lax.axis_index(name)
    cur = x[None]
    bit = 0
    while (1 << bit) < size:
        other = lax.ppermute(cur, name, partners(size, bit))
        low = (idx // (1 << bit)) % 2 == 0
        cur = jnp.where(low, jnp.concatenate([cur, other], 0), jnp.concatenate([other, cur], 0))
        bit += 1
    return cur.reshape((size * x.shape[0],) + x.shape[1:])


def halving_scatter(parts, name):
    size = lax.axis_size(name)
    idx = lax.axis_index(name)
    cur = [p.reshape((size, p.shape[0] // size) + p.shape[1:]) for p in parts]
    bit = 0
    while (1 << bit) < size:
        mine = (idx // (1 << bit)) % 2
        pairs = [c.reshape((c.shape[0] // 2, 2) + c.shape[1:]) for c in cur]
        keep = [lax.dynamic_index_in_dim(p, mine, axis=1, keepdims=False) for p in pairs]
        give = [lax.dynamic_index_in_dim(p, 1 - mine, axis=1, keepdims=False) for p in pairs]
        got = lax.ppermute(tuple(give), name, partners(size, bit))
        cur = [k + g for k, g in zip(keep, got)]
        bit += 1
    return [c.reshape(c.shape[1:]) for c in cur]


def butterfly_sum(parts, name):
    size = lax.axis_size(name)
    cur = tuple(parts)
    bit = 0
    while (1 << bit) < size:
        got = lax.ppermute(cur, name, partners(size, bit))
        cur = tuple(c + g for c, g in zip(cur, got))
        bit += 1
    return cur


def shards(features, head_weight, gain, shift, node_weights, subtree_map, node_ids):
    rows = features.shape[0]
    images_here = rows // P_SIZE
    width = head_weight.shape[1]
    slots_dev = node_weights.shape[0]
    blocks = slots_dev // SUB_SIZE
    n_dp = lax.axis_size("dp")
    leaf = lax.axis_index("leaf")

    select = (
        jnp.arange(rows, dtype=jnp.int32)[None, :] // P_SIZE
        == jnp.arange(images_here, dtype=jnp.int32)[:, None]
    ).astype(jnp.float32)

    linear_scores = jnp.dot(features, head_weight, preferred_element_type=jnp.float32)
    shifted = gain * linear_scores + shift
    sig = jax.nn.sigmoid(shifted)
    active = shifted * sig
    image_sum = jnp.dot(select, active, precision=HIGHEST, preferred_element_type=jnp.float32)
    embedded = (image_sum / P_SIZE).astype(jnp.bfloat16)
    grouped = doubling_gather(embedded, "leaf")
    group = grouped.shape[0]

    valid = node_ids >= 0
    safe_ids = jnp.where(valid, node_ids, 0)
    subtree_ids = jnp.arange(subtree_map.shape[0], dtype=jnp.int32)[None, :]
    lead_sub = safe_ids[:, jnp.array([0, KPOS])] // SUB_SIZE
    pos_block = jnp.sum(jnp.where(lead_sub[:, :1] == subtree_ids, subtree_map[None, :], 0), axis=1)
    neg_block = jnp.sum(jnp.where(lead_sub[:, 1:] == subtree_ids, subtree_map[None, :], 0), axis=1)
    pos_here = jnp.where(pos_block // blocks == leaf, pos_block % blocks, -1)
    neg_here = jnp.where(neg_block // blocks == leaf, neg_block % blocks, -1)
    pos_mask = lane_mask(safe_ids[:, :KPOS], valid[:, :KPOS])
    neg_mask = lane_mask(safe_ids[:, KPOS:], valid[:, KPOS:])

    scores = lax.dot_general(
        grouped, node_weights, (((1,), (1,)), ((), ())), preferred_element_type=jnp.float32
    )
    pos_logit = pick_block(scores, pos_here, blocks)
    neg_logit = pick_block(scores, neg_here, blocks)
    pos_coef = jnp.where(pos_mask & (pos_here >= 0)[:, None], jax.nn.sigmoid(pos_logit) - 1.0, 0.0)
    neg_coef = jnp.where(neg_mask & (neg_here >= 0)[:, None], jax.nn.sigmoid(neg_logit), 0.0)
    pos_coef = pos_coef.astype(jnp.bfloat16)
    neg_coef = neg_coef.astype(jnp.bfloat16)
    table = block_table(pos_coef, pos_here, neg_coef, neg_here, blocks).astype(jnp.bfloat16)
    grad_part = jnp.dot(table, node_weights, preferred_element_type=jnp.float32)
    (emb_grad,) = halving_scatter([grad_part], "leaf")

    col_width = width // n_dp
    column_chunks = grouped.reshape(group, n_dp, col_width).transpose(1, 0, 2)
    compact = jnp.concatenate(
        [
            pos_coef,
            neg_coef,
            pos_here[:, None].astype(jnp.bfloat16),
            neg_here[:, None].astype(jnp.bfloat16),
        ],
        axis=1,
    )
    send = jnp.concatenate(
        [column_chunks, jnp.broadcast_to(compact[None], (n_dp,) + compact.shape)], axis=2
    )
    recv = lax.all_to_all(send, "dp", split_axis=0, concat_axis=0, tiled=True)
    columns = recv[:, :, :col_width].reshape(n_dp * group, col_width)
    info = recv[:, :, col_width:].reshape(n_dp * group, compact.shape[1])
    all_pos = info[:, :SUB_SIZE]
    all_neg = info[:, SUB_SIZE : 2 * SUB_SIZE]
    all_pos_blk = info[:, 2 * SUB_SIZE].astype(jnp.int32)
    all_neg_blk = info[:, 2 * SUB_SIZE + 1].astype(jnp.int32)
    all_table = block_table(all_pos, all_pos_blk, all_neg, all_neg_blk, blocks).astype(jnp.bfloat16)
    node_grad = lax.dot_general(
        all_table, columns, (((0,), (0,)), ((), ())), preferred_element_type=jnp.float32
    )

    spread = jnp.dot(select.T, emb_grad / P_SIZE, precision=HIGHEST, preferred_element_type=jnp.float32)
    pixel_gradient = spread * (sig * (1.0 + shifted * (1.0 - sig)))
    lin_grad = (pixel_gradient * gain).astype(jnp.bfloat16)
    head_term = lax.dot_general(
        lin_grad, features, (((0,), (0,)), ((), ())), preferred_element_type=jnp.float32
    )
    gain_term = jnp.sum(pixel_gradient * linear_scores, axis=0)
    shift_term = jnp.sum(pixel_gradient, axis=0)
    e_size = head_term.shape[1]
    chunk = width // n_dp
    extra = -(-2 * chunk // e_size)
    side_rows = jnp.stack([gain_term, shift_term], axis=1).reshape(n_dp, 2 * chunk)
    side_rows = jnp.pad(side_rows, ((0, 0), (0, extra * e_size - 2 * chunk)))
    stacked = jnp.concatenate(
        [head_term.reshape(n_dp, chunk, e_size), side_rows.reshape(n_dp, extra, e_size)], axis=1
    )
    (part,) = halving_scatter([stacked], "dp")
    (total,) = butterfly_sum([part[0]], "leaf")
    side_sum = total[chunk:].reshape(-1)[: 2 * chunk].reshape(chunk, 2)
    return (total[:chunk].T, side_sum[:, 0], side_sum[:, 1], node_grad)


def solution(mesh):
    in_specs = (P(("dp", "leaf"), None), P(), P(), P(), P("leaf", None), P(), P("dp", None))
    out_specs = (P(None, "dp"), P("dp"), P("dp"), P("leaf", "dp"))
    return jax.shard_map(shards, mesh=mesh, in_specs=in_specs, out_specs=out_specs, check_vma=False)
```

```python
import jax
import jax.numpy as jnp
from jax import lax
from jax.sharding import PartitionSpec as P

P_SIZE = 100
SUB_SIZE = 64
KPOS = 16
HIGHEST = lax.Precision.HIGHEST


def block_table(pos_vec, pos_blk, neg_vec, neg_blk, blocks):
    lane_block = jnp.arange(blocks * SUB_SIZE, dtype=jnp.int32)[None, :] // SUB_SIZE
    pos_wide = jnp.tile(pos_vec, (1, blocks))
    neg_wide = jnp.tile(neg_vec, (1, blocks))
    pos_part = jnp.where(lane_block == pos_blk[:, None], pos_wide, 0.0)
    neg_part = jnp.where(lane_block == neg_blk[:, None], neg_wide, 0.0)
    return pos_part + neg_part


def pick_block(values, blk, blocks):
    rows = values.shape[0]
    split = values.reshape(rows, blocks, SUB_SIZE)
    hit = jnp.arange(blocks, dtype=jnp.int32)[None, :, None] == blk[:, None, None]
    return jnp.sum(jnp.where(hit, split, 0.0), axis=1)


def lane_mask(ids, valid):
    column = jnp.arange(SUB_SIZE, dtype=jnp.int32)[None, None, :]
    hit = ((ids % SUB_SIZE)[:, :, None] == column) & valid[:, :, None]
    return jnp.any(hit, axis=1)


def partners(size, bit):
    return [(i, i ^ (1 << bit)) for i in range(size)]


def doubling_gather(x, name):
    size = lax.axis_size(name)
    idx = lax.axis_index(name)
    cur = x[None]
    bit = 0
    while (1 << bit) < size:
        other = lax.ppermute(cur, name, partners(size, bit))
        low = (idx // (1 << bit)) % 2 == 0
        cur = jnp.where(low, jnp.concatenate([cur, other], 0), jnp.concatenate([other, cur], 0))
        bit += 1
    return cur.reshape((size * x.shape[0],) + x.shape[1:])


def halving_scatter(parts, name):
    size = lax.axis_size(name)
    idx = lax.axis_index(name)
    cur = [p.reshape((size, p.shape[0] // size) + p.shape[1:]) for p in parts]
    bit = 0
    while (1 << bit) < size:
        mine = (idx // (1 << bit)) % 2
        pairs = [c.reshape((c.shape[0] // 2, 2) + c.shape[1:]) for c in cur]
        keep = [lax.dynamic_index_in_dim(p, mine, axis=1, keepdims=False) for p in pairs]
        give = [lax.dynamic_index_in_dim(p, 1 - mine, axis=1, keepdims=False) for p in pairs]
        got = lax.ppermute(tuple(give), name, partners(size, bit))
        cur = [k + g for k, g in zip(keep, got)]
        bit += 1
    return [c.reshape(c.shape[1:]) for c in cur]


def butterfly_sum(parts, name):
    size = lax.axis_size(name)
    cur = tuple(parts)
    bit = 0
    while (1 << bit) < size:
        got = lax.ppermute(cur, name, partners(size, bit))
        cur = tuple(c + g for c, g in zip(cur, got))
        bit += 1
    return cur


def shards(features, head_weight, gain, shift, node_weights, subtree_map, node_ids):
    rows = features.shape[0]
    images_here = rows // P_SIZE
    width = head_weight.shape[1]
    slots_dev = node_weights.shape[0]
    blocks = slots_dev // SUB_SIZE
    n_dp = lax.axis_size("dp")
    leaf = lax.axis_index("leaf")

    select = (
        jnp.arange(rows, dtype=jnp.int32)[None, :] // P_SIZE
        == jnp.arange(images_here, dtype=jnp.int32)[:, None]
    ).astype(jnp.float32)

    linear_scores = jnp.dot(features, head_weight, preferred_element_type=jnp.float32)
    shifted = gain * linear_scores + shift
    sig = jax.nn.sigmoid(shifted)
    active = shifted * sig
    image_sum = jnp.dot(select, active, precision=HIGHEST, preferred_element_type=jnp.float32)
    embedded = (image_sum / P_SIZE).astype(jnp.bfloat16)
    grouped = doubling_gather(embedded, "leaf")
    group = grouped.shape[0]

    valid = node_ids >= 0
    safe_ids = jnp.where(valid, node_ids, 0)
    subtree_ids = jnp.arange(subtree_map.shape[0], dtype=jnp.int32)[None, :]
    lead_sub = safe_ids[:, jnp.array([0, KPOS])] // SUB_SIZE
    pos_block = jnp.sum(jnp.where(lead_sub[:, :1] == subtree_ids, subtree_map[None, :], 0), axis=1)
    neg_block = jnp.sum(jnp.where(lead_sub[:, 1:] == subtree_ids, subtree_map[None, :], 0), axis=1)
    pos_here = jnp.where(pos_block // blocks == leaf, pos_block % blocks, -1)
    neg_here = jnp.where(neg_block // blocks == leaf, neg_block % blocks, -1)
    pos_mask = lane_mask(safe_ids[:, :KPOS], valid[:, :KPOS])
    neg_mask = lane_mask(safe_ids[:, KPOS:], valid[:, KPOS:])

    scores = lax.dot_general(
        grouped, node_weights, (((1,), (1,)), ((), ())), preferred_element_type=jnp.float32
    )
    pos_logit = pick_block(scores, pos_here, blocks)
    neg_logit = pick_block(scores, neg_here, blocks)
    pos_coef = jnp.where(pos_mask & (pos_here >= 0)[:, None], jax.nn.sigmoid(pos_logit) - 1.0, 0.0)
    neg_coef = jnp.where(neg_mask & (neg_here >= 0)[:, None], jax.nn.sigmoid(neg_logit), 0.0)
    pos_coef = pos_coef.astype(jnp.bfloat16)
    neg_coef = neg_coef.astype(jnp.bfloat16)
    table = block_table(pos_coef, pos_here, neg_coef, neg_here, blocks).astype(jnp.bfloat16)
    grad_part = jnp.dot(table, node_weights, preferred_element_type=jnp.float32)
    (emb_grad,) = halving_scatter([grad_part], "leaf")

    col_width = width // n_dp
    column_chunks = grouped.reshape(group, n_dp, col_width).transpose(1, 0, 2)
    compact = jnp.concatenate(
        [
            pos_coef,
            neg_coef,
            pos_here[:, None].astype(jnp.bfloat16),
            neg_here[:, None].astype(jnp.bfloat16),
        ],
        axis=1,
    )
    send = jnp.concatenate(
        [column_chunks, jnp.broadcast_to(compact[None], (n_dp,) + compact.shape)], axis=2
    )
    recv = lax.all_to_all(send, "dp", split_axis=0, concat_axis=0, tiled=True)
    recv, emb_grad = lax.optimization_barrier((recv, emb_grad))
    columns = recv[:, :, :col_width].reshape(n_dp * group, col_width)
    info = recv[:, :, col_width:].reshape(n_dp * group, compact.shape[1])
    all_pos = info[:, :SUB_SIZE]
    all_neg = info[:, SUB_SIZE : 2 * SUB_SIZE]
    all_pos_blk = info[:, 2 * SUB_SIZE].astype(jnp.int32)
    all_neg_blk = info[:, 2 * SUB_SIZE + 1].astype(jnp.int32)
    all_table = block_table(all_pos, all_pos_blk, all_neg, all_neg_blk, blocks).astype(jnp.bfloat16)
    node_grad = lax.dot_general(
        all_table, columns, (((0,), (0,)), ((), ())), preferred_element_type=jnp.float32
    )

    spread = jnp.dot(select.T, emb_grad / P_SIZE, precision=HIGHEST, preferred_element_type=jnp.float32)
    pixel_gradient = spread * (sig * (1.0 + shifted * (1.0 - sig)))
    lin_grad = (pixel_gradient * gain).astype(jnp.bfloat16)
    head_term = lax.dot_general(
        lin_grad, features, (((0,), (0,)), ((), ())), preferred_element_type=jnp.float32
    )
    gain_term = jnp.sum(pixel_gradient * linear_scores, axis=0)
    shift_term = jnp.sum(pixel_gradient, axis=0)
    e_size = head_term.shape[1]
    chunk = width // n_dp
    extra = -(-2 * chunk // e_size)
    side_rows = jnp.stack([gain_term, shift_term], axis=1).reshape(n_dp, 2 * chunk)
    side_rows = jnp.pad(side_rows, ((0, 0), (0, extra * e_size - 2 * chunk)))
    stacked = jnp.concatenate(
        [head_term.reshape(n_dp, chunk, e_size), side_rows.reshape(n_dp, extra, e_size)], axis=1
    )
    (part,) = halving_scatter([stacked], "dp")
    (total,) = butterfly_sum([part[0]], "leaf")
    side_sum = total[chunk:].reshape(-1)[: 2 * chunk].reshape(chunk, 2)
    return (total[:chunk].T, side_sum[:, 0], side_sum[:, 1], node_grad)


def solution(mesh):
    in_specs = (P(("dp", "leaf"), None), P(), P(), P(), P("leaf", None), P(), P("dp", None))
    out_specs = (P(None, "dp"), P("dp"), P("dp"), P("leaf", "dp"))
    return jax.shard_map(shards, mesh=mesh, in_specs=in_specs, out_specs=out_specs, check_vma=False)
```

```python
import jax
import jax.numpy as jnp
from jax import lax
from jax.sharding import PartitionSpec as P

P_SIZE = 100
SUB_SIZE = 64
KPOS = 16
HIGHEST = lax.Precision.HIGHEST


def block_table(pos_vec, pos_blk, neg_vec, neg_blk, blocks):
    lane_block = jnp.arange(blocks * SUB_SIZE, dtype=jnp.int32)[None, :] // SUB_SIZE
    pos_wide = jnp.tile(pos_vec, (1, blocks))
    neg_wide = jnp.tile(neg_vec, (1, blocks))
    pos_part = jnp.where(lane_block == pos_blk[:, None], pos_wide, 0.0)
    neg_part = jnp.where(lane_block == neg_blk[:, None], neg_wide, 0.0)
    return pos_part + neg_part


def pick_block(values, blk, blocks):
    rows = values.shape[0]
    split = values.reshape(rows, blocks, SUB_SIZE)
    hit = jnp.arange(blocks, dtype=jnp.int32)[None, :, None] == blk[:, None, None]
    return jnp.sum(jnp.where(hit, split, 0.0), axis=1)


def lane_mask(ids, valid):
    column = jnp.arange(SUB_SIZE, dtype=jnp.int32)[None, None, :]
    hit = ((ids % SUB_SIZE)[:, :, None] == column) & valid[:, :, None]
    return jnp.any(hit, axis=1)


def partners(size, bit):
    return [(i, i ^ (1 << bit)) for i in range(size)]


def doubling_gather(x, name):
    size = lax.axis_size(name)
    idx = lax.axis_index(name)
    cur = x[None]
    bit = 0
    while (1 << bit) < size:
        other = lax.ppermute(cur, name, partners(size, bit))
        low = (idx // (1 << bit)) % 2 == 0
        cur = jnp.where(low, jnp.concatenate([cur, other], 0), jnp.concatenate([other, cur], 0))
        bit += 1
    return cur.reshape((size * x.shape[0],) + x.shape[1:])


def halving_scatter(parts, name):
    size = lax.axis_size(name)
    idx = lax.axis_index(name)
    cur = [p.reshape((size, p.shape[0] // size) + p.shape[1:]) for p in parts]
    bit = 0
    while (1 << bit) < size:
        mine = (idx // (1 << bit)) % 2
        pairs = [c.reshape((c.shape[0] // 2, 2) + c.shape[1:]) for c in cur]
        keep = [lax.dynamic_index_in_dim(p, mine, axis=1, keepdims=False) for p in pairs]
        give = [lax.dynamic_index_in_dim(p, 1 - mine, axis=1, keepdims=False) for p in pairs]
        got = lax.ppermute(tuple(give), name, partners(size, bit))
        cur = [k + g for k, g in zip(keep, got)]
        bit += 1
    return [c.reshape(c.shape[1:]) for c in cur]


def butterfly_sum(parts, name):
    size = lax.axis_size(name)
    cur = tuple(parts)
    bit = 0
    while (1 << bit) < size:
        got = lax.ppermute(cur, name, partners(size, bit))
        cur = tuple(c + g for c, g in zip(cur, got))
        bit += 1
    return cur


def halve_steps(x, name, axis, bits):
    idx = lax.axis_index(name)
    size = lax.axis_size(name)
    for bit in bits:
        n = x.shape[axis]
        pairs = x.reshape(x.shape[:axis] + (n // 2, 2) + x.shape[axis + 1 :])
        mine = (idx // (1 << bit)) % 2
        keep = lax.dynamic_index_in_dim(pairs, mine, axis + 1, keepdims=False)
        give = lax.dynamic_index_in_dim(pairs, 1 - mine, axis + 1, keepdims=False)
        x = keep + lax.ppermute(give, name, partners(size, bit))
    return x


def double_steps(x, name, axis, bits):
    idx = lax.axis_index(name)
    size = lax.axis_size(name)
    for bit in bits:
        other = lax.ppermute(x, name, partners(size, bit))
        low = (idx // (1 << bit)) % 2 == 0
        x = jnp.where(low, jnp.concatenate([x, other], axis), jnp.concatenate([other, x], axis))
    return x


def axis_bits(name):
    size = lax.axis_size(name)
    bit = 0
    while (1 << bit) < size:
        bit += 1
    return list(range(bit))


def shards(features, head_weight, gain, shift, node_weights, subtree_map, node_ids):
    rows = features.shape[0]
    images_here = rows // P_SIZE
    width = head_weight.shape[1]
    slots_dev = node_weights.shape[0]
    blocks = slots_dev // SUB_SIZE
    n_dp = lax.axis_size("dp")
    leaf = lax.axis_index("leaf")

    select = (
        jnp.arange(rows, dtype=jnp.int32)[None, :] // P_SIZE
        == jnp.arange(images_here, dtype=jnp.int32)[:, None]
    ).astype(jnp.float32)

    linear_scores = jnp.dot(features, head_weight, preferred_element_type=jnp.float32)
    shifted = gain * linear_scores + shift
    sig = jax.nn.sigmoid(shifted)
    active = shifted * sig
    image_sum = jnp.dot(select, active, precision=HIGHEST, preferred_element_type=jnp.float32)
    embedded = (image_sum / P_SIZE).astype(jnp.bfloat16)
    grouped = doubling_gather(embedded, "leaf")
    group = grouped.shape[0]

    valid = node_ids >= 0
    safe_ids = jnp.where(valid, node_ids, 0)
    subtree_ids = jnp.arange(subtree_map.shape[0], dtype=jnp.int32)[None, :]
    lead_sub = safe_ids[:, jnp.array([0, KPOS])] // SUB_SIZE
    pos_block = jnp.sum(jnp.where(lead_sub[:, :1] == subtree_ids, subtree_map[None, :], 0), axis=1)
    neg_block = jnp.sum(jnp.where(lead_sub[:, 1:] == subtree_ids, subtree_map[None, :], 0), axis=1)
    pos_here = jnp.where(pos_block // blocks == leaf, pos_block % blocks, -1)
    neg_here = jnp.where(neg_block // blocks == leaf, neg_block % blocks, -1)
    pos_mask = lane_mask(safe_ids[:, :KPOS], valid[:, :KPOS])
    neg_mask = lane_mask(safe_ids[:, KPOS:], valid[:, KPOS:])

    scores = lax.dot_general(
        grouped, node_weights, (((1,), (1,)), ((), ())), preferred_element_type=jnp.float32
    )
    pos_logit = pick_block(scores, pos_here, blocks)
    neg_logit = pick_block(scores, neg_here, blocks)
    pos_coef = jnp.where(pos_mask & (pos_here >= 0)[:, None], jax.nn.sigmoid(pos_logit) - 1.0, 0.0)
    neg_coef = jnp.where(neg_mask & (neg_here >= 0)[:, None], jax.nn.sigmoid(neg_logit), 0.0)
    pos_coef = pos_coef.astype(jnp.bfloat16)
    neg_coef = neg_coef.astype(jnp.bfloat16)
    table = block_table(pos_coef, pos_here, neg_coef, neg_here, blocks).astype(jnp.bfloat16)
    grad_part = jnp.dot(table, node_weights, preferred_element_type=jnp.float32)
    (emb_grad,) = halving_scatter([grad_part], "leaf")

    col_width = width // n_dp
    column_chunks = grouped.reshape(group, n_dp, col_width).transpose(1, 0, 2)
    compact = jnp.concatenate(
        [
            pos_coef,
            neg_coef,
            pos_here[:, None].astype(jnp.bfloat16),
            neg_here[:, None].astype(jnp.bfloat16),
        ],
        axis=1,
    )
    send = jnp.concatenate(
        [column_chunks, jnp.broadcast_to(compact[None], (n_dp,) + compact.shape)], axis=2
    )
    recv = lax.all_to_all(send, "dp", split_axis=0, concat_axis=0, tiled=True)
    columns = recv[:, :, :col_width].reshape(n_dp * group, col_width)
    info = recv[:, :, col_width:].reshape(n_dp * group, compact.shape[1])
    all_pos = info[:, :SUB_SIZE]
    all_neg = info[:, SUB_SIZE : 2 * SUB_SIZE]
    all_pos_blk = info[:, 2 * SUB_SIZE].astype(jnp.int32)
    all_neg_blk = info[:, 2 * SUB_SIZE + 1].astype(jnp.int32)
    all_table = block_table(all_pos, all_pos_blk, all_neg, all_neg_blk, blocks).astype(jnp.bfloat16)
    node_grad = lax.dot_general(
        all_table, columns, (((0,), (0,)), ((), ())), preferred_element_type=jnp.float32
    )

    spread = jnp.dot(select.T, emb_grad / P_SIZE, precision=HIGHEST, preferred_element_type=jnp.float32)
    pixel_gradient = spread * (sig * (1.0 + shifted * (1.0 - sig)))
    lin_grad = (pixel_gradient * gain).astype(jnp.bfloat16)
    head_term = lax.dot_general(
        lin_grad, features, (((0,), (0,)), ((), ())), preferred_element_type=jnp.float32
    )
    gain_term = jnp.sum(pixel_gradient * linear_scores, axis=0)
    shift_term = jnp.sum(pixel_gradient, axis=0)
    e_size = head_term.shape[1]
    chunk = width // n_dp
    extra = -(-2 * chunk // e_size)
    n_leaf = lax.axis_size("leaf")
    padded = -(-(chunk + extra) // (8 * n_leaf)) * 8 * n_leaf
    side_rows = jnp.stack([gain_term, shift_term], axis=1).reshape(n_dp, 2 * chunk)
    side_rows = jnp.pad(side_rows, ((0, 0), (0, extra * e_size - 2 * chunk)))
    stacked = jnp.concatenate(
        [
            head_term.reshape(n_dp, chunk, e_size),
            side_rows.reshape(n_dp, extra, e_size),
            jnp.zeros((n_dp, padded - chunk - extra, e_size), jnp.float32),
        ],
        axis=1,
    )
    dbits = axis_bits("dp")
    lbits = axis_bits("leaf")
    part = halve_steps(stacked, "dp", 0, dbits[:1])
    part = part.reshape(part.shape[0], n_leaf, padded // n_leaf, e_size)
    part = halve_steps(part, "leaf", 1, lbits)
    part = halve_steps(part, "dp", 0, dbits[1:])
    total = double_steps(part, "leaf", 1, lbits).reshape(padded, e_size)
    side_sum = total[chunk : chunk + extra].reshape(-1)[: 2 * chunk].reshape(chunk, 2)
    return (total[:chunk].T, side_sum[:, 0], side_sum[:, 1], node_grad)


def solution(mesh):
    in_specs = (P(("dp", "leaf"), None), P(), P(), P(), P("leaf", None), P(), P("dp", None))
    out_specs = (P(None, "dp"), P("dp"), P("dp"), P("leaf", "dp"))
    return jax.shard_map(shards, mesh=mesh, in_specs=in_specs, out_specs=out_specs, check_vma=False)
```

```python
import jax
import jax.numpy as jnp
from jax import lax
from jax.sharding import PartitionSpec as P

P_SIZE = 100
SUB_SIZE = 64
KPOS = 16
HIGHEST = lax.Precision.HIGHEST


def block_table(pos_vec, pos_blk, neg_vec, neg_blk, blocks):
    lane_block = jnp.arange(blocks * SUB_SIZE, dtype=jnp.int32)[None, :] // SUB_SIZE
    pos_wide = jnp.tile(pos_vec, (1, blocks))
    neg_wide = jnp.tile(neg_vec, (1, blocks))
    pos_part = jnp.where(lane_block == pos_blk[:, None], pos_wide, 0.0)
    neg_part = jnp.where(lane_block == neg_blk[:, None], neg_wide, 0.0)
    return pos_part + neg_part


def pick_block(values, blk, blocks):
    rows = values.shape[0]
    split = values.reshape(rows, blocks, SUB_SIZE)
    hit = jnp.arange(blocks, dtype=jnp.int32)[None, :, None] == blk[:, None, None]
    return jnp.sum(jnp.where(hit, split, 0.0), axis=1)


def lane_mask(ids, valid):
    column = jnp.arange(SUB_SIZE, dtype=jnp.int32)[None, None, :]
    hit = ((ids % SUB_SIZE)[:, :, None] == column) & valid[:, :, None]
    return jnp.any(hit, axis=1)


def partners(size, bit):
    return [(i, i ^ (1 << bit)) for i in range(size)]


def doubling_gather(x, name):
    size = lax.axis_size(name)
    idx = lax.axis_index(name)
    cur = x[None]
    bit = 0
    while (1 << bit) < size:
        other = lax.ppermute(cur, name, partners(size, bit))
        low = (idx // (1 << bit)) % 2 == 0
        cur = jnp.where(low, jnp.concatenate([cur, other], 0), jnp.concatenate([other, cur], 0))
        bit += 1
    return cur.reshape((size * x.shape[0],) + x.shape[1:])


def halving_scatter(parts, name):
    size = lax.axis_size(name)
    idx = lax.axis_index(name)
    cur = [p.reshape((size, p.shape[0] // size) + p.shape[1:]) for p in parts]
    bit = 0
    while (1 << bit) < size:
        mine = (idx // (1 << bit)) % 2
        pairs = [c.reshape((c.shape[0] // 2, 2) + c.shape[1:]) for c in cur]
        keep = [lax.dynamic_index_in_dim(p, mine, axis=1, keepdims=False) for p in pairs]
        give = [lax.dynamic_index_in_dim(p, 1 - mine, axis=1, keepdims=False) for p in pairs]
        got = lax.ppermute(tuple(give), name, partners(size, bit))
        cur = [k + g for k, g in zip(keep, got)]
        bit += 1
    return [c.reshape(c.shape[1:]) for c in cur]


def butterfly_sum(parts, name):
    size = lax.axis_size(name)
    cur = tuple(parts)
    bit = 0
    while (1 << bit) < size:
        got = lax.ppermute(cur, name, partners(size, bit))
        cur = tuple(c + g for c, g in zip(cur, got))
        bit += 1
    return cur


def direct_gather(x, name):
    size = lax.axis_size(name)
    idx = lax.axis_index(name)
    got = [x] + [lax.ppermute(x, name, [(i, i ^ k) for i in range(size)]) for k in range(1, size)]
    order = jnp.bitwise_xor(jnp.arange(size, dtype=jnp.int32), idx)
    return jnp.take(jnp.stack(got), order, axis=0).reshape((size * x.shape[0],) + x.shape[1:])


def direct_scatter(x, name):
    size = lax.axis_size(name)
    idx = lax.axis_index(name)
    blocks = x.reshape((size, x.shape[0] // size) + x.shape[1:])
    total = lax.dynamic_index_in_dim(blocks, idx, 0, keepdims=False)
    for k in range(1, size):
        give = lax.dynamic_index_in_dim(blocks, jnp.bitwise_xor(idx, k), 0, keepdims=False)
        total = total + lax.ppermute(give, name, [(i, i ^ k) for i in range(size)])
    return total


def shards(features, head_weight, gain, shift, node_weights, subtree_map, node_ids):
    rows = features.shape[0]
    images_here = rows // P_SIZE
    width = head_weight.shape[1]
    slots_dev = node_weights.shape[0]
    blocks = slots_dev // SUB_SIZE
    n_dp = lax.axis_size("dp")
    leaf = lax.axis_index("leaf")

    select = (
        jnp.arange(rows, dtype=jnp.int32)[None, :] // P_SIZE
        == jnp.arange(images_here, dtype=jnp.int32)[:, None]
    ).astype(jnp.float32)

    linear_scores = jnp.dot(features, head_weight, preferred_element_type=jnp.float32)
    shifted = gain * linear_scores + shift
    sig = jax.nn.sigmoid(shifted)
    active = shifted * sig
    image_sum = jnp.dot(select, active, precision=HIGHEST, preferred_element_type=jnp.float32)
    embedded = (image_sum / P_SIZE).astype(jnp.bfloat16)
    direct = lax.axis_size("leaf") <= 4
    grouped = direct_gather(embedded, "leaf") if direct else doubling_gather(embedded, "leaf")
    group = grouped.shape[0]

    valid = node_ids >= 0
    safe_ids = jnp.where(valid, node_ids, 0)
    subtree_ids = jnp.arange(subtree_map.shape[0], dtype=jnp.int32)[None, :]
    lead_sub = safe_ids[:, jnp.array([0, KPOS])] // SUB_SIZE
    pos_block = jnp.sum(jnp.where(lead_sub[:, :1] == subtree_ids, subtree_map[None, :], 0), axis=1)
    neg_block = jnp.sum(jnp.where(lead_sub[:, 1:] == subtree_ids, subtree_map[None, :], 0), axis=1)
    pos_here = jnp.where(pos_block // blocks == leaf, pos_block % blocks, -1)
    neg_here = jnp.where(neg_block // blocks == leaf, neg_block % blocks, -1)
    pos_mask = lane_mask(safe_ids[:, :KPOS], valid[:, :KPOS])
    neg_mask = lane_mask(safe_ids[:, KPOS:], valid[:, KPOS:])

    scores = lax.dot_general(
        grouped, node_weights, (((1,), (1,)), ((), ())), preferred_element_type=jnp.float32
    )
    pos_logit = pick_block(scores, pos_here, blocks)
    neg_logit = pick_block(scores, neg_here, blocks)
    pos_coef = jnp.where(pos_mask & (pos_here >= 0)[:, None], jax.nn.sigmoid(pos_logit) - 1.0, 0.0)
    neg_coef = jnp.where(neg_mask & (neg_here >= 0)[:, None], jax.nn.sigmoid(neg_logit), 0.0)
    pos_coef = pos_coef.astype(jnp.bfloat16)
    neg_coef = neg_coef.astype(jnp.bfloat16)
    table = block_table(pos_coef, pos_here, neg_coef, neg_here, blocks).astype(jnp.bfloat16)
    grad_part = jnp.dot(table, node_weights, preferred_element_type=jnp.float32)
    if direct:
        emb_grad = direct_scatter(grad_part, "leaf")
    else:
        (emb_grad,) = halving_scatter([grad_part], "leaf")

    col_width = width // n_dp
    column_chunks = grouped.reshape(group, n_dp, col_width).transpose(1, 0, 2)
    compact = jnp.concatenate(
        [
            pos_coef,
            neg_coef,
            pos_here[:, None].astype(jnp.bfloat16),
            neg_here[:, None].astype(jnp.bfloat16),
        ],
        axis=1,
    )
    send = jnp.concatenate(
        [column_chunks, jnp.broadcast_to(compact[None], (n_dp,) + compact.shape)], axis=2
    )
    recv = lax.all_to_all(send, "dp", split_axis=0, concat_axis=0, tiled=True)
    columns = recv[:, :, :col_width].reshape(n_dp * group, col_width)
    info = recv[:, :, col_width:].reshape(n_dp * group, compact.shape[1])
    all_pos = info[:, :SUB_SIZE]
    all_neg = info[:, SUB_SIZE : 2 * SUB_SIZE]
    all_pos_blk = info[:, 2 * SUB_SIZE].astype(jnp.int32)
    all_neg_blk = info[:, 2 * SUB_SIZE + 1].astype(jnp.int32)
    all_table = block_table(all_pos, all_pos_blk, all_neg, all_neg_blk, blocks).astype(jnp.bfloat16)
    node_grad = lax.dot_general(
        all_table, columns, (((0,), (0,)), ((), ())), preferred_element_type=jnp.float32
    )

    spread = jnp.dot(select.T, emb_grad / P_SIZE, precision=HIGHEST, preferred_element_type=jnp.float32)
    pixel_gradient = spread * (sig * (1.0 + shifted * (1.0 - sig)))
    lin_grad = (pixel_gradient * gain).astype(jnp.bfloat16)
    head_term = lax.dot_general(
        lin_grad, features, (((0,), (0,)), ((), ())), preferred_element_type=jnp.float32
    )
    gain_term = jnp.sum(pixel_gradient * linear_scores, axis=0)
    shift_term = jnp.sum(pixel_gradient, axis=0)
    e_size = head_term.shape[1]
    chunk = width // n_dp
    extra = -(-2 * chunk // e_size)
    side_rows = jnp.stack([gain_term, shift_term], axis=1).reshape(n_dp, 2 * chunk)
    side_rows = jnp.pad(side_rows, ((0, 0), (0, extra * e_size - 2 * chunk)))
    stacked = jnp.concatenate(
        [head_term.reshape(n_dp, chunk, e_size), side_rows.reshape(n_dp, extra, e_size)], axis=1
    )
    (part,) = halving_scatter([stacked], "dp")
    (total,) = butterfly_sum([part[0]], "leaf")
    side_sum = total[chunk:].reshape(-1)[: 2 * chunk].reshape(chunk, 2)
    return (total[:chunk].T, side_sum[:, 0], side_sum[:, 1], node_grad)


def solution(mesh):
    in_specs = (P(("dp", "leaf"), None), P(), P(), P(), P("leaf", None), P(), P("dp", None))
    out_specs = (P(None, "dp"), P("dp"), P("dp"), P("leaf", "dp"))
    return jax.shard_map(shards, mesh=mesh, in_specs=in_specs, out_specs=out_specs, check_vma=False)
```

```python
import jax
import jax.numpy as jnp
from jax import lax
from jax.sharding import PartitionSpec as P

P_SIZE = 100
SUB_SIZE = 64
KPOS = 16
HIGHEST = lax.Precision.HIGHEST


def block_table(pos_vec, pos_blk, neg_vec, neg_blk, blocks):
    lane_block = jnp.arange(blocks * SUB_SIZE, dtype=jnp.int32)[None, :] // SUB_SIZE
    pos_wide = jnp.tile(pos_vec, (1, blocks))
    neg_wide = jnp.tile(neg_vec, (1, blocks))
    pos_part = jnp.where(lane_block == pos_blk[:, None], pos_wide, 0.0)
    neg_part = jnp.where(lane_block == neg_blk[:, None], neg_wide, 0.0)
    return pos_part + neg_part


def pick_block(values, blk, blocks):
    rows = values.shape[0]
    split = values.reshape(rows, blocks, SUB_SIZE)
    hit = jnp.arange(blocks, dtype=jnp.int32)[None, :, None] == blk[:, None, None]
    return jnp.sum(jnp.where(hit, split, 0.0), axis=1)


def lane_mask(ids, valid):
    column = jnp.arange(SUB_SIZE, dtype=jnp.int32)[None, None, :]
    hit = ((ids % SUB_SIZE)[:, :, None] == column) & valid[:, :, None]
    return jnp.any(hit, axis=1)


def partners(size, bit):
    return [(i, i ^ (1 << bit)) for i in range(size)]


def doubling_gather(x, name):
    size = lax.axis_size(name)
    idx = lax.axis_index(name)
    cur = x[None]
    bit = 0
    while (1 << bit) < size:
        other = lax.ppermute(cur, name, partners(size, bit))
        low = (idx // (1 << bit)) % 2 == 0
        cur = jnp.where(low, jnp.concatenate([cur, other], 0), jnp.concatenate([other, cur], 0))
        bit += 1
    return cur.reshape((size * x.shape[0],) + x.shape[1:])


def halving_scatter(parts, name):
    size = lax.axis_size(name)
    idx = lax.axis_index(name)
    cur = [p.reshape((size, p.shape[0] // size) + p.shape[1:]) for p in parts]
    bit = 0
    while (1 << bit) < size:
        mine = (idx // (1 << bit)) % 2
        pairs = [c.reshape((c.shape[0] // 2, 2) + c.shape[1:]) for c in cur]
        keep = [lax.dynamic_index_in_dim(p, mine, axis=1, keepdims=False) for p in pairs]
        give = [lax.dynamic_index_in_dim(p, 1 - mine, axis=1, keepdims=False) for p in pairs]
        got = lax.ppermute(tuple(give), name, partners(size, bit))
        cur = [k + g for k, g in zip(keep, got)]
        bit += 1
    return [c.reshape(c.shape[1:]) for c in cur]


def butterfly_sum(parts, name):
    size = lax.axis_size(name)
    cur = tuple(parts)
    bit = 0
    while (1 << bit) < size:
        got = lax.ppermute(cur, name, partners(size, bit))
        cur = tuple(c + g for c, g in zip(cur, got))
        bit += 1
    return cur


def shards(features, head_weight, gain, shift, node_weights, subtree_map, node_ids):
    rows = features.shape[0]
    images_here = rows // P_SIZE
    width = head_weight.shape[1]
    slots_dev = node_weights.shape[0]
    blocks = slots_dev // SUB_SIZE
    n_dp = lax.axis_size("dp")
    leaf = lax.axis_index("leaf")

    select = (
        jnp.arange(rows, dtype=jnp.int32)[None, :] // P_SIZE
        == jnp.arange(images_here, dtype=jnp.int32)[:, None]
    ).astype(jnp.float32)

    linear_scores = jnp.dot(features, head_weight, preferred_element_type=jnp.float32)
    shifted = gain * linear_scores + shift
    sig = jax.nn.sigmoid(shifted)
    active = shifted * sig
    image_sum = jnp.dot(select, active, precision=HIGHEST, preferred_element_type=jnp.float32)
    embedded = (image_sum / P_SIZE).astype(jnp.bfloat16)
    grouped = doubling_gather(embedded, "leaf")
    group = grouped.shape[0]

    valid = node_ids >= 0
    safe_ids = jnp.where(valid, node_ids, 0)
    subtree_ids = jnp.arange(subtree_map.shape[0], dtype=jnp.int32)[None, :]
    lead_sub = safe_ids[:, jnp.array([0, KPOS])] // SUB_SIZE
    pos_block = jnp.sum(jnp.where(lead_sub[:, :1] == subtree_ids, subtree_map[None, :], 0), axis=1)
    neg_block = jnp.sum(jnp.where(lead_sub[:, 1:] == subtree_ids, subtree_map[None, :], 0), axis=1)
    pos_here = jnp.where(pos_block // blocks == leaf, pos_block % blocks, -1)
    neg_here = jnp.where(neg_block // blocks == leaf, neg_block % blocks, -1)
    pos_mask = lane_mask(safe_ids[:, :KPOS], valid[:, :KPOS])
    neg_mask = lane_mask(safe_ids[:, KPOS:], valid[:, KPOS:])

    scores = lax.dot_general(
        grouped, node_weights, (((1,), (1,)), ((), ())), preferred_element_type=jnp.float32
    )
    pos_logit = pick_block(scores, pos_here, blocks)
    neg_logit = pick_block(scores, neg_here, blocks)
    pos_coef = jnp.where(pos_mask & (pos_here >= 0)[:, None], jax.nn.sigmoid(pos_logit) - 1.0, 0.0)
    neg_coef = jnp.where(neg_mask & (neg_here >= 0)[:, None], jax.nn.sigmoid(neg_logit), 0.0)
    pos_coef = pos_coef.astype(jnp.bfloat16)
    neg_coef = neg_coef.astype(jnp.bfloat16)
    table = block_table(pos_coef, pos_here, neg_coef, neg_here, blocks).astype(jnp.bfloat16)
    grad_part = jnp.dot(table, node_weights, preferred_element_type=jnp.float32)
    (emb_grad,) = halving_scatter([grad_part], "leaf")

    col_width = width // n_dp
    column_chunks = grouped.reshape(group, n_dp, col_width).transpose(1, 0, 2)
    compact = jnp.concatenate(
        [
            pos_coef,
            neg_coef,
            pos_here[:, None].astype(jnp.bfloat16),
            neg_here[:, None].astype(jnp.bfloat16),
        ],
        axis=1,
    )
    send = jnp.concatenate(
        [column_chunks, jnp.broadcast_to(compact[None], (n_dp,) + compact.shape)], axis=2
    )
    recv = lax.all_to_all(send, "dp", split_axis=0, concat_axis=0, tiled=True)
    columns = recv[:, :, :col_width].reshape(n_dp * group, col_width)
    info = recv[:, :, col_width:].reshape(n_dp * group, compact.shape[1])
    all_pos = info[:, :SUB_SIZE]
    all_neg = info[:, SUB_SIZE : 2 * SUB_SIZE]
    all_pos_blk = info[:, 2 * SUB_SIZE].astype(jnp.int32)
    all_neg_blk = info[:, 2 * SUB_SIZE + 1].astype(jnp.int32)
    all_table = block_table(all_pos, all_pos_blk, all_neg, all_neg_blk, blocks).astype(jnp.bfloat16)
    node_grad = lax.dot_general(
        all_table, columns, (((0,), (0,)), ((), ())), preferred_element_type=jnp.float32
    )

    spread = jnp.dot(select.T, emb_grad / P_SIZE, precision=HIGHEST, preferred_element_type=jnp.float32)
    pixel_gradient = spread * (sig * (1.0 + shifted * (1.0 - sig)))
    lin_grad = (pixel_gradient * gain).astype(jnp.bfloat16)
    head_term = lax.dot_general(
        lin_grad, features, (((0,), (0,)), ((), ())), preferred_element_type=jnp.float32
    )
    gain_term = jnp.sum(pixel_gradient * linear_scores, axis=0)
    shift_term = jnp.sum(pixel_gradient, axis=0)
    e_size = head_term.shape[1]
    chunk = width // n_dp
    extra = -(-2 * chunk // e_size)
    pad_rows = -(-extra // 8) * 8
    side_rows = jnp.concatenate(
        [gain_term.reshape(n_dp, chunk), shift_term.reshape(n_dp, chunk)], axis=1
    )
    side_rows = jnp.pad(side_rows, ((0, 0), (0, pad_rows * e_size - 2 * chunk)))
    stacked = jnp.concatenate(
        [head_term.reshape(n_dp, chunk, e_size), side_rows.reshape(n_dp, pad_rows, e_size)], axis=1
    )
    (part,) = halving_scatter([stacked], "dp")
    (total,) = butterfly_sum([part[0]], "leaf")
    side_flat = total[chunk:].reshape(-1)
    side_sum = jnp.stack([side_flat[:chunk], side_flat[chunk : 2 * chunk]], axis=1)
    return (total[:chunk].T, side_sum[:, 0], side_sum[:, 1], node_grad)


def solution(mesh):
    in_specs = (P(("dp", "leaf"), None), P(), P(), P(), P("leaf", None), P(), P("dp", None))
    out_specs = (P(None, "dp"), P("dp"), P("dp"), P("leaf", "dp"))
    return jax.shard_map(shards, mesh=mesh, in_specs=in_specs, out_specs=out_specs, check_vma=False)
```

```python
import jax
import jax.numpy as jnp
from jax import lax
from jax.sharding import PartitionSpec as P

P_SIZE = 100
SUB_SIZE = 64
KPOS = 16
HIGHEST = lax.Precision.HIGHEST


def block_table(pos_vec, pos_blk, neg_vec, neg_blk, blocks):
    lane_block = jnp.arange(blocks * SUB_SIZE, dtype=jnp.int32)[None, :] // SUB_SIZE
    pos_wide = jnp.tile(pos_vec, (1, blocks))
    neg_wide = jnp.tile(neg_vec, (1, blocks))
    pos_part = jnp.where(lane_block == pos_blk[:, None], pos_wide, 0.0)
    neg_part = jnp.where(lane_block == neg_blk[:, None], neg_wide, 0.0)
    return pos_part + neg_part


def pick_block(values, blk, blocks):
    rows = values.shape[0]
    split = values.reshape(rows, blocks, SUB_SIZE)
    hit = jnp.arange(blocks, dtype=jnp.int32)[None, :, None] == blk[:, None, None]
    return jnp.sum(jnp.where(hit, split, 0.0), axis=1)


def lane_mask(ids, valid):
    column = jnp.arange(SUB_SIZE, dtype=jnp.int32)[None, None, :]
    hit = ((ids % SUB_SIZE)[:, :, None] == column) & valid[:, :, None]
    return jnp.any(hit, axis=1)


def split3(x):
    hi = lax.reduce_precision(x, exponent_bits=8, mantissa_bits=7)
    rest = x - hi
    mid = lax.reduce_precision(rest, exponent_bits=8, mantissa_bits=7)
    lo = rest - mid
    return hi.astype(jnp.bfloat16), mid.astype(jnp.bfloat16), lo.astype(jnp.bfloat16)


def partners(size, bit):
    return [(i, i ^ (1 << bit)) for i in range(size)]


def doubling_gather(x, name):
    size = lax.axis_size(name)
    idx = lax.axis_index(name)
    cur = x[None]
    bit = 0
    while (1 << bit) < size:
        other = lax.ppermute(cur, name, partners(size, bit))
        low = (idx // (1 << bit)) % 2 == 0
        cur = jnp.where(low, jnp.concatenate([cur, other], 0), jnp.concatenate([other, cur], 0))
        bit += 1
    return cur.reshape((size * x.shape[0],) + x.shape[1:])


def halving_scatter(parts, name):
    size = lax.axis_size(name)
    idx = lax.axis_index(name)
    cur = [p.reshape((size, p.shape[0] // size) + p.shape[1:]) for p in parts]
    bit = 0
    while (1 << bit) < size:
        mine = (idx // (1 << bit)) % 2
        pairs = [c.reshape((c.shape[0] // 2, 2) + c.shape[1:]) for c in cur]
        keep = [lax.dynamic_index_in_dim(p, mine, axis=1, keepdims=False) for p in pairs]
        give = [lax.dynamic_index_in_dim(p, 1 - mine, axis=1, keepdims=False) for p in pairs]
        got = lax.ppermute(tuple(give), name, partners(size, bit))
        cur = [k + g for k, g in zip(keep, got)]
        bit += 1
    return [c.reshape(c.shape[1:]) for c in cur]


def butterfly_sum(parts, name):
    size = lax.axis_size(name)
    cur = tuple(parts)
    bit = 0
    while (1 << bit) < size:
        got = lax.ppermute(cur, name, partners(size, bit))
        cur = tuple(c + g for c, g in zip(cur, got))
        bit += 1
    return cur


def shards(features, head_weight, gain, shift, node_weights, subtree_map, node_ids):
    rows = features.shape[0]
    images_here = rows // P_SIZE
    width = head_weight.shape[1]
    slots_dev = node_weights.shape[0]
    blocks = slots_dev // SUB_SIZE
    n_dp = lax.axis_size("dp")
    leaf = lax.axis_index("leaf")

    select = (
        jnp.arange(rows, dtype=jnp.int32)[None, :] // P_SIZE
        == jnp.arange(images_here, dtype=jnp.int32)[:, None]
    ).astype(jnp.float32)

    linear_scores = jnp.dot(features, head_weight, preferred_element_type=jnp.float32)
    shifted = gain * linear_scores + shift
    sig = jax.nn.sigmoid(shifted)
    active = shifted * sig
    image_sum = jnp.dot(select, active, precision=HIGHEST, preferred_element_type=jnp.float32)
    embedded = (image_sum / P_SIZE).astype(jnp.bfloat16)
    grouped = doubling_gather(embedded, "leaf")
    group = grouped.shape[0]

    valid = node_ids >= 0
    safe_ids = jnp.where(valid, node_ids, 0)
    subtree_ids = jnp.arange(subtree_map.shape[0], dtype=jnp.int32)[None, :]
    lead_sub = safe_ids[:, jnp.array([0, KPOS])] // SUB_SIZE
    pos_block = jnp.sum(jnp.where(lead_sub[:, :1] == subtree_ids, subtree_map[None, :], 0), axis=1)
    neg_block = jnp.sum(jnp.where(lead_sub[:, 1:] == subtree_ids, subtree_map[None, :], 0), axis=1)
    pos_here = jnp.where(pos_block // blocks == leaf, pos_block % blocks, -1)
    neg_here = jnp.where(neg_block // blocks == leaf, neg_block % blocks, -1)
    pos_mask = lane_mask(safe_ids[:, :KPOS], valid[:, :KPOS])
    neg_mask = lane_mask(safe_ids[:, KPOS:], valid[:, KPOS:])

    scores = lax.dot_general(
        grouped, node_weights, (((1,), (1,)), ((), ())), preferred_element_type=jnp.float32
    )
    pos_logit = pick_block(scores, pos_here, blocks)
    neg_logit = pick_block(scores, neg_here, blocks)
    pos_coef = jnp.where(pos_mask & (pos_here >= 0)[:, None], jax.nn.sigmoid(pos_logit) - 1.0, 0.0)
    neg_coef = jnp.where(neg_mask & (neg_here >= 0)[:, None], jax.nn.sigmoid(neg_logit), 0.0)
    pos_coef = pos_coef.astype(jnp.bfloat16)
    neg_coef = neg_coef.astype(jnp.bfloat16)
    table = block_table(pos_coef, pos_here, neg_coef, neg_here, blocks).astype(jnp.bfloat16)
    grad_part = jnp.dot(table, node_weights, preferred_element_type=jnp.float32)
    (emb_grad,) = halving_scatter([grad_part], "leaf")

    col_width = width // n_dp
    column_chunks = grouped.reshape(group, n_dp, col_width).transpose(1, 0, 2)
    compact = jnp.concatenate(
        [
            pos_coef,
            neg_coef,
            pos_here[:, None].astype(jnp.bfloat16),
            neg_here[:, None].astype(jnp.bfloat16),
        ],
        axis=1,
    )
    send = jnp.concatenate(
        [column_chunks, jnp.broadcast_to(compact[None], (n_dp,) + compact.shape)], axis=2
    )
    recv = lax.all_to_all(send, "dp", split_axis=0, concat_axis=0, tiled=True)
    columns = recv[:, :, :col_width].reshape(n_dp * group, col_width)
    info = recv[:, :, col_width:].reshape(n_dp * group, compact.shape[1])
    all_pos = info[:, :SUB_SIZE]
    all_neg = info[:, SUB_SIZE : 2 * SUB_SIZE]
    all_pos_blk = info[:, 2 * SUB_SIZE].astype(jnp.int32)
    all_neg_blk = info[:, 2 * SUB_SIZE + 1].astype(jnp.int32)
    all_table = block_table(all_pos, all_pos_blk, all_neg, all_neg_blk, blocks).astype(jnp.bfloat16)
    node_grad = lax.dot_general(
        all_table, columns, (((0,), (0,)), ((), ())), preferred_element_type=jnp.float32
    )

    spread = jnp.dot(
        jnp.concatenate([select.T.astype(jnp.bfloat16)] * 3, axis=1),
        jnp.concatenate(split3(emb_grad / P_SIZE), axis=0),
        preferred_element_type=jnp.float32,
    )
    pixel_gradient = spread * (sig * (1.0 + shifted * (1.0 - sig)))
    lin_grad = (pixel_gradient * gain).astype(jnp.bfloat16)
    head_term = lax.dot_general(
        lin_grad, features, (((0,), (0,)), ((), ())), preferred_element_type=jnp.float32
    )
    gain_term = jnp.sum(pixel_gradient * linear_scores, axis=0)
    shift_term = jnp.sum(pixel_gradient, axis=0)
    e_size = head_term.shape[1]
    chunk = width // n_dp
    extra = -(-2 * chunk // e_size)
    pad_rows = -(-extra // 8) * 8
    side_rows = jnp.concatenate(
        [gain_term.reshape(n_dp, chunk), shift_term.reshape(n_dp, chunk)], axis=1
    )
    side_rows = jnp.pad(side_rows, ((0, 0), (0, pad_rows * e_size - 2 * chunk)))
    stacked = jnp.concatenate(
        [head_term.reshape(n_dp, chunk, e_size), side_rows.reshape(n_dp, pad_rows, e_size)], axis=1
    )
    (part,) = halving_scatter([stacked], "dp")
    (total,) = butterfly_sum([part[0]], "leaf")
    side_flat = total[chunk:].reshape(-1)
    side_sum = jnp.stack([side_flat[:chunk], side_flat[chunk : 2 * chunk]], axis=1)
    return (total[:chunk].T, side_sum[:, 0], side_sum[:, 1], node_grad)


def solution(mesh):
    in_specs = (P(("dp", "leaf"), None), P(), P(), P(), P("leaf", None), P(), P("dp", None))
    out_specs = (P(None, "dp"), P("dp"), P("dp"), P("leaf", "dp"))
    return jax.shard_map(shards, mesh=mesh, in_specs=in_specs, out_specs=out_specs, check_vma=False)
```

```python
import jax
import jax.numpy as jnp
from jax import lax
from jax.sharding import PartitionSpec as P

P_SIZE = 100
SUB_SIZE = 64
KPOS = 16
HIGHEST = lax.Precision.HIGHEST


def block_table(pos_vec, pos_blk, neg_vec, neg_blk, blocks):
    lane_block = jnp.arange(blocks * SUB_SIZE, dtype=jnp.int32)[None, :] // SUB_SIZE
    pos_wide = jnp.tile(pos_vec, (1, blocks))
    neg_wide = jnp.tile(neg_vec, (1, blocks))
    pos_part = jnp.where(lane_block == pos_blk[:, None], pos_wide, 0.0)
    neg_part = jnp.where(lane_block == neg_blk[:, None], neg_wide, 0.0)
    return pos_part + neg_part


def pick_block(values, blk, blocks):
    rows = values.shape[0]
    split = values.reshape(rows, blocks, SUB_SIZE)
    hit = jnp.arange(blocks, dtype=jnp.int32)[None, :, None] == blk[:, None, None]
    return jnp.sum(jnp.where(hit, split, 0.0), axis=1)


def lane_mask(ids, valid):
    column = jnp.arange(SUB_SIZE, dtype=jnp.int32)[None, None, :]
    hit = ((ids % SUB_SIZE)[:, :, None] == column) & valid[:, :, None]
    return jnp.any(hit, axis=1)


def split3(x):
    hi = lax.reduce_precision(x, exponent_bits=8, mantissa_bits=7)
    rest = x - hi
    mid = lax.reduce_precision(rest, exponent_bits=8, mantissa_bits=7)
    lo = rest - mid
    return hi.astype(jnp.bfloat16), mid.astype(jnp.bfloat16), lo.astype(jnp.bfloat16)


def partners(size, bit):
    return [(i, i ^ (1 << bit)) for i in range(size)]


def doubling_gather(x, name):
    size = lax.axis_size(name)
    idx = lax.axis_index(name)
    cur = x[None]
    bit = 0
    while (1 << bit) < size:
        other = lax.ppermute(cur, name, partners(size, bit))
        low = (idx // (1 << bit)) % 2 == 0
        cur = jnp.where(low, jnp.concatenate([cur, other], 0), jnp.concatenate([other, cur], 0))
        bit += 1
    return cur.reshape((size * x.shape[0],) + x.shape[1:])


def halving_scatter(parts, name):
    size = lax.axis_size(name)
    idx = lax.axis_index(name)
    cur = [p.reshape((size, p.shape[0] // size) + p.shape[1:]) for p in parts]
    bit = 0
    while (1 << bit) < size:
        mine = (idx // (1 << bit)) % 2
        pairs = [c.reshape((c.shape[0] // 2, 2) + c.shape[1:]) for c in cur]
        keep = [lax.dynamic_index_in_dim(p, mine, axis=1, keepdims=False) for p in pairs]
        give = [lax.dynamic_index_in_dim(p, 1 - mine, axis=1, keepdims=False) for p in pairs]
        got = lax.ppermute(tuple(give), name, partners(size, bit))
        cur = [k + g for k, g in zip(keep, got)]
        bit += 1
    return [c.reshape(c.shape[1:]) for c in cur]


def butterfly_sum(parts, name):
    size = lax.axis_size(name)
    cur = tuple(parts)
    bit = 0
    while (1 << bit) < size:
        got = lax.ppermute(cur, name, partners(size, bit))
        cur = tuple(c + g for c, g in zip(cur, got))
        bit += 1
    return cur


def direct_scatter(x, name):
    size = lax.axis_size(name)
    idx = lax.axis_index(name)
    blocks = x.reshape((size, x.shape[0] // size) + x.shape[1:])
    total = lax.dynamic_index_in_dim(blocks, idx, 0, keepdims=False)
    for k in range(1, size):
        give = lax.dynamic_index_in_dim(blocks, jnp.bitwise_xor(idx, k), 0, keepdims=False)
        total = total + lax.ppermute(give, name, [(i, i ^ k) for i in range(size)])
    return total


def shards(features, head_weight, gain, shift, node_weights, subtree_map, node_ids):
    rows = features.shape[0]
    images_here = rows // P_SIZE
    width = head_weight.shape[1]
    slots_dev = node_weights.shape[0]
    blocks = slots_dev // SUB_SIZE
    n_dp = lax.axis_size("dp")
    leaf = lax.axis_index("leaf")

    select = (
        jnp.arange(rows, dtype=jnp.int32)[None, :] // P_SIZE
        == jnp.arange(images_here, dtype=jnp.int32)[:, None]
    ).astype(jnp.float32)

    linear_scores = jnp.dot(features, head_weight, preferred_element_type=jnp.float32)
    shifted = gain * linear_scores + shift
    sig = jax.nn.sigmoid(shifted)
    active = shifted * sig
    image_sum = jnp.dot(select, active, precision=HIGHEST, preferred_element_type=jnp.float32)
    embedded = (image_sum / P_SIZE).astype(jnp.bfloat16)
    grouped = doubling_gather(embedded, "leaf")
    group = grouped.shape[0]

    valid = node_ids >= 0
    safe_ids = jnp.where(valid, node_ids, 0)
    subtree_ids = jnp.arange(subtree_map.shape[0], dtype=jnp.int32)[None, :]
    lead_sub = safe_ids[:, jnp.array([0, KPOS])] // SUB_SIZE
    pos_block = jnp.sum(jnp.where(lead_sub[:, :1] == subtree_ids, subtree_map[None, :], 0), axis=1)
    neg_block = jnp.sum(jnp.where(lead_sub[:, 1:] == subtree_ids, subtree_map[None, :], 0), axis=1)
    pos_here = jnp.where(pos_block // blocks == leaf, pos_block % blocks, -1)
    neg_here = jnp.where(neg_block // blocks == leaf, neg_block % blocks, -1)
    pos_mask = lane_mask(safe_ids[:, :KPOS], valid[:, :KPOS])
    neg_mask = lane_mask(safe_ids[:, KPOS:], valid[:, KPOS:])

    scores = lax.dot_general(
        grouped, node_weights, (((1,), (1,)), ((), ())), preferred_element_type=jnp.float32
    )
    pos_logit = pick_block(scores, pos_here, blocks)
    neg_logit = pick_block(scores, neg_here, blocks)
    pos_coef = jnp.where(pos_mask & (pos_here >= 0)[:, None], jax.nn.sigmoid(pos_logit) - 1.0, 0.0)
    neg_coef = jnp.where(neg_mask & (neg_here >= 0)[:, None], jax.nn.sigmoid(neg_logit), 0.0)
    pos_coef = pos_coef.astype(jnp.bfloat16)
    neg_coef = neg_coef.astype(jnp.bfloat16)
    table = block_table(pos_coef, pos_here, neg_coef, neg_here, blocks).astype(jnp.bfloat16)
    grad_part = jnp.dot(table, node_weights, preferred_element_type=jnp.float32)
    if lax.axis_size("leaf") <= 4:
        emb_grad = direct_scatter(grad_part, "leaf")
    else:
        (emb_grad,) = halving_scatter([grad_part], "leaf")

    col_width = width // n_dp
    column_chunks = grouped.reshape(group, n_dp, col_width).transpose(1, 0, 2)
    compact = jnp.concatenate(
        [
            pos_coef,
            neg_coef,
            pos_here[:, None].astype(jnp.bfloat16),
            neg_here[:, None].astype(jnp.bfloat16),
        ],
        axis=1,
    )
    send = jnp.concatenate(
        [column_chunks, jnp.broadcast_to(compact[None], (n_dp,) + compact.shape)], axis=2
    )
    recv = lax.all_to_all(send, "dp", split_axis=0, concat_axis=0, tiled=True)
    columns = recv[:, :, :col_width].reshape(n_dp * group, col_width)
    info = recv[:, :, col_width:].reshape(n_dp * group, compact.shape[1])
    all_pos = info[:, :SUB_SIZE]
    all_neg = info[:, SUB_SIZE : 2 * SUB_SIZE]
    all_pos_blk = info[:, 2 * SUB_SIZE].astype(jnp.int32)
    all_neg_blk = info[:, 2 * SUB_SIZE + 1].astype(jnp.int32)
    all_table = block_table(all_pos, all_pos_blk, all_neg, all_neg_blk, blocks).astype(jnp.bfloat16)
    node_grad = lax.dot_general(
        all_table, columns, (((0,), (0,)), ((), ())), preferred_element_type=jnp.float32
    )

    spread = jnp.dot(
        jnp.concatenate([select.T.astype(jnp.bfloat16)] * 3, axis=1),
        jnp.concatenate(split3(emb_grad / P_SIZE), axis=0),
        preferred_element_type=jnp.float32,
    )
    pixel_gradient = spread * (sig * (1.0 + shifted * (1.0 - sig)))
    lin_grad = (pixel_gradient * gain).astype(jnp.bfloat16)
    head_term = lax.dot_general(
        lin_grad, features, (((0,), (0,)), ((), ())), preferred_element_type=jnp.float32
    )
    gain_term = jnp.sum(pixel_gradient * linear_scores, axis=0)
    shift_term = jnp.sum(pixel_gradient, axis=0)
    e_size = head_term.shape[1]
    chunk = width // n_dp
    extra = -(-2 * chunk // e_size)
    pad_rows = -(-extra // 8) * 8
    side_rows = jnp.concatenate(
        [gain_term.reshape(n_dp, chunk), shift_term.reshape(n_dp, chunk)], axis=1
    )
    side_rows = jnp.pad(side_rows, ((0, 0), (0, pad_rows * e_size - 2 * chunk)))
    stacked = jnp.concatenate(
        [head_term.reshape(n_dp, chunk, e_size), side_rows.reshape(n_dp, pad_rows, e_size)], axis=1
    )
    (part,) = halving_scatter([stacked], "dp")
    (total,) = butterfly_sum([part[0]], "leaf")
    side_flat = total[chunk:].reshape(-1)
    side_sum = jnp.stack([side_flat[:chunk], side_flat[chunk : 2 * chunk]], axis=1)
    return (total[:chunk].T, side_sum[:, 0], side_sum[:, 1], node_grad)


def solution(mesh):
    in_specs = (P(("dp", "leaf"), None), P(), P(), P(), P("leaf", None), P(), P("dp", None))
    out_specs = (P(None, "dp"), P("dp"), P("dp"), P("leaf", "dp"))
    return jax.shard_map(shards, mesh=mesh, in_specs=in_specs, out_specs=out_specs, check_vma=False)
```

```python
import jax
import jax.numpy as jnp
from jax import lax
from jax.sharding import PartitionSpec as P

P_SIZE = 100
SUB_SIZE = 64
KPOS = 16
HIGHEST = lax.Precision.HIGHEST


def block_table(pos_vec, pos_blk, neg_vec, neg_blk, blocks):
    lane_block = jnp.arange(blocks * SUB_SIZE, dtype=jnp.int32)[None, :] // SUB_SIZE
    pos_wide = jnp.tile(pos_vec, (1, blocks))
    neg_wide = jnp.tile(neg_vec, (1, blocks))
    pos_part = jnp.where(lane_block == pos_blk[:, None], pos_wide, 0.0)
    neg_part = jnp.where(lane_block == neg_blk[:, None], neg_wide, 0.0)
    return pos_part + neg_part


def pick_block(values, blk, blocks):
    rows = values.shape[0]
    split = values.reshape(rows, blocks, SUB_SIZE)
    hit = jnp.arange(blocks, dtype=jnp.int32)[None, :, None] == blk[:, None, None]
    return jnp.sum(jnp.where(hit, split, 0.0), axis=1)


def lane_mask(ids, valid):
    column = jnp.arange(SUB_SIZE, dtype=jnp.int32)[None, None, :]
    hit = ((ids % SUB_SIZE)[:, :, None] == column) & valid[:, :, None]
    return jnp.any(hit, axis=1)


def split3(x):
    hi = lax.reduce_precision(x, exponent_bits=8, mantissa_bits=7)
    rest = x - hi
    mid = lax.reduce_precision(rest, exponent_bits=8, mantissa_bits=7)
    lo = rest - mid
    return hi.astype(jnp.bfloat16), mid.astype(jnp.bfloat16), lo.astype(jnp.bfloat16)


def partners(size, bit):
    return [(i, i ^ (1 << bit)) for i in range(size)]


def doubling_gather(x, name):
    size = lax.axis_size(name)
    idx = lax.axis_index(name)
    cur = x[None]
    bit = 0
    while (1 << bit) < size:
        other = lax.ppermute(cur, name, partners(size, bit))
        low = (idx // (1 << bit)) % 2 == 0
        cur = jnp.where(low, jnp.concatenate([cur, other], 0), jnp.concatenate([other, cur], 0))
        bit += 1
    return cur.reshape((size * x.shape[0],) + x.shape[1:])


def halving_scatter(parts, name):
    size = lax.axis_size(name)
    idx = lax.axis_index(name)
    cur = [p.reshape((size, p.shape[0] // size) + p.shape[1:]) for p in parts]
    bit = 0
    while (1 << bit) < size:
        mine = (idx // (1 << bit)) % 2
        pairs = [c.reshape((c.shape[0] // 2, 2) + c.shape[1:]) for c in cur]
        keep = [lax.dynamic_index_in_dim(p, mine, axis=1, keepdims=False) for p in pairs]
        give = [lax.dynamic_index_in_dim(p, 1 - mine, axis=1, keepdims=False) for p in pairs]
        got = lax.ppermute(tuple(give), name, partners(size, bit))
        cur = [k + g for k, g in zip(keep, got)]
        bit += 1
    return [c.reshape(c.shape[1:]) for c in cur]


def butterfly_sum(parts, name):
    size = lax.axis_size(name)
    cur = tuple(parts)
    bit = 0
    while (1 << bit) < size:
        got = lax.ppermute(cur, name, partners(size, bit))
        cur = tuple(c + g for c, g in zip(cur, got))
        bit += 1
    return cur


def direct_scatter(x, name):
    size = lax.axis_size(name)
    idx = lax.axis_index(name)
    blocks = x.reshape((size, x.shape[0] // size) + x.shape[1:])
    total = lax.dynamic_index_in_dim(blocks, idx, 0, keepdims=False)
    for k in range(1, size):
        give = lax.dynamic_index_in_dim(blocks, jnp.bitwise_xor(idx, k), 0, keepdims=False)
        total = total + lax.ppermute(give, name, [(i, i ^ k) for i in range(size)])
    return total


def direct_sum(x, name):
    size = lax.axis_size(name)
    idx = lax.axis_index(name)
    got = [x] + [lax.ppermute(x, name, [(i, i ^ k) for i in range(size)]) for k in range(1, size)]
    stacked = jnp.stack(got)
    order = jnp.bitwise_xor(jnp.arange(size, dtype=jnp.int32), idx)
    total = lax.dynamic_index_in_dim(stacked, order[0], 0, keepdims=False)
    for j in range(1, size):
        total = total + lax.dynamic_index_in_dim(stacked, order[j], 0, keepdims=False)
    return total


def shards(features, head_weight, gain, shift, node_weights, subtree_map, node_ids):
    rows = features.shape[0]
    images_here = rows // P_SIZE
    width = head_weight.shape[1]
    slots_dev = node_weights.shape[0]
    blocks = slots_dev // SUB_SIZE
    n_dp = lax.axis_size("dp")
    leaf = lax.axis_index("leaf")

    select = (
        jnp.arange(rows, dtype=jnp.int32)[None, :] // P_SIZE
        == jnp.arange(images_here, dtype=jnp.int32)[:, None]
    ).astype(jnp.float32)

    linear_scores = jnp.dot(features, head_weight, preferred_element_type=jnp.float32)
    shifted = gain * linear_scores + shift
    sig = jax.nn.sigmoid(shifted)
    active = shifted * sig
    image_sum = jnp.dot(select, active, precision=HIGHEST, preferred_element_type=jnp.float32)
    embedded = (image_sum / P_SIZE).astype(jnp.bfloat16)
    grouped = doubling_gather(embedded, "leaf")
    group = grouped.shape[0]

    valid = node_ids >= 0
    safe_ids = jnp.where(valid, node_ids, 0)
    subtree_ids = jnp.arange(subtree_map.shape[0], dtype=jnp.int32)[None, :]
    lead_sub = safe_ids[:, jnp.array([0, KPOS])] // SUB_SIZE
    pos_block = jnp.sum(jnp.where(lead_sub[:, :1] == subtree_ids, subtree_map[None, :], 0), axis=1)
    neg_block = jnp.sum(jnp.where(lead_sub[:, 1:] == subtree_ids, subtree_map[None, :], 0), axis=1)
    pos_here = jnp.where(pos_block // blocks == leaf, pos_block % blocks, -1)
    neg_here = jnp.where(neg_block // blocks == leaf, neg_block % blocks, -1)
    pos_mask = lane_mask(safe_ids[:, :KPOS], valid[:, :KPOS])
    neg_mask = lane_mask(safe_ids[:, KPOS:], valid[:, KPOS:])

    scores = lax.dot_general(
        grouped, node_weights, (((1,), (1,)), ((), ())), preferred_element_type=jnp.float32
    )
    pos_logit = pick_block(scores, pos_here, blocks)
    neg_logit = pick_block(scores, neg_here, blocks)
    pos_coef = jnp.where(pos_mask & (pos_here >= 0)[:, None], jax.nn.sigmoid(pos_logit) - 1.0, 0.0)
    neg_coef = jnp.where(neg_mask & (neg_here >= 0)[:, None], jax.nn.sigmoid(neg_logit), 0.0)
    pos_coef = pos_coef.astype(jnp.bfloat16)
    neg_coef = neg_coef.astype(jnp.bfloat16)
    table = block_table(pos_coef, pos_here, neg_coef, neg_here, blocks).astype(jnp.bfloat16)
    grad_part = jnp.dot(table, node_weights, preferred_element_type=jnp.float32)
    if lax.axis_size("leaf") <= 4:
        emb_grad = direct_scatter(grad_part, "leaf")
    else:
        (emb_grad,) = halving_scatter([grad_part], "leaf")

    col_width = width // n_dp
    column_chunks = grouped.reshape(group, n_dp, col_width).transpose(1, 0, 2)
    compact = jnp.concatenate(
        [
            pos_coef,
            neg_coef,
            pos_here[:, None].astype(jnp.bfloat16),
            neg_here[:, None].astype(jnp.bfloat16),
        ],
        axis=1,
    )
    send = jnp.concatenate(
        [column_chunks, jnp.broadcast_to(compact[None], (n_dp,) + compact.shape)], axis=2
    )
    recv = lax.all_to_all(send, "dp", split_axis=0, concat_axis=0, tiled=True)
    columns = recv[:, :, :col_width].reshape(n_dp * group, col_width)
    info = recv[:, :, col_width:].reshape(n_dp * group, compact.shape[1])
    all_pos = info[:, :SUB_SIZE]
    all_neg = info[:, SUB_SIZE : 2 * SUB_SIZE]
    all_pos_blk = info[:, 2 * SUB_SIZE].astype(jnp.int32)
    all_neg_blk = info[:, 2 * SUB_SIZE + 1].astype(jnp.int32)
    all_table = block_table(all_pos, all_pos_blk, all_neg, all_neg_blk, blocks).astype(jnp.bfloat16)
    node_grad = lax.dot_general(
        all_table, columns, (((0,), (0,)), ((), ())), preferred_element_type=jnp.float32
    )

    spread = jnp.dot(
        jnp.concatenate([select.T.astype(jnp.bfloat16)] * 3, axis=1),
        jnp.concatenate(split3(emb_grad / P_SIZE), axis=0),
        preferred_element_type=jnp.float32,
    )
    pixel_gradient = spread * (sig * (1.0 + shifted * (1.0 - sig)))
    lin_grad = (pixel_gradient * gain).astype(jnp.bfloat16)
    head_term = lax.dot_general(
        lin_grad, features, (((0,), (0,)), ((), ())), preferred_element_type=jnp.float32
    )
    gain_term = jnp.sum(pixel_gradient * linear_scores, axis=0)
    shift_term = jnp.sum(pixel_gradient, axis=0)
    e_size = head_term.shape[1]
    chunk = width // n_dp
    extra = -(-2 * chunk // e_size)
    pad_rows = -(-extra // 8) * 8
    side_rows = jnp.concatenate(
        [gain_term.reshape(n_dp, chunk), shift_term.reshape(n_dp, chunk)], axis=1
    )
    side_rows = jnp.pad(side_rows, ((0, 0), (0, pad_rows * e_size - 2 * chunk)))
    stacked = jnp.concatenate(
        [head_term.reshape(n_dp, chunk, e_size), side_rows.reshape(n_dp, pad_rows, e_size)], axis=1
    )
    (part,) = halving_scatter([stacked], "dp")
    if lax.axis_size("leaf") <= 4:
        total = direct_sum(part[0], "leaf")
    else:
        (total,) = butterfly_sum([part[0]], "leaf")
    side_flat = total[chunk:].reshape(-1)
    side_sum = jnp.stack([side_flat[:chunk], side_flat[chunk : 2 * chunk]], axis=1)
    return (total[:chunk].T, side_sum[:, 0], side_sum[:, 1], node_grad)


def solution(mesh):
    in_specs = (P(("dp", "leaf"), None), P(), P(), P(), P("leaf", None), P(), P("dp", None))
    out_specs = (P(None, "dp"), P("dp"), P("dp"), P("leaf", "dp"))
    return jax.shard_map(shards, mesh=mesh, in_specs=in_specs, out_specs=out_specs, check_vma=False)
```

```python
import jax
import jax.numpy as jnp
from jax import lax
from jax.sharding import PartitionSpec as P

P_SIZE = 100
SUB_SIZE = 64
KPOS = 16
HIGHEST = lax.Precision.HIGHEST


def block_table(pos_vec, pos_blk, neg_vec, neg_blk, blocks):
    lane_block = jnp.arange(blocks * SUB_SIZE, dtype=jnp.int32)[None, :] // SUB_SIZE
    pos_wide = jnp.tile(pos_vec, (1, blocks))
    neg_wide = jnp.tile(neg_vec, (1, blocks))
    pos_part = jnp.where(lane_block == pos_blk[:, None], pos_wide, 0.0)
    neg_part = jnp.where(lane_block == neg_blk[:, None], neg_wide, 0.0)
    return pos_part + neg_part


def pick_block(values, blk, blocks):
    rows = values.shape[0]
    split = values.reshape(rows, blocks, SUB_SIZE)
    hit = jnp.arange(blocks, dtype=jnp.int32)[None, :, None] == blk[:, None, None]
    return jnp.sum(jnp.where(hit, split, 0.0), axis=1)


def lane_mask(ids, valid):
    column = jnp.arange(SUB_SIZE, dtype=jnp.int32)[None, None, :]
    hit = ((ids % SUB_SIZE)[:, :, None] == column) & valid[:, :, None]
    return jnp.any(hit, axis=1)


def split3(x):
    hi = lax.reduce_precision(x, exponent_bits=8, mantissa_bits=7)
    rest = x - hi
    mid = lax.reduce_precision(rest, exponent_bits=8, mantissa_bits=7)
    lo = rest - mid
    return hi.astype(jnp.bfloat16), mid.astype(jnp.bfloat16), lo.astype(jnp.bfloat16)


def partners(size, bit):
    return [(i, i ^ (1 << bit)) for i in range(size)]


def doubling_gather(x, name):
    size = lax.axis_size(name)
    idx = lax.axis_index(name)
    cur = x[None]
    bit = 0
    while (1 << bit) < size:
        other = lax.ppermute(cur, name, partners(size, bit))
        low = (idx // (1 << bit)) % 2 == 0
        cur = jnp.where(low, jnp.concatenate([cur, other], 0), jnp.concatenate([other, cur], 0))
        bit += 1
    return cur.reshape((size * x.shape[0],) + x.shape[1:])


def halving_scatter(parts, name):
    size = lax.axis_size(name)
    idx = lax.axis_index(name)
    cur = [p.reshape((size, p.shape[0] // size) + p.shape[1:]) for p in parts]
    bit = 0
    while (1 << bit) < size:
        mine = (idx // (1 << bit)) % 2
        pairs = [c.reshape((c.shape[0] // 2, 2) + c.shape[1:]) for c in cur]
        keep = [lax.dynamic_index_in_dim(p, mine, axis=1, keepdims=False) for p in pairs]
        give = [lax.dynamic_index_in_dim(p, 1 - mine, axis=1, keepdims=False) for p in pairs]
        got = lax.ppermute(tuple(give), name, partners(size, bit))
        cur = [k + g for k, g in zip(keep, got)]
        bit += 1
    return [c.reshape(c.shape[1:]) for c in cur]


def butterfly_sum(parts, name):
    size = lax.axis_size(name)
    cur = tuple(parts)
    bit = 0
    while (1 << bit) < size:
        got = lax.ppermute(cur, name, partners(size, bit))
        cur = tuple(c + g for c, g in zip(cur, got))
        bit += 1
    return cur


def direct_scatter(x, name):
    size = lax.axis_size(name)
    idx = lax.axis_index(name)
    blocks = x.reshape((size, x.shape[0] // size) + x.shape[1:])
    total = lax.dynamic_index_in_dim(blocks, idx, 0, keepdims=False)
    for k in range(1, size):
        give = lax.dynamic_index_in_dim(blocks, jnp.bitwise_xor(idx, k), 0, keepdims=False)
        total = total + lax.ppermute(give, name, [(i, i ^ k) for i in range(size)])
    return total


def shards(features, head_weight, gain, shift, node_weights, subtree_map, node_ids):
    rows = features.shape[0]
    images_here = rows // P_SIZE
    width = head_weight.shape[1]
    slots_dev = node_weights.shape[0]
    blocks = slots_dev // SUB_SIZE
    n_dp = lax.axis_size("dp")
    leaf = lax.axis_index("leaf")

    select = (
        jnp.arange(rows, dtype=jnp.int32)[None, :] // P_SIZE
        == jnp.arange(images_here, dtype=jnp.int32)[:, None]
    ).astype(jnp.float32)

    linear_scores = jnp.dot(features, head_weight, preferred_element_type=jnp.float32)
    shifted = gain * linear_scores + shift
    sig = jax.nn.sigmoid(shifted)
    active = shifted * sig
    active_hi = lax.reduce_precision(active, exponent_bits=8, mantissa_bits=7)
    pieces = jnp.concatenate(
        [active_hi.astype(jnp.bfloat16), (active - active_hi).astype(jnp.bfloat16)], axis=0
    )
    image_sum = jnp.dot(
        jnp.concatenate([select.astype(jnp.bfloat16)] * 2, axis=1), pieces, preferred_element_type=jnp.float32
    )
    embedded = (image_sum / P_SIZE).astype(jnp.bfloat16)
    grouped = doubling_gather(embedded, "leaf")
    group = grouped.shape[0]

    valid = node_ids >= 0
    safe_ids = jnp.where(valid, node_ids, 0)
    subtree_ids = jnp.arange(subtree_map.shape[0], dtype=jnp.int32)[None, :]
    lead_sub = safe_ids[:, jnp.array([0, KPOS])] // SUB_SIZE
    pos_block = jnp.sum(jnp.where(lead_sub[:, :1] == subtree_ids, subtree_map[None, :], 0), axis=1)
    neg_block = jnp.sum(jnp.where(lead_sub[:, 1:] == subtree_ids, subtree_map[None, :], 0), axis=1)
    pos_here = jnp.where(pos_block // blocks == leaf, pos_block % blocks, -1)
    neg_here = jnp.where(neg_block // blocks == leaf, neg_block % blocks, -1)
    pos_mask = lane_mask(safe_ids[:, :KPOS], valid[:, :KPOS])
    neg_mask = lane_mask(safe_ids[:, KPOS:], valid[:, KPOS:])

    scores = lax.dot_general(
        grouped, node_weights, (((1,), (1,)), ((), ())), preferred_element_type=jnp.float32
    )
    pos_logit = pick_block(scores, pos_here, blocks)
    neg_logit = pick_block(scores, neg_here, blocks)
    pos_coef = jnp.where(pos_mask & (pos_here >= 0)[:, None], jax.nn.sigmoid(pos_logit) - 1.0, 0.0)
    neg_coef = jnp.where(neg_mask & (neg_here >= 0)[:, None], jax.nn.sigmoid(neg_logit), 0.0)
    pos_coef = pos_coef.astype(jnp.bfloat16)
    neg_coef = neg_coef.astype(jnp.bfloat16)
    table = block_table(pos_coef, pos_here, neg_coef, neg_here, blocks).astype(jnp.bfloat16)
    grad_part = jnp.dot(table, node_weights, preferred_element_type=jnp.float32)
    if lax.axis_size("leaf") <= 4:
        emb_grad = direct_scatter(grad_part, "leaf")
    else:
        (emb_grad,) = halving_scatter([grad_part], "leaf")

    col_width = width // n_dp
    column_chunks = grouped.reshape(group, n_dp, col_width).transpose(1, 0, 2)
    compact = jnp.concatenate(
        [
            pos_coef,
            neg_coef,
            pos_here[:, None].astype(jnp.bfloat16),
            neg_here[:, None].astype(jnp.bfloat16),
        ],
        axis=1,
    )
    send = jnp.concatenate(
        [column_chunks, jnp.broadcast_to(compact[None], (n_dp,) + compact.shape)], axis=2
    )
    recv = lax.all_to_all(send, "dp", split_axis=0, concat_axis=0, tiled=True)
    columns = recv[:, :, :col_width].reshape(n_dp * group, col_width)
    info = recv[:, :, col_width:].reshape(n_dp * group, compact.shape[1])
    all_pos = info[:, :SUB_SIZE]
    all_neg = info[:, SUB_SIZE : 2 * SUB_SIZE]
    all_pos_blk = info[:, 2 * SUB_SIZE].astype(jnp.int32)
    all_neg_blk = info[:, 2 * SUB_SIZE + 1].astype(jnp.int32)
    all_table = block_table(all_pos, all_pos_blk, all_neg, all_neg_blk, blocks).astype(jnp.bfloat16)
    node_grad = lax.dot_general(
        all_table, columns, (((0,), (0,)), ((), ())), preferred_element_type=jnp.float32
    )

    spread = jnp.dot(
        jnp.concatenate([select.T.astype(jnp.bfloat16)] * 3, axis=1),
        jnp.concatenate(split3(emb_grad / P_SIZE), axis=0),
        preferred_element_type=jnp.float32,
    )
    pixel_gradient = spread * (sig * (1.0 + shifted * (1.0 - sig)))
    lin_grad = (pixel_gradient * gain).astype(jnp.bfloat16)
    head_term = lax.dot_general(
        lin_grad, features, (((0,), (0,)), ((), ())), preferred_element_type=jnp.float32
    )
    gain_term = jnp.sum(pixel_gradient * linear_scores, axis=0)
    shift_term = jnp.sum(pixel_gradient, axis=0)
    e_size = head_term.shape[1]
    chunk = width // n_dp
    extra = -(-2 * chunk // e_size)
    pad_rows = -(-extra // 8) * 8
    side_rows = jnp.concatenate(
        [gain_term.reshape(n_dp, chunk), shift_term.reshape(n_dp, chunk)], axis=1
    )
    side_rows = jnp.pad(side_rows, ((0, 0), (0, pad_rows * e_size - 2 * chunk)))
    stacked = jnp.concatenate(
        [head_term.reshape(n_dp, chunk, e_size), side_rows.reshape(n_dp, pad_rows, e_size)], axis=1
    )
    (part,) = halving_scatter([stacked], "dp")
    (total,) = butterfly_sum([part[0]], "leaf")
    side_flat = total[chunk:].reshape(-1)
    side_sum = jnp.stack([side_flat[:chunk], side_flat[chunk : 2 * chunk]], axis=1)
    return (total[:chunk].T, side_sum[:, 0], side_sum[:, 1], node_grad)


def solution(mesh):
    in_specs = (P(("dp", "leaf"), None), P(), P(), P(), P("leaf", None), P(), P("dp", None))
    out_specs = (P(None, "dp"), P("dp"), P("dp"), P("leaf", "dp"))
    return jax.shard_map(shards, mesh=mesh, in_specs=in_specs, out_specs=out_specs, check_vma=False)
```

```python
import jax
import jax.numpy as jnp
from jax import lax
from jax.sharding import PartitionSpec as P

P_SIZE = 100
SUB_SIZE = 64
KPOS = 16
HIGHEST = lax.Precision.HIGHEST


def block_table(pos_vec, pos_blk, neg_vec, neg_blk, blocks):
    lane_block = jnp.arange(blocks * SUB_SIZE, dtype=jnp.int32)[None, :] // SUB_SIZE
    pos_wide = jnp.tile(pos_vec, (1, blocks))
    neg_wide = jnp.tile(neg_vec, (1, blocks))
    pos_part = jnp.where(lane_block == pos_blk[:, None], pos_wide, 0.0)
    neg_part = jnp.where(lane_block == neg_blk[:, None], neg_wide, 0.0)
    return pos_part + neg_part


def pick_block(values, blk, blocks):
    rows = values.shape[0]
    split = values.reshape(rows, blocks, SUB_SIZE)
    hit = jnp.arange(blocks, dtype=jnp.int32)[None, :, None] == blk[:, None, None]
    return jnp.sum(jnp.where(hit, split, 0.0), axis=1)


def lane_mask(ids, valid):
    column = jnp.arange(SUB_SIZE, dtype=jnp.int32)[None, None, :]
    hit = ((ids % SUB_SIZE)[:, :, None] == column) & valid[:, :, None]
    return jnp.any(hit, axis=1)


def split3(x):
    hi = lax.reduce_precision(x, exponent_bits=8, mantissa_bits=7)
    rest = x - hi
    mid = lax.reduce_precision(rest, exponent_bits=8, mantissa_bits=7)
    lo = rest - mid
    return hi.astype(jnp.bfloat16), mid.astype(jnp.bfloat16), lo.astype(jnp.bfloat16)


def partners(size, bit):
    return [(i, i ^ (1 << bit)) for i in range(size)]


def doubling_gather(x, name):
    size = lax.axis_size(name)
    idx = lax.axis_index(name)
    cur = x[None]
    bit = 0
    while (1 << bit) < size:
        other = lax.ppermute(cur, name, partners(size, bit))
        low = (idx // (1 << bit)) % 2 == 0
        cur = jnp.where(low, jnp.concatenate([cur, other], 0), jnp.concatenate([other, cur], 0))
        bit += 1
    return cur.reshape((size * x.shape[0],) + x.shape[1:])


def halving_scatter(parts, name):
    size = lax.axis_size(name)
    idx = lax.axis_index(name)
    cur = [p.reshape((size, p.shape[0] // size) + p.shape[1:]) for p in parts]
    bit = 0
    while (1 << bit) < size:
        mine = (idx // (1 << bit)) % 2
        pairs = [c.reshape((c.shape[0] // 2, 2) + c.shape[1:]) for c in cur]
        keep = [lax.dynamic_index_in_dim(p, mine, axis=1, keepdims=False) for p in pairs]
        give = [lax.dynamic_index_in_dim(p, 1 - mine, axis=1, keepdims=False) for p in pairs]
        got = lax.ppermute(tuple(give), name, partners(size, bit))
        cur = [k + g for k, g in zip(keep, got)]
        bit += 1
    return [c.reshape(c.shape[1:]) for c in cur]


def butterfly_sum(parts, name):
    size = lax.axis_size(name)
    cur = tuple(parts)
    bit = 0
    while (1 << bit) < size:
        got = lax.ppermute(cur, name, partners(size, bit))
        cur = tuple(c + g for c, g in zip(cur, got))
        bit += 1
    return cur


def direct_scatter(x, name):
    size = lax.axis_size(name)
    idx = lax.axis_index(name)
    blocks = x.reshape((size, x.shape[0] // size) + x.shape[1:])
    total = lax.dynamic_index_in_dim(blocks, idx, 0, keepdims=False)
    for k in range(1, size):
        give = lax.dynamic_index_in_dim(blocks, jnp.bitwise_xor(idx, k), 0, keepdims=False)
        total = total + lax.ppermute(give, name, [(i, i ^ k) for i in range(size)])
    return total


def shards(features, head_weight, gain, shift, node_weights, subtree_map, node_ids):
    rows = features.shape[0]
    images_here = rows // P_SIZE
    width = head_weight.shape[1]
    slots_dev = node_weights.shape[0]
    blocks = slots_dev // SUB_SIZE
    n_dp = lax.axis_size("dp")
    leaf = lax.axis_index("leaf")

    select = (
        jnp.arange(rows, dtype=jnp.int32)[None, :] // P_SIZE
        == jnp.arange(images_here, dtype=jnp.int32)[:, None]
    ).astype(jnp.float32)

    linear_scores = jnp.dot(features, head_weight, preferred_element_type=jnp.float32)
    shifted = gain * linear_scores + shift
    sig = jax.nn.sigmoid(shifted)
    active = shifted * sig
    image_sum = jnp.dot(select, active, precision=HIGHEST, preferred_element_type=jnp.float32)
    embedded = (image_sum / P_SIZE).astype(jnp.bfloat16)
    grouped = doubling_gather(embedded, "leaf")
    group = grouped.shape[0]

    valid = node_ids >= 0
    safe_ids = jnp.where(valid, node_ids, 0)
    subtree_ids = jnp.arange(subtree_map.shape[0], dtype=jnp.int32)[None, :]
    lead_sub = safe_ids[:, jnp.array([0, KPOS])] // SUB_SIZE
    pos_block = jnp.sum(jnp.where(lead_sub[:, :1] == subtree_ids, subtree_map[None, :], 0), axis=1)
    neg_block = jnp.sum(jnp.where(lead_sub[:, 1:] == subtree_ids, subtree_map[None, :], 0), axis=1)
    pos_here = jnp.where(pos_block // blocks == leaf, pos_block % blocks, -1)
    neg_here = jnp.where(neg_block // blocks == leaf, neg_block % blocks, -1)
    pos_mask = lane_mask(safe_ids[:, :KPOS], valid[:, :KPOS])
    neg_mask = lane_mask(safe_ids[:, KPOS:], valid[:, KPOS:])

    scores = lax.dot_general(
        grouped, node_weights, (((1,), (1,)), ((), ())), preferred_element_type=jnp.float32
    )
    pos_logit = pick_block(scores, pos_here, blocks)
    neg_logit = pick_block(scores, neg_here, blocks)
    pos_coef = jnp.where(pos_mask & (pos_here >= 0)[:, None], jax.nn.sigmoid(pos_logit) - 1.0, 0.0)
    neg_coef = jnp.where(neg_mask & (neg_here >= 0)[:, None], jax.nn.sigmoid(neg_logit), 0.0)
    pos_coef = pos_coef.astype(jnp.bfloat16)
    neg_coef = neg_coef.astype(jnp.bfloat16)
    table = block_table(pos_coef, pos_here, neg_coef, neg_here, blocks).astype(jnp.bfloat16)
    grad_part = jnp.dot(table, node_weights, preferred_element_type=jnp.float32)
    if lax.axis_size("leaf") <= 4:
        emb_grad = direct_scatter(grad_part, "leaf")
    else:
        (emb_grad,) = halving_scatter([grad_part], "leaf")

    col_width = width // n_dp
    column_chunks = grouped.reshape(group, n_dp, col_width).transpose(1, 0, 2)
    compact = jnp.concatenate(
        [
            pos_coef,
            neg_coef,
            pos_here[:, None].astype(jnp.bfloat16),
            neg_here[:, None].astype(jnp.bfloat16),
        ],
        axis=1,
    )
    send = jnp.concatenate(
        [column_chunks, jnp.broadcast_to(compact[None], (n_dp,) + compact.shape)], axis=2
    )
    spread = jnp.dot(
        jnp.concatenate([select.T.astype(jnp.bfloat16)] * 3, axis=1),
        jnp.concatenate(split3(emb_grad / P_SIZE), axis=0),
        preferred_element_type=jnp.float32,
    )
    pixel_gradient = spread * (sig * (1.0 + shifted * (1.0 - sig)))
    lin_grad = (pixel_gradient * gain).astype(jnp.bfloat16)
    head_term = lax.dot_general(
        lin_grad, features, (((0,), (0,)), ((), ())), preferred_element_type=jnp.float32
    )
    gain_term = jnp.sum(pixel_gradient * linear_scores, axis=0)
    shift_term = jnp.sum(pixel_gradient, axis=0)
    e_size = head_term.shape[1]
    chunk = width // n_dp
    extra = -(-2 * chunk // e_size)
    pad_rows = -(-extra // 8) * 8
    side_rows = jnp.concatenate(
        [gain_term.reshape(n_dp, chunk), shift_term.reshape(n_dp, chunk)], axis=1
    )
    side_rows = jnp.pad(side_rows, ((0, 0), (0, pad_rows * e_size - 2 * chunk)))
    stacked = jnp.concatenate(
        [head_term.reshape(n_dp, chunk, e_size), side_rows.reshape(n_dp, pad_rows, e_size)], axis=1
    )
    (part,) = halving_scatter([stacked], "dp")
    send, part = lax.optimization_barrier((send, part))
    recv = lax.all_to_all(send, "dp", split_axis=0, concat_axis=0, tiled=True)
    columns = recv[:, :, :col_width].reshape(n_dp * group, col_width)
    info = recv[:, :, col_width:].reshape(n_dp * group, compact.shape[1])
    all_pos = info[:, :SUB_SIZE]
    all_neg = info[:, SUB_SIZE : 2 * SUB_SIZE]
    all_pos_blk = info[:, 2 * SUB_SIZE].astype(jnp.int32)
    all_neg_blk = info[:, 2 * SUB_SIZE + 1].astype(jnp.int32)
    all_table = block_table(all_pos, all_pos_blk, all_neg, all_neg_blk, blocks).astype(jnp.bfloat16)
    node_grad = lax.dot_general(
        all_table, columns, (((0,), (0,)), ((), ())), preferred_element_type=jnp.float32
    )

    (total,) = butterfly_sum([part[0]], "leaf")
    side_flat = total[chunk:].reshape(-1)
    side_sum = jnp.stack([side_flat[:chunk], side_flat[chunk : 2 * chunk]], axis=1)
    return (total[:chunk].T, side_sum[:, 0], side_sum[:, 1], node_grad)


def solution(mesh):
    in_specs = (P(("dp", "leaf"), None), P(), P(), P(), P("leaf", None), P(), P("dp", None))
    out_specs = (P(None, "dp"), P("dp"), P("dp"), P("leaf", "dp"))
    return jax.shard_map(shards, mesh=mesh, in_specs=in_specs, out_specs=out_specs, check_vma=False)
```

```python
import jax
import jax.numpy as jnp
from jax import lax
from jax.sharding import PartitionSpec as P

P_SIZE = 100
SUB_SIZE = 64
KPOS = 16
HIGHEST = lax.Precision.HIGHEST


def block_table(pos_vec, pos_blk, neg_vec, neg_blk, blocks):
    lane_block = jnp.arange(blocks * SUB_SIZE, dtype=jnp.int32)[None, :] // SUB_SIZE
    pos_wide = jnp.tile(pos_vec, (1, blocks))
    neg_wide = jnp.tile(neg_vec, (1, blocks))
    pos_part = jnp.where(lane_block == pos_blk[:, None], pos_wide, 0.0)
    neg_part = jnp.where(lane_block == neg_blk[:, None], neg_wide, 0.0)
    return pos_part + neg_part


def pick_block(values, blk, blocks):
    rows = values.shape[0]
    split = values.reshape(rows, blocks, SUB_SIZE)
    hit = jnp.arange(blocks, dtype=jnp.int32)[None, :, None] == blk[:, None, None]
    return jnp.sum(jnp.where(hit, split, 0.0), axis=1)


def lane_mask(ids, valid):
    column = jnp.arange(SUB_SIZE, dtype=jnp.int32)[None, None, :]
    hit = ((ids % SUB_SIZE)[:, :, None] == column) & valid[:, :, None]
    return jnp.any(hit, axis=1)


def split3(x):
    hi = lax.reduce_precision(x, exponent_bits=8, mantissa_bits=7)
    rest = x - hi
    mid = lax.reduce_precision(rest, exponent_bits=8, mantissa_bits=7)
    lo = rest - mid
    return hi.astype(jnp.bfloat16), mid.astype(jnp.bfloat16), lo.astype(jnp.bfloat16)


def partners(size, bit):
    return [(i, i ^ (1 << bit)) for i in range(size)]


def doubling_gather(x, name):
    size = lax.axis_size(name)
    idx = lax.axis_index(name)
    cur = x[None]
    bit = 0
    while (1 << bit) < size:
        other = lax.ppermute(cur, name, partners(size, bit))
        low = (idx // (1 << bit)) % 2 == 0
        cur = jnp.where(low, jnp.concatenate([cur, other], 0), jnp.concatenate([other, cur], 0))
        bit += 1
    return cur.reshape((size * x.shape[0],) + x.shape[1:])


def halving_scatter(parts, name):
    size = lax.axis_size(name)
    idx = lax.axis_index(name)
    cur = [p.reshape((size, p.shape[0] // size) + p.shape[1:]) for p in parts]
    bit = 0
    while (1 << bit) < size:
        mine = (idx // (1 << bit)) % 2
        pairs = [c.reshape((c.shape[0] // 2, 2) + c.shape[1:]) for c in cur]
        keep = [lax.dynamic_index_in_dim(p, mine, axis=1, keepdims=False) for p in pairs]
        give = [lax.dynamic_index_in_dim(p, 1 - mine, axis=1, keepdims=False) for p in pairs]
        got = lax.ppermute(tuple(give), name, partners(size, bit))
        cur = [k + g for k, g in zip(keep, got)]
        bit += 1
    return [c.reshape(c.shape[1:]) for c in cur]


def butterfly_sum(parts, name):
    size = lax.axis_size(name)
    cur = tuple(parts)
    bit = 0
    while (1 << bit) < size:
        got = lax.ppermute(cur, name, partners(size, bit))
        cur = tuple(c + g for c, g in zip(cur, got))
        bit += 1
    return cur


def crossed_sum(x, name, split):
    size = lax.axis_size(name)
    bits = []
    while (1 << len(bits)) < size:
        bits.append(len(bits))
    first, second = x[:split], x[split:]
    for low, high in zip(bits, bits[::-1]):
        first = first + lax.ppermute(first, name, partners(size, low))
        second = second + lax.ppermute(second, name, partners(size, high))
    return jnp.concatenate([first, second], axis=0)


def direct_scatter(x, name):
    size = lax.axis_size(name)
    idx = lax.axis_index(name)
    blocks = x.reshape((size, x.shape[0] // size) + x.shape[1:])
    total = lax.dynamic_index_in_dim(blocks, idx, 0, keepdims=False)
    for k in range(1, size):
        give = lax.dynamic_index_in_dim(blocks, jnp.bitwise_xor(idx, k), 0, keepdims=False)
        total = total + lax.ppermute(give, name, [(i, i ^ k) for i in range(size)])
    return total


def shards(features, head_weight, gain, shift, node_weights, subtree_map, node_ids):
    rows = features.shape[0]
    images_here = rows // P_SIZE
    width = head_weight.shape[1]
    slots_dev = node_weights.shape[0]
    blocks = slots_dev // SUB_SIZE
    n_dp = lax.axis_size("dp")
    leaf = lax.axis_index("leaf")

    select = (
        jnp.arange(rows, dtype=jnp.int32)[None, :] // P_SIZE
        == jnp.arange(images_here, dtype=jnp.int32)[:, None]
    ).astype(jnp.float32)

    linear_scores = jnp.dot(features, head_weight, preferred_element_type=jnp.float32)
    shifted = gain * linear_scores + shift
    sig = jax.nn.sigmoid(shifted)
    active = shifted * sig
    image_sum = jnp.dot(select, active, precision=HIGHEST, preferred_element_type=jnp.float32)
    embedded = (image_sum / P_SIZE).astype(jnp.bfloat16)
    grouped = doubling_gather(embedded, "leaf")
    group = grouped.shape[0]

    valid = node_ids >= 0
    safe_ids = jnp.where(valid, node_ids, 0)
    subtree_ids = jnp.arange(subtree_map.shape[0], dtype=jnp.int32)[None, :]
    lead_sub = safe_ids[:, jnp.array([0, KPOS])] // SUB_SIZE
    pos_block = jnp.sum(jnp.where(lead_sub[:, :1] == subtree_ids, subtree_map[None, :], 0), axis=1)
    neg_block = jnp.sum(jnp.where(lead_sub[:, 1:] == subtree_ids, subtree_map[None, :], 0), axis=1)
    pos_here = jnp.where(pos_block // blocks == leaf, pos_block % blocks, -1)
    neg_here = jnp.where(neg_block // blocks == leaf, neg_block % blocks, -1)
    pos_mask = lane_mask(safe_ids[:, :KPOS], valid[:, :KPOS])
    neg_mask = lane_mask(safe_ids[:, KPOS:], valid[:, KPOS:])

    scores = lax.dot_general(
        grouped, node_weights, (((1,), (1,)), ((), ())), preferred_element_type=jnp.float32
    )
    pos_logit = pick_block(scores, pos_here, blocks)
    neg_logit = pick_block(scores, neg_here, blocks)
    pos_coef = jnp.where(pos_mask & (pos_here >= 0)[:, None], jax.nn.sigmoid(pos_logit) - 1.0, 0.0)
    neg_coef = jnp.where(neg_mask & (neg_here >= 0)[:, None], jax.nn.sigmoid(neg_logit), 0.0)
    pos_coef = pos_coef.astype(jnp.bfloat16)
    neg_coef = neg_coef.astype(jnp.bfloat16)
    table = block_table(pos_coef, pos_here, neg_coef, neg_here, blocks).astype(jnp.bfloat16)
    grad_part = jnp.dot(table, node_weights, preferred_element_type=jnp.float32)
    if lax.axis_size("leaf") <= 4:
        emb_grad = direct_scatter(grad_part, "leaf")
    else:
        (emb_grad,) = halving_scatter([grad_part], "leaf")

    col_width = width // n_dp
    column_chunks = grouped.reshape(group, n_dp, col_width).transpose(1, 0, 2)
    compact = jnp.concatenate(
        [
            pos_coef,
            neg_coef,
            pos_here[:, None].astype(jnp.bfloat16),
            neg_here[:, None].astype(jnp.bfloat16),
        ],
        axis=1,
    )
    send = jnp.concatenate(
        [column_chunks, jnp.broadcast_to(compact[None], (n_dp,) + compact.shape)], axis=2
    )
    recv = lax.all_to_all(send, "dp", split_axis=0, concat_axis=0, tiled=True)
    columns = recv[:, :, :col_width].reshape(n_dp * group, col_width)
    info = recv[:, :, col_width:].reshape(n_dp * group, compact.shape[1])
    all_pos = info[:, :SUB_SIZE]
    all_neg = info[:, SUB_SIZE : 2 * SUB_SIZE]
    all_pos_blk = info[:, 2 * SUB_SIZE].astype(jnp.int32)
    all_neg_blk = info[:, 2 * SUB_SIZE + 1].astype(jnp.int32)
    all_table = block_table(all_pos, all_pos_blk, all_neg, all_neg_blk, blocks).astype(jnp.bfloat16)
    node_grad = lax.dot_general(
        all_table, columns, (((0,), (0,)), ((), ())), preferred_element_type=jnp.float32
    )

    spread = jnp.dot(
        jnp.concatenate([select.T.astype(jnp.bfloat16)] * 3, axis=1),
        jnp.concatenate(split3(emb_grad / P_SIZE), axis=0),
        preferred_element_type=jnp.float32,
    )
    pixel_gradient = spread * (sig * (1.0 + shifted * (1.0 - sig)))
    lin_grad = (pixel_gradient * gain).astype(jnp.bfloat16)
    head_term = lax.dot_general(
        lin_grad, features, (((0,), (0,)), ((), ())), preferred_element_type=jnp.float32
    )
    gain_term = jnp.sum(pixel_gradient * linear_scores, axis=0)
    shift_term = jnp.sum(pixel_gradient, axis=0)
    e_size = head_term.shape[1]
    chunk = width // n_dp
    extra = -(-2 * chunk // e_size)
    pad_rows = -(-extra // 8) * 8
    side_rows = jnp.concatenate(
        [gain_term.reshape(n_dp, chunk), shift_term.reshape(n_dp, chunk)], axis=1
    )
    side_rows = jnp.pad(side_rows, ((0, 0), (0, pad_rows * e_size - 2 * chunk)))
    stacked = jnp.concatenate(
        [head_term.reshape(n_dp, chunk, e_size), side_rows.reshape(n_dp, pad_rows, e_size)], axis=1
    )
    (part,) = halving_scatter([stacked], "dp")
    total = crossed_sum(part[0], "leaf", (chunk + pad_rows) // 16 * 8)
    side_flat = total[chunk:].reshape(-1)
    side_sum = jnp.stack([side_flat[:chunk], side_flat[chunk : 2 * chunk]], axis=1)
    return (total[:chunk].T, side_sum[:, 0], side_sum[:, 1], node_grad)


def solution(mesh):
    in_specs = (P(("dp", "leaf"), None), P(), P(), P(), P("leaf", None), P(), P("dp", None))
    out_specs = (P(None, "dp"), P("dp"), P("dp"), P("leaf", "dp"))
    return jax.shard_map(shards, mesh=mesh, in_specs=in_specs, out_specs=out_specs, check_vma=False)
```

```python
import jax
import jax.numpy as jnp
from jax import lax
from jax.sharding import PartitionSpec as P

P_SIZE = 100
SUB_SIZE = 64
KPOS = 16
HIGHEST = lax.Precision.HIGHEST


def block_table(pos_vec, pos_blk, neg_vec, neg_blk, blocks):
    lane_block = jnp.arange(blocks * SUB_SIZE, dtype=jnp.int32)[None, :] // SUB_SIZE
    pos_wide = jnp.tile(pos_vec, (1, blocks))
    neg_wide = jnp.tile(neg_vec, (1, blocks))
    pos_part = jnp.where(lane_block == pos_blk[:, None], pos_wide, 0.0)
    neg_part = jnp.where(lane_block == neg_blk[:, None], neg_wide, 0.0)
    return pos_part + neg_part


def pick_block(values, blk, blocks):
    rows = values.shape[0]
    split = values.reshape(rows, blocks, SUB_SIZE)
    hit = jnp.arange(blocks, dtype=jnp.int32)[None, :, None] == blk[:, None, None]
    return jnp.sum(jnp.where(hit, split, 0.0), axis=1)


def lane_mask(ids, valid):
    column = jnp.arange(SUB_SIZE, dtype=jnp.int32)[None, None, :]
    hit = ((ids % SUB_SIZE)[:, :, None] == column) & valid[:, :, None]
    return jnp.any(hit, axis=1)


def split3(x):
    hi = lax.reduce_precision(x, exponent_bits=8, mantissa_bits=7)
    rest = x - hi
    mid = lax.reduce_precision(rest, exponent_bits=8, mantissa_bits=7)
    lo = rest - mid
    return hi.astype(jnp.bfloat16), mid.astype(jnp.bfloat16), lo.astype(jnp.bfloat16)


def partners(size, bit):
    return [(i, i ^ (1 << bit)) for i in range(size)]


def doubling_gather(x, name):
    size = lax.axis_size(name)
    idx = lax.axis_index(name)
    cur = x[None]
    bit = 0
    while (1 << bit) < size:
        other = lax.ppermute(cur, name, partners(size, bit))
        low = (idx // (1 << bit)) % 2 == 0
        cur = jnp.where(low, jnp.concatenate([cur, other], 0), jnp.concatenate([other, cur], 0))
        bit += 1
    return cur.reshape((size * x.shape[0],) + x.shape[1:])


def halving_scatter(parts, name):
    size = lax.axis_size(name)
    idx = lax.axis_index(name)
    cur = [p.reshape((size, p.shape[0] // size) + p.shape[1:]) for p in parts]
    bit = 0
    while (1 << bit) < size:
        mine = (idx // (1 << bit)) % 2
        pairs = [c.reshape((c.shape[0] // 2, 2) + c.shape[1:]) for c in cur]
        keep = [lax.dynamic_index_in_dim(p, mine, axis=1, keepdims=False) for p in pairs]
        give = [lax.dynamic_index_in_dim(p, 1 - mine, axis=1, keepdims=False) for p in pairs]
        got = lax.ppermute(tuple(give), name, partners(size, bit))
        cur = [k + g for k, g in zip(keep, got)]
        bit += 1
    return [c.reshape(c.shape[1:]) for c in cur]


def butterfly_sum(parts, name):
    size = lax.axis_size(name)
    cur = tuple(parts)
    bit = 0
    while (1 << bit) < size:
        got = lax.ppermute(cur, name, partners(size, bit))
        cur = tuple(c + g for c, g in zip(cur, got))
        bit += 1
    return cur


def direct_scatter(x, name):
    size = lax.axis_size(name)
    idx = lax.axis_index(name)
    blocks = x.reshape((size, x.shape[0] // size) + x.shape[1:])
    total = lax.dynamic_index_in_dim(blocks, idx, 0, keepdims=False)
    for k in range(1, size):
        give = lax.dynamic_index_in_dim(blocks, jnp.bitwise_xor(idx, k), 0, keepdims=False)
        total = total + lax.ppermute(give, name, [(i, i ^ k) for i in range(size)])
    return total


def shards(features, head_weight, gain, shift, node_weights, subtree_map, node_ids):
    rows = features.shape[0]
    images_here = rows // P_SIZE
    width = head_weight.shape[1]
    slots_dev = node_weights.shape[0]
    blocks = slots_dev // SUB_SIZE
    n_dp = lax.axis_size("dp")
    leaf = lax.axis_index("leaf")

    select = (
        jnp.arange(rows, dtype=jnp.int32)[None, :] // P_SIZE
        == jnp.arange(images_here, dtype=jnp.int32)[:, None]
    ).astype(jnp.float32)

    linear_scores = jnp.dot(features, head_weight, preferred_element_type=jnp.float32)
    shifted = gain * linear_scores + shift
    sig = jax.nn.sigmoid(shifted)
    active = shifted * sig
    image_sum = jnp.dot(select, active, precision=HIGHEST, preferred_element_type=jnp.float32)
    embedded = (image_sum / P_SIZE).astype(jnp.bfloat16)
    grouped = doubling_gather(embedded, "leaf")
    group = grouped.shape[0]

    valid = node_ids >= 0
    safe_ids = jnp.where(valid, node_ids, 0)
    subtree_ids = jnp.arange(subtree_map.shape[0], dtype=jnp.int32)[None, :]
    lead_sub = safe_ids[:, jnp.array([0, KPOS])] // SUB_SIZE
    pos_block = jnp.sum(jnp.where(lead_sub[:, :1] == subtree_ids, subtree_map[None, :], 0), axis=1)
    neg_block = jnp.sum(jnp.where(lead_sub[:, 1:] == subtree_ids, subtree_map[None, :], 0), axis=1)
    pos_here = jnp.where(pos_block // blocks == leaf, pos_block % blocks, -1)
    neg_here = jnp.where(neg_block // blocks == leaf, neg_block % blocks, -1)
    pos_mask = lane_mask(safe_ids[:, :KPOS], valid[:, :KPOS])
    neg_mask = lane_mask(safe_ids[:, KPOS:], valid[:, KPOS:])

    scores = lax.dot_general(
        grouped, node_weights, (((1,), (1,)), ((), ())), preferred_element_type=jnp.float32
    )
    pos_logit = pick_block(scores, pos_here, blocks)
    neg_logit = pick_block(scores, neg_here, blocks)
    pos_coef = jnp.where(pos_mask & (pos_here >= 0)[:, None], jax.nn.sigmoid(pos_logit) - 1.0, 0.0)
    neg_coef = jnp.where(neg_mask & (neg_here >= 0)[:, None], jax.nn.sigmoid(neg_logit), 0.0)
    pos_coef = pos_coef.astype(jnp.bfloat16)
    neg_coef = neg_coef.astype(jnp.bfloat16)
    table = block_table(pos_coef, pos_here, neg_coef, neg_here, blocks).astype(jnp.bfloat16)
    grad_part = jnp.dot(table, node_weights, preferred_element_type=jnp.float32)
    if lax.axis_size("leaf") <= 4:
        emb_grad = direct_scatter(grad_part, "leaf")
    else:
        (emb_grad,) = halving_scatter([grad_part], "leaf")

    col_width = width // n_dp
    column_chunks = grouped.reshape(group, n_dp, col_width).transpose(1, 0, 2)
    compact = jnp.concatenate(
        [
            pos_coef,
            neg_coef,
            pos_here[:, None].astype(jnp.bfloat16),
            neg_here[:, None].astype(jnp.bfloat16),
        ],
        axis=1,
    )
    send = jnp.concatenate(
        [column_chunks, jnp.broadcast_to(compact[None], (n_dp,) + compact.shape)], axis=2
    )
    per_dest = send.shape[1] * send.shape[2]
    if per_dest % 128 == 0:
        flat = lax.all_to_all(
            send.reshape(n_dp, per_dest // 128, 128), "dp", split_axis=0, concat_axis=0, tiled=True
        )
        recv = flat.reshape(send.shape)
    else:
        recv = lax.all_to_all(send, "dp", split_axis=0, concat_axis=0, tiled=True)
    columns = recv[:, :, :col_width].reshape(n_dp * group, col_width)
    info = recv[:, :, col_width:].reshape(n_dp * group, compact.shape[1])
    all_pos = info[:, :SUB_SIZE]
    all_neg = info[:, SUB_SIZE : 2 * SUB_SIZE]
    all_pos_blk = info[:, 2 * SUB_SIZE].astype(jnp.int32)
    all_neg_blk = info[:, 2 * SUB_SIZE + 1].astype(jnp.int32)
    all_table = block_table(all_pos, all_pos_blk, all_neg, all_neg_blk, blocks).astype(jnp.bfloat16)
    node_grad = lax.dot_general(
        all_table, columns, (((0,), (0,)), ((), ())), preferred_element_type=jnp.float32
    )

    spread = jnp.dot(
        jnp.concatenate([select.T.astype(jnp.bfloat16)] * 3, axis=1),
        jnp.concatenate(split3(emb_grad / P_SIZE), axis=0),
        preferred_element_type=jnp.float32,
    )
    pixel_gradient = spread * (sig * (1.0 + shifted * (1.0 - sig)))
    lin_grad = (pixel_gradient * gain).astype(jnp.bfloat16)
    head_term = lax.dot_general(
        lin_grad, features, (((0,), (0,)), ((), ())), preferred_element_type=jnp.float32
    )
    gain_term = jnp.sum(pixel_gradient * linear_scores, axis=0)
    shift_term = jnp.sum(pixel_gradient, axis=0)
    e_size = head_term.shape[1]
    chunk = width // n_dp
    extra = -(-2 * chunk // e_size)
    pad_rows = -(-extra // 8) * 8
    side_rows = jnp.concatenate(
        [gain_term.reshape(n_dp, chunk), shift_term.reshape(n_dp, chunk)], axis=1
    )
    side_rows = jnp.pad(side_rows, ((0, 0), (0, pad_rows * e_size - 2 * chunk)))
    stacked = jnp.concatenate(
        [head_term.reshape(n_dp, chunk, e_size), side_rows.reshape(n_dp, pad_rows, e_size)], axis=1
    )
    (part,) = halving_scatter([stacked], "dp")
    (total,) = butterfly_sum([part[0]], "leaf")
    side_flat = total[chunk:].reshape(-1)
    side_sum = jnp.stack([side_flat[:chunk], side_flat[chunk : 2 * chunk]], axis=1)
    return (total[:chunk].T, side_sum[:, 0], side_sum[:, 1], node_grad)


def solution(mesh):
    in_specs = (P(("dp", "leaf"), None), P(), P(), P(), P("leaf", None), P(), P("dp", None))
    out_specs = (P(None, "dp"), P("dp"), P("dp"), P("leaf", "dp"))
    return jax.shard_map(shards, mesh=mesh, in_specs=in_specs, out_specs=out_specs, check_vma=False)
```

```python
import jax
import jax.numpy as jnp
from jax import lax
from jax.sharding import PartitionSpec as P

P_SIZE = 100
SUB_SIZE = 64
KPOS = 16
HIGHEST = lax.Precision.HIGHEST


def block_table(pos_vec, pos_blk, neg_vec, neg_blk, blocks):
    lane_block = jnp.arange(blocks * SUB_SIZE, dtype=jnp.int32)[None, :] // SUB_SIZE
    pos_wide = jnp.tile(pos_vec, (1, blocks))
    neg_wide = jnp.tile(neg_vec, (1, blocks))
    pos_part = jnp.where(lane_block == pos_blk[:, None], pos_wide, 0.0)
    neg_part = jnp.where(lane_block == neg_blk[:, None], neg_wide, 0.0)
    return pos_part + neg_part


def pick_block(values, blk, blocks):
    rows = values.shape[0]
    split = values.reshape(rows, blocks, SUB_SIZE)
    hit = jnp.arange(blocks, dtype=jnp.int32)[None, :, None] == blk[:, None, None]
    return jnp.sum(jnp.where(hit, split, 0.0), axis=1)


def lane_mask(ids, valid):
    column = jnp.arange(SUB_SIZE, dtype=jnp.int32)[None, None, :]
    hit = ((ids % SUB_SIZE)[:, :, None] == column) & valid[:, :, None]
    return jnp.any(hit, axis=1)


def split3(x):
    hi = lax.reduce_precision(x, exponent_bits=8, mantissa_bits=7)
    rest = x - hi
    mid = lax.reduce_precision(rest, exponent_bits=8, mantissa_bits=7)
    lo = rest - mid
    return hi.astype(jnp.bfloat16), mid.astype(jnp.bfloat16), lo.astype(jnp.bfloat16)


def partners(size, bit):
    return [(i, i ^ (1 << bit)) for i in range(size)]


def doubling_gather(x, name):
    size = lax.axis_size(name)
    idx = lax.axis_index(name)
    cur = x[None]
    bit = 0
    while (1 << bit) < size:
        other = lax.ppermute(cur, name, partners(size, bit))
        low = (idx // (1 << bit)) % 2 == 0
        cur = jnp.where(low, jnp.concatenate([cur, other], 0), jnp.concatenate([other, cur], 0))
        bit += 1
    return cur.reshape((size * x.shape[0],) + x.shape[1:])


def halving_scatter(parts, name):
    size = lax.axis_size(name)
    idx = lax.axis_index(name)
    cur = [p.reshape((size, p.shape[0] // size) + p.shape[1:]) for p in parts]
    bit = 0
    while (1 << bit) < size:
        mine = (idx // (1 << bit)) % 2
        pairs = [c.reshape((c.shape[0] // 2, 2) + c.shape[1:]) for c in cur]
        keep = [lax.dynamic_index_in_dim(p, mine, axis=1, keepdims=False) for p in pairs]
        give = [lax.dynamic_index_in_dim(p, 1 - mine, axis=1, keepdims=False) for p in pairs]
        got = lax.ppermute(tuple(give), name, partners(size, bit))
        cur = [k + g for k, g in zip(keep, got)]
        bit += 1
    return [c.reshape(c.shape[1:]) for c in cur]


def butterfly_sum(parts, name):
    size = lax.axis_size(name)
    cur = tuple(parts)
    bit = 0
    while (1 << bit) < size:
        got = lax.ppermute(cur, name, partners(size, bit))
        cur = tuple(c + g for c, g in zip(cur, got))
        bit += 1
    return cur


def direct_scatter(x, name):
    size = lax.axis_size(name)
    idx = lax.axis_index(name)
    blocks = x.reshape((size, x.shape[0] // size) + x.shape[1:])
    total = lax.dynamic_index_in_dim(blocks, idx, 0, keepdims=False)
    for k in range(1, size):
        give = lax.dynamic_index_in_dim(blocks, jnp.bitwise_xor(idx, k), 0, keepdims=False)
        total = total + lax.ppermute(give, name, [(i, i ^ k) for i in range(size)])
    return total


def shards(features, head_weight, gain, shift, node_weights, subtree_map, node_ids):
    rows = features.shape[0]
    images_here = rows // P_SIZE
    width = head_weight.shape[1]
    slots_dev = node_weights.shape[0]
    blocks = slots_dev // SUB_SIZE
    n_dp = lax.axis_size("dp")
    leaf = lax.axis_index("leaf")

    select = (
        jnp.arange(rows, dtype=jnp.int32)[None, :] // P_SIZE
        == jnp.arange(images_here, dtype=jnp.int32)[:, None]
    ).astype(jnp.float32)

    linear_scores = jnp.dot(features, head_weight, preferred_element_type=jnp.float32)
    shifted = gain * linear_scores + shift
    sig = jax.nn.sigmoid(shifted)
    active = shifted * sig
    image_sum = jnp.dot(select, active, precision=HIGHEST, preferred_element_type=jnp.float32)
    embedded = (image_sum / P_SIZE).astype(jnp.bfloat16)
    grouped = doubling_gather(embedded, "leaf")
    group = grouped.shape[0]

    valid = node_ids >= 0
    safe_ids = jnp.where(valid, node_ids, 0)
    subtree_ids = jnp.arange(subtree_map.shape[0], dtype=jnp.int32)[None, :]
    lead_sub = safe_ids[:, jnp.array([0, KPOS])] // SUB_SIZE
    pos_block = jnp.sum(jnp.where(lead_sub[:, :1] == subtree_ids, subtree_map[None, :], 0), axis=1)
    neg_block = jnp.sum(jnp.where(lead_sub[:, 1:] == subtree_ids, subtree_map[None, :], 0), axis=1)
    pos_here = jnp.where(pos_block // blocks == leaf, pos_block % blocks, -1)
    neg_here = jnp.where(neg_block // blocks == leaf, neg_block % blocks, -1)
    pos_mask = lane_mask(safe_ids[:, :KPOS], valid[:, :KPOS])
    neg_mask = lane_mask(safe_ids[:, KPOS:], valid[:, KPOS:])

    scores = lax.dot_general(
        grouped, node_weights, (((1,), (1,)), ((), ())), preferred_element_type=jnp.float32
    )
    pos_logit = pick_block(scores, pos_here, blocks)
    neg_logit = pick_block(scores, neg_here, blocks)
    pos_coef = jnp.where(pos_mask & (pos_here >= 0)[:, None], jax.nn.sigmoid(pos_logit) - 1.0, 0.0)
    neg_coef = jnp.where(neg_mask & (neg_here >= 0)[:, None], jax.nn.sigmoid(neg_logit), 0.0)
    pos_coef = pos_coef.astype(jnp.bfloat16)
    neg_coef = neg_coef.astype(jnp.bfloat16)
    table = block_table(pos_coef, pos_here, neg_coef, neg_here, blocks).astype(jnp.bfloat16)
    grad_part = jnp.dot(table, node_weights, preferred_element_type=jnp.float32)
    if lax.axis_size("leaf") <= 4:
        emb_grad = direct_scatter(grad_part, "leaf")
    else:
        (emb_grad,) = halving_scatter([grad_part], "leaf")

    col_width = width // n_dp
    column_chunks = grouped.reshape(group, n_dp, col_width).transpose(1, 0, 2)
    compact = jnp.concatenate(
        [
            pos_coef,
            neg_coef,
            pos_here[:, None].astype(jnp.bfloat16),
            neg_here[:, None].astype(jnp.bfloat16),
        ],
        axis=1,
    )
    send = jnp.concatenate(
        [column_chunks, jnp.broadcast_to(compact[None], (n_dp,) + compact.shape)], axis=2
    )
    recv = lax.all_to_all(send, "dp", split_axis=0, concat_axis=0, tiled=True)
    columns = recv[:, :, :col_width].reshape(n_dp * group, col_width)
    info = recv[:, :, col_width:].reshape(n_dp * group, compact.shape[1])
    all_pos = info[:, :SUB_SIZE]
    all_neg = info[:, SUB_SIZE : 2 * SUB_SIZE]
    all_pos_blk = info[:, 2 * SUB_SIZE].astype(jnp.int32)
    all_neg_blk = info[:, 2 * SUB_SIZE + 1].astype(jnp.int32)
    all_table = block_table(all_pos, all_pos_blk, all_neg, all_neg_blk, blocks).astype(jnp.bfloat16)
    node_grad = lax.dot_general(
        all_table, columns, (((0,), (0,)), ((), ())), preferred_element_type=jnp.float32
    )

    spread = jnp.dot(
        jnp.concatenate([select.T.astype(jnp.bfloat16)] * 3, axis=1),
        jnp.concatenate(split3(emb_grad / P_SIZE), axis=0),
        preferred_element_type=jnp.float32,
    )
    pixel_gradient = spread * (sig * (1.0 + shifted * (1.0 - sig)))
    lin_grad = (pixel_gradient * gain).astype(jnp.bfloat16)
    head_term = lax.dot_general(
        lin_grad, features, (((0,), (0,)), ((), ())), preferred_element_type=jnp.float32
    )
    gain_term = jnp.sum(pixel_gradient * linear_scores, axis=0)
    shift_term = jnp.sum(pixel_gradient, axis=0)
    e_size = head_term.shape[1]
    chunk = width // n_dp
    extra = -(-2 * chunk // e_size)
    pad_rows = -(-extra // 8) * 8
    side_rows = jnp.concatenate(
        [gain_term.reshape(n_dp, chunk), shift_term.reshape(n_dp, chunk)], axis=1
    )
    side_rows = jnp.pad(side_rows, ((0, 0), (0, pad_rows * e_size - 2 * chunk)))
    dp_idx = lax.axis_index("dp")
    mine = dp_idx % 2
    head_pairs = head_term.reshape(n_dp // 2, 2, chunk, e_size)
    side_pairs = side_rows.reshape(n_dp // 2, 2, pad_rows, e_size)

    def half(which):
        return jnp.concatenate(
            [
                lax.dynamic_index_in_dim(head_pairs, which, axis=1, keepdims=False),
                lax.dynamic_index_in_dim(side_pairs, which, axis=1, keepdims=False),
            ],
            axis=1,
        )

    part = half(mine) + lax.ppermute(half(1 - mine), "dp", partners(n_dp, 0))
    bit = 1
    while (1 << bit) < n_dp:
        pairs = part.reshape((part.shape[0] // 2, 2) + part.shape[1:])
        own = (dp_idx // (1 << bit)) % 2
        keep = lax.dynamic_index_in_dim(pairs, own, axis=1, keepdims=False)
        give = lax.dynamic_index_in_dim(pairs, 1 - own, axis=1, keepdims=False)
        part = keep + lax.ppermute(give, "dp", partners(n_dp, bit))
        bit += 1
    (total,) = butterfly_sum([part[0]], "leaf")
    side_flat = total[chunk:].reshape(-1)
    side_sum = jnp.stack([side_flat[:chunk], side_flat[chunk : 2 * chunk]], axis=1)
    return (total[:chunk].T, side_sum[:, 0], side_sum[:, 1], node_grad)


def solution(mesh):
    in_specs = (P(("dp", "leaf"), None), P(), P(), P(), P("leaf", None), P(), P("dp", None))
    out_specs = (P(None, "dp"), P("dp"), P("dp"), P("leaf", "dp"))
    return jax.shard_map(shards, mesh=mesh, in_specs=in_specs, out_specs=out_specs, check_vma=False)
```

```python
import jax
import jax.numpy as jnp
from jax import lax
from jax.sharding import PartitionSpec as P

P_SIZE = 100
SUB_SIZE = 64
KPOS = 16
HIGHEST = lax.Precision.HIGHEST


def block_table(pos_vec, pos_blk, neg_vec, neg_blk, blocks):
    lane_block = jnp.arange(blocks * SUB_SIZE, dtype=jnp.int32)[None, :] // SUB_SIZE
    pos_wide = jnp.tile(pos_vec, (1, blocks))
    neg_wide = jnp.tile(neg_vec, (1, blocks))
    pos_part = jnp.where(lane_block == pos_blk[:, None], pos_wide, 0.0)
    neg_part = jnp.where(lane_block == neg_blk[:, None], neg_wide, 0.0)
    return pos_part + neg_part


def pick_block(values, blk, blocks):
    rows = values.shape[0]
    split = values.reshape(rows, blocks, SUB_SIZE)
    hit = jnp.arange(blocks, dtype=jnp.int32)[None, :, None] == blk[:, None, None]
    return jnp.sum(jnp.where(hit, split, 0.0), axis=1)


def lane_mask(ids, valid):
    column = jnp.arange(SUB_SIZE, dtype=jnp.int32)[None, None, :]
    hit = ((ids % SUB_SIZE)[:, :, None] == column) & valid[:, :, None]
    return jnp.any(hit, axis=1)


def split3(x):
    hi = lax.reduce_precision(x, exponent_bits=8, mantissa_bits=7)
    rest = x - hi
    mid = lax.reduce_precision(rest, exponent_bits=8, mantissa_bits=7)
    lo = rest - mid
    return hi.astype(jnp.bfloat16), mid.astype(jnp.bfloat16), lo.astype(jnp.bfloat16)


def partners(size, bit):
    return [(i, i ^ (1 << bit)) for i in range(size)]


def doubling_gather(x, name):
    size = lax.axis_size(name)
    idx = lax.axis_index(name)
    cur = x[None]
    bit = 0
    while (1 << bit) < size:
        other = lax.ppermute(cur, name, partners(size, bit))
        low = (idx // (1 << bit)) % 2 == 0
        cur = jnp.where(low, jnp.concatenate([cur, other], 0), jnp.concatenate([other, cur], 0))
        bit += 1
    return cur.reshape((size * x.shape[0],) + x.shape[1:])


def halving_scatter(parts, name):
    size = lax.axis_size(name)
    idx = lax.axis_index(name)
    cur = [p.reshape((size, p.shape[0] // size) + p.shape[1:]) for p in parts]
    bit = 0
    while (1 << bit) < size:
        mine = (idx // (1 << bit)) % 2
        pairs = [c.reshape((c.shape[0] // 2, 2) + c.shape[1:]) for c in cur]
        keep = [lax.dynamic_index_in_dim(p, mine, axis=1, keepdims=False) for p in pairs]
        give = [lax.dynamic_index_in_dim(p, 1 - mine, axis=1, keepdims=False) for p in pairs]
        got = lax.ppermute(tuple(give), name, partners(size, bit))
        cur = [k + g for k, g in zip(keep, got)]
        bit += 1
    return [c.reshape(c.shape[1:]) for c in cur]


def butterfly_sum(parts, name):
    size = lax.axis_size(name)
    cur = tuple(parts)
    bit = 0
    while (1 << bit) < size:
        got = lax.ppermute(cur, name, partners(size, bit))
        cur = tuple(c + g for c, g in zip(cur, got))
        bit += 1
    return cur


def direct_scatter(x, name):
    size = lax.axis_size(name)
    idx = lax.axis_index(name)
    blocks = x.reshape((size, x.shape[0] // size) + x.shape[1:])
    total = lax.dynamic_index_in_dim(blocks, idx, 0, keepdims=False)
    for k in range(1, size):
        give = lax.dynamic_index_in_dim(blocks, jnp.bitwise_xor(idx, k), 0, keepdims=False)
        total = total + lax.ppermute(give, name, [(i, i ^ k) for i in range(size)])
    return total


def shards(features, head_weight, gain, shift, node_weights, subtree_map, node_ids):
    rows = features.shape[0]
    images_here = rows // P_SIZE
    width = head_weight.shape[1]
    slots_dev = node_weights.shape[0]
    blocks = slots_dev // SUB_SIZE
    n_dp = lax.axis_size("dp")
    leaf = lax.axis_index("leaf")

    select = (
        jnp.arange(rows, dtype=jnp.int32)[None, :] // P_SIZE
        == jnp.arange(images_here, dtype=jnp.int32)[:, None]
    ).astype(jnp.float32)

    linear_scores = jnp.dot(features, head_weight, preferred_element_type=jnp.float32)
    shifted = gain * linear_scores + shift
    sig = jax.nn.sigmoid(shifted)
    active = shifted * sig
    image_sum = jnp.dot(select, active, precision=HIGHEST, preferred_element_type=jnp.float32)
    embedded = (image_sum / P_SIZE).astype(jnp.bfloat16)
    grouped = lax.all_gather(embedded, "leaf", axis=0, tiled=True)
    group = grouped.shape[0]

    valid = node_ids >= 0
    safe_ids = jnp.where(valid, node_ids, 0)
    subtree_ids = jnp.arange(subtree_map.shape[0], dtype=jnp.int32)[None, :]
    lead_sub = safe_ids[:, jnp.array([0, KPOS])] // SUB_SIZE
    pos_block = jnp.sum(jnp.where(lead_sub[:, :1] == subtree_ids, subtree_map[None, :], 0), axis=1)
    neg_block = jnp.sum(jnp.where(lead_sub[:, 1:] == subtree_ids, subtree_map[None, :], 0), axis=1)
    pos_here = jnp.where(pos_block // blocks == leaf, pos_block % blocks, -1)
    neg_here = jnp.where(neg_block // blocks == leaf, neg_block % blocks, -1)
    pos_mask = lane_mask(safe_ids[:, :KPOS], valid[:, :KPOS])
    neg_mask = lane_mask(safe_ids[:, KPOS:], valid[:, KPOS:])

    scores = lax.dot_general(
        grouped, node_weights, (((1,), (1,)), ((), ())), preferred_element_type=jnp.float32
    )
    pos_logit = pick_block(scores, pos_here, blocks)
    neg_logit = pick_block(scores, neg_here, blocks)
    pos_coef = jnp.where(pos_mask & (pos_here >= 0)[:, None], jax.nn.sigmoid(pos_logit) - 1.0, 0.0)
    neg_coef = jnp.where(neg_mask & (neg_here >= 0)[:, None], jax.nn.sigmoid(neg_logit), 0.0)
    pos_coef = pos_coef.astype(jnp.bfloat16)
    neg_coef = neg_coef.astype(jnp.bfloat16)
    table = block_table(pos_coef, pos_here, neg_coef, neg_here, blocks).astype(jnp.bfloat16)
    grad_part = jnp.dot(table, node_weights, preferred_element_type=jnp.float32)
    if lax.axis_size("leaf") <= 4:
        emb_grad = direct_scatter(grad_part, "leaf")
    else:
        (emb_grad,) = halving_scatter([grad_part], "leaf")

    col_width = width // n_dp
    column_chunks = grouped.reshape(group, n_dp, col_width).transpose(1, 0, 2)
    compact = jnp.concatenate(
        [
            pos_coef,
            neg_coef,
            pos_here[:, None].astype(jnp.bfloat16),
            neg_here[:, None].astype(jnp.bfloat16),
        ],
        axis=1,
    )
    send = jnp.concatenate(
        [column_chunks, jnp.broadcast_to(compact[None], (n_dp,) + compact.shape)], axis=2
    )
    recv = lax.all_to_all(send, "dp", split_axis=0, concat_axis=0, tiled=True)
    columns = recv[:, :, :col_width].reshape(n_dp * group, col_width)
    info = recv[:, :, col_width:].reshape(n_dp * group, compact.shape[1])
    all_pos = info[:, :SUB_SIZE]
    all_neg = info[:, SUB_SIZE : 2 * SUB_SIZE]
    all_pos_blk = info[:, 2 * SUB_SIZE].astype(jnp.int32)
    all_neg_blk = info[:, 2 * SUB_SIZE + 1].astype(jnp.int32)
    all_table = block_table(all_pos, all_pos_blk, all_neg, all_neg_blk, blocks).astype(jnp.bfloat16)
    node_grad = lax.dot_general(
        all_table, columns, (((0,), (0,)), ((), ())), preferred_element_type=jnp.float32
    )

    spread = jnp.dot(
        jnp.concatenate([select.T.astype(jnp.bfloat16)] * 3, axis=1),
        jnp.concatenate(split3(emb_grad / P_SIZE), axis=0),
        preferred_element_type=jnp.float32,
    )
    pixel_gradient = spread * (sig * (1.0 + shifted * (1.0 - sig)))
    lin_grad = (pixel_gradient * gain).astype(jnp.bfloat16)
    head_term = lax.dot_general(
        lin_grad, features, (((0,), (0,)), ((), ())), preferred_element_type=jnp.float32
    )
    gain_term = jnp.sum(pixel_gradient * linear_scores, axis=0)
    shift_term = jnp.sum(pixel_gradient, axis=0)
    e_size = head_term.shape[1]
    chunk = width // n_dp
    extra = -(-2 * chunk // e_size)
    pad_rows = -(-extra // 8) * 8
    side_rows = jnp.concatenate(
        [gain_term.reshape(n_dp, chunk), shift_term.reshape(n_dp, chunk)], axis=1
    )
    side_rows = jnp.pad(side_rows, ((0, 0), (0, pad_rows * e_size - 2 * chunk)))
    stacked = jnp.concatenate(
        [head_term.reshape(n_dp, chunk, e_size), side_rows.reshape(n_dp, pad_rows, e_size)], axis=1
    )
    (part,) = halving_scatter([stacked], "dp")
    (total,) = butterfly_sum([part[0]], "leaf")
    side_flat = total[chunk:].reshape(-1)
    side_sum = jnp.stack([side_flat[:chunk], side_flat[chunk : 2 * chunk]], axis=1)
    return (total[:chunk].T, side_sum[:, 0], side_sum[:, 1], node_grad)


def solution(mesh):
    in_specs = (P(("dp", "leaf"), None), P(), P(), P(), P("leaf", None), P(), P("dp", None))
    out_specs = (P(None, "dp"), P("dp"), P("dp"), P("leaf", "dp"))
    return jax.shard_map(shards, mesh=mesh, in_specs=in_specs, out_specs=out_specs, check_vma=False)
```

```python
import jax
import jax.numpy as jnp
from jax import lax
from jax.sharding import PartitionSpec as P

P_SIZE = 100
SUB_SIZE = 64
KPOS = 16
HIGHEST = lax.Precision.HIGHEST


def block_table(pos_vec, pos_blk, neg_vec, neg_blk, blocks):
    lane_block = jnp.arange(blocks * SUB_SIZE, dtype=jnp.int32)[None, :] // SUB_SIZE
    pos_wide = jnp.tile(pos_vec, (1, blocks))
    neg_wide = jnp.tile(neg_vec, (1, blocks))
    pos_part = jnp.where(lane_block == pos_blk[:, None], pos_wide, 0.0)
    neg_part = jnp.where(lane_block == neg_blk[:, None], neg_wide, 0.0)
    return pos_part + neg_part


def pick_block(values, blk, blocks):
    rows = values.shape[0]
    split = values.reshape(rows, blocks, SUB_SIZE)
    hit = jnp.arange(blocks, dtype=jnp.int32)[None, :, None] == blk[:, None, None]
    return jnp.sum(jnp.where(hit, split, 0.0), axis=1)


def lane_mask(ids, valid):
    column = jnp.arange(SUB_SIZE, dtype=jnp.int32)[None, None, :]
    hit = ((ids % SUB_SIZE)[:, :, None] == column) & valid[:, :, None]
    return jnp.any(hit, axis=1)


def split3(x):
    hi = lax.reduce_precision(x, exponent_bits=8, mantissa_bits=7)
    rest = x - hi
    mid = lax.reduce_precision(rest, exponent_bits=8, mantissa_bits=7)
    lo = rest - mid
    return hi.astype(jnp.bfloat16), mid.astype(jnp.bfloat16), lo.astype(jnp.bfloat16)


def partners(size, bit):
    return [(i, i ^ (1 << bit)) for i in range(size)]


def doubling_gather(x, name):
    size = lax.axis_size(name)
    idx = lax.axis_index(name)
    cur = x[None]
    bit = 0
    while (1 << bit) < size:
        other = lax.ppermute(cur, name, partners(size, bit))
        low = (idx // (1 << bit)) % 2 == 0
        cur = jnp.where(low, jnp.concatenate([cur, other], 0), jnp.concatenate([other, cur], 0))
        bit += 1
    return cur.reshape((size * x.shape[0],) + x.shape[1:])


def halving_scatter(parts, name):
    size = lax.axis_size(name)
    idx = lax.axis_index(name)
    cur = [p.reshape((size, p.shape[0] // size) + p.shape[1:]) for p in parts]
    bit = 0
    while (1 << bit) < size:
        mine = (idx // (1 << bit)) % 2
        pairs = [c.reshape((c.shape[0] // 2, 2) + c.shape[1:]) for c in cur]
        keep = [lax.dynamic_index_in_dim(p, mine, axis=1, keepdims=False) for p in pairs]
        give = [lax.dynamic_index_in_dim(p, 1 - mine, axis=1, keepdims=False) for p in pairs]
        got = lax.ppermute(tuple(give), name, partners(size, bit))
        cur = [k + g for k, g in zip(keep, got)]
        bit += 1
    return [c.reshape(c.shape[1:]) for c in cur]


def butterfly_sum(parts, name):
    size = lax.axis_size(name)
    cur = tuple(parts)
    bit = 0
    while (1 << bit) < size:
        got = lax.ppermute(cur, name, partners(size, bit))
        cur = tuple(c + g for c, g in zip(cur, got))
        bit += 1
    return cur


def direct_scatter(x, name):
    size = lax.axis_size(name)
    idx = lax.axis_index(name)
    blocks = x.reshape((size, x.shape[0] // size) + x.shape[1:])
    total = lax.dynamic_index_in_dim(blocks, idx, 0, keepdims=False)
    for k in range(1, size):
        give = lax.dynamic_index_in_dim(blocks, jnp.bitwise_xor(idx, k), 0, keepdims=False)
        total = total + lax.ppermute(give, name, [(i, i ^ k) for i in range(size)])
    return total


def direct_gather(x, name):
    size = lax.axis_size(name)
    idx = lax.axis_index(name)
    got = [x] + [lax.ppermute(x, name, [(i, i ^ k) for i in range(size)]) for k in range(1, size)]
    placed = []
    for j in range(size):
        source = jnp.bitwise_xor(idx, j)
        block = got[0]
        for k in range(1, size):
            block = jnp.where(source == k, got[k], block)
        placed.append(block)
    return jnp.concatenate(placed, axis=0)


def shards(features, head_weight, gain, shift, node_weights, subtree_map, node_ids):
    rows = features.shape[0]
    images_here = rows // P_SIZE
    width = head_weight.shape[1]
    slots_dev = node_weights.shape[0]
    blocks = slots_dev // SUB_SIZE
    n_dp = lax.axis_size("dp")
    leaf = lax.axis_index("leaf")

    select = (
        jnp.arange(rows, dtype=jnp.int32)[None, :] // P_SIZE
        == jnp.arange(images_here, dtype=jnp.int32)[:, None]
    ).astype(jnp.float32)

    linear_scores = jnp.dot(features, head_weight, preferred_element_type=jnp.float32)
    shifted = gain * linear_scores + shift
    sig = jax.nn.sigmoid(shifted)
    active = shifted * sig
    image_sum = jnp.dot(select, active, precision=HIGHEST, preferred_element_type=jnp.float32)
    embedded = (image_sum / P_SIZE).astype(jnp.bfloat16)
    if lax.axis_size("leaf") <= 4:
        grouped = direct_gather(embedded, "leaf")
    else:
        grouped = doubling_gather(embedded, "leaf")
    group = grouped.shape[0]

    valid = node_ids >= 0
    safe_ids = jnp.where(valid, node_ids, 0)
    subtree_ids = jnp.arange(subtree_map.shape[0], dtype=jnp.int32)[None, :]
    lead_sub = safe_ids[:, jnp.array([0, KPOS])] // SUB_SIZE
    pos_block = jnp.sum(jnp.where(lead_sub[:, :1] == subtree_ids, subtree_map[None, :], 0), axis=1)
    neg_block = jnp.sum(jnp.where(lead_sub[:, 1:] == subtree_ids, subtree_map[None, :], 0), axis=1)
    pos_here = jnp.where(pos_block // blocks == leaf, pos_block % blocks, -1)
    neg_here = jnp.where(neg_block // blocks == leaf, neg_block % blocks, -1)
    pos_mask = lane_mask(safe_ids[:, :KPOS], valid[:, :KPOS])
    neg_mask = lane_mask(safe_ids[:, KPOS:], valid[:, KPOS:])

    scores = lax.dot_general(
        grouped, node_weights, (((1,), (1,)), ((), ())), preferred_element_type=jnp.float32
    )
    pos_logit = pick_block(scores, pos_here, blocks)
    neg_logit = pick_block(scores, neg_here, blocks)
    pos_coef = jnp.where(pos_mask & (pos_here >= 0)[:, None], jax.nn.sigmoid(pos_logit) - 1.0, 0.0)
    neg_coef = jnp.where(neg_mask & (neg_here >= 0)[:, None], jax.nn.sigmoid(neg_logit), 0.0)
    pos_coef = pos_coef.astype(jnp.bfloat16)
    neg_coef = neg_coef.astype(jnp.bfloat16)
    table = block_table(pos_coef, pos_here, neg_coef, neg_here, blocks).astype(jnp.bfloat16)
    grad_part = jnp.dot(table, node_weights, preferred_element_type=jnp.float32)
    if lax.axis_size("leaf") <= 4:
        emb_grad = direct_scatter(grad_part, "leaf")
    else:
        (emb_grad,) = halving_scatter([grad_part], "leaf")

    col_width = width // n_dp
    column_chunks = grouped.reshape(group, n_dp, col_width).transpose(1, 0, 2)
    compact = jnp.concatenate(
        [
            pos_coef,
            neg_coef,
            pos_here[:, None].astype(jnp.bfloat16),
            neg_here[:, None].astype(jnp.bfloat16),
        ],
        axis=1,
    )
    send = jnp.concatenate(
        [column_chunks, jnp.broadcast_to(compact[None], (n_dp,) + compact.shape)], axis=2
    )
    recv = lax.all_to_all(send, "dp", split_axis=0, concat_axis=0, tiled=True)
    columns = recv[:, :, :col_width].reshape(n_dp * group, col_width)
    info = recv[:, :, col_width:].reshape(n_dp * group, compact.shape[1])
    all_pos = info[:, :SUB_SIZE]
    all_neg = info[:, SUB_SIZE : 2 * SUB_SIZE]
    all_pos_blk = info[:, 2 * SUB_SIZE].astype(jnp.int32)
    all_neg_blk = info[:, 2 * SUB_SIZE + 1].astype(jnp.int32)
    all_table = block_table(all_pos, all_pos_blk, all_neg, all_neg_blk, blocks).astype(jnp.bfloat16)
    node_grad = lax.dot_general(
        all_table, columns, (((0,), (0,)), ((), ())), preferred_element_type=jnp.float32
    )

    spread = jnp.dot(
        jnp.concatenate([select.T.astype(jnp.bfloat16)] * 3, axis=1),
        jnp.concatenate(split3(emb_grad / P_SIZE), axis=0),
        preferred_element_type=jnp.float32,
    )
    pixel_gradient = spread * (sig * (1.0 + shifted * (1.0 - sig)))
    lin_grad = (pixel_gradient * gain).astype(jnp.bfloat16)
    head_term = lax.dot_general(
        lin_grad, features, (((0,), (0,)), ((), ())), preferred_element_type=jnp.float32
    )
    gain_term = jnp.sum(pixel_gradient * linear_scores, axis=0)
    shift_term = jnp.sum(pixel_gradient, axis=0)
    e_size = head_term.shape[1]
    chunk = width // n_dp
    extra = -(-2 * chunk // e_size)
    pad_rows = -(-extra // 8) * 8
    side_rows = jnp.concatenate(
        [gain_term.reshape(n_dp, chunk), shift_term.reshape(n_dp, chunk)], axis=1
    )
    side_rows = jnp.pad(side_rows, ((0, 0), (0, pad_rows * e_size - 2 * chunk)))
    stacked = jnp.concatenate(
        [head_term.reshape(n_dp, chunk, e_size), side_rows.reshape(n_dp, pad_rows, e_size)], axis=1
    )
    (part,) = halving_scatter([stacked], "dp")
    (total,) = butterfly_sum([part[0]], "leaf")
    side_flat = total[chunk:].reshape(-1)
    side_sum = jnp.stack([side_flat[:chunk], side_flat[chunk : 2 * chunk]], axis=1)
    return (total[:chunk].T, side_sum[:, 0], side_sum[:, 1], node_grad)


def solution(mesh):
    in_specs = (P(("dp", "leaf"), None), P(), P(), P(), P("leaf", None), P(), P("dp", None))
    out_specs = (P(None, "dp"), P("dp"), P("dp"), P("leaf", "dp"))
    return jax.shard_map(shards, mesh=mesh, in_specs=in_specs, out_specs=out_specs, check_vma=False)
```
